512 devices in a mesh: rows: 64 (over z, y), feat: 8 (over x, core).
Axes of the slice: x: 4, y: 8, z: 8, core: 2. Of those that a mesh axis runs over, the one named last changes fastest.
Arguments:
- node_feats: bfloat16 [65536, 256], P('rows', 'feat'), may hold values from -6 to 6
- band_weights: bfloat16 [65536, 384], P('rows'), may hold values from 0 to 1.5, as said below
- far_weights: bfloat16 [65536, 256], P('rows'), may hold values from 0 to 1.5, as said below
- far_owner: int32 [512, 2], P('rows'), may hold values from 0 to 63, all different within a row; in each aligned block of 8 rows (0 to 7, 8 to 15, ...) at most 2 rows name the same one
- far_local: int32 [512, 2], P('rows'), may hold values from 0 to 7
- w_self: bfloat16 [256, 256], replicated, may hold values from -0.375 to 0.375
- w_neigh: bfloat16 [256, 256], replicated, may hold values from -0.375 to 0.375
- bias: float32 [256], P('feat'), may hold values from -3 to 3
- cotangent: bfloat16 [65536, 256], P('rows', 'feat'), may hold values from -16 to 16
Outputs:
- layer_out: bfloat16 [65536, 256], P('rows', 'feat')
- grad_feats: float32 [65536, 256], P('rows', 'feat')
- grad_self: float32 [256, 256], P('feat')
- grad_neigh: float32 [256, 256], P('feat')
The draws below stay inside these ranges and needn't reach their ends.
Inputs may be any that keep to these rules, and one draw needn't show every extreme that they name: `far_owner`: among the far entries of the 8 row blocks of one device, no owner is named more than 2 times, and in every draw some owner is named exactly 2 times in some device's blocks; the 2 owners of one row block differ. `band_weights`: each row has a positive weight on the node's own entry of its own block; other entries are zero or positive. `far_weights`: entries are zero or positive.
All inputs are finite; a program needn't handle non-finite values.
Results may differ from the reference program's by a relative error of at most 0.0049.
Values may be sent and summed in bfloat16 or wider, within the bound.
No kernel may reach another device: no remote copies, remote signals or barrier semaphores. Data moves between devices by JAX's collectives and lax.ppermute only.
A program may use at most 64 MiB of HBM per device.

```python
import math
import jax
import jax.numpy as jnp
import numpy as np

F = 256
TILE = 128
KF = 2
TB = 8
NBLK = 512
NODES = 65536
CAP = 2
N_ROWS = 64


def sparse_weights(key, columns):
    key_mask, key_value = jax.random.split(key, 2)
    chance = jax.random.uniform(key_mask, (NODES, columns), jnp.float32)
    values = jax.random.uniform(key_value, (NODES, columns), jnp.float32, minval=0.5, maxval=1.5)
    return jnp.where(chance < 0.0625, values, 0.0)


def draw_band_weights(key, part):
    key_edges = jax.random.fold_in(key, 11)
    key_self = jax.random.fold_in(key, 12)
    weights = sparse_weights(key_edges, 3 * TILE)
    row_pos = jnp.arange(NODES, dtype=jnp.int32)[:, None] % TILE
    col_pos = jnp.arange(3 * TILE, dtype=jnp.int32)[None, :]
    self_weight = jax.random.uniform(key_self, (NODES, 1), jnp.float32, minval=0.5, maxval=1.5)
    weights = jnp.where(col_pos == TILE + row_pos, self_weight, weights)
    return weights.astype(jnp.bfloat16)


def draw_far_weights(key, part):
    weights = sparse_weights(jax.random.fold_in(key, 21), KF * TILE)
    return weights.astype(jnp.bfloat16)


def with_ends(result, rng, least, top_value):
    extent = result.shape
    index_at = [jax.random.randint(jax.random.fold_in(rng, axis), (), 0, extent[axis]) for axis in range(len(extent))]
    result = result.at[tuple(index_at)].set(least)
    longest = extent.index(max(extent))
    index_at[longest] = (index_at[longest] + 1) % extent[longest]
    return result.at[tuple(index_at)].set(top_value)


def raised(drawn, own_key, source, target, shards_of, factor):
    def block_of(position):
        return (jnp.arange(drawn.shape[position]) // (drawn.shape[position] // shards_of)).reshape((-1,) + (1,) * (drawn.ndim - 1 - position))

    one_side = jax.random.permutation(own_key, shards_of)[block_of(target)]
    far = (block_of(target) + shards_of // 2) % shards_of
    return jnp.where((block_of(source) == one_side) | (block_of(source) == far), factor * drawn, drawn)


def block_scale(stream_key, shape, cuts, smallest, top_value):
    def one(position, shards_of):
        draws = jax.random.uniform(jax.random.fold_in(jax.random.fold_in(stream_key, 6), position), (shards_of,), jnp.float32, smallest / len(cuts), top_value / len(cuts))
        return jnp.repeat(jnp.exp(draws), shape[position] // shards_of).reshape((-1,) + (1,) * (len(shape) - position - 1))

    loudness = one(*cuts[0])
    for cut in cuts[1:]:
        loudness = loudness * one(*cut)
    return loudness


def routed_block(key, own, number, rows, number_of, top, limit, lean):
    order = jax.random.permutation(key, number_of)
    packed, usual = shares(number_of, rows * top, limit, lean, True), shares(number_of, rows * top, limit, lean, False)
    places = jnp.arange(number_of)

    def named(sizes, turn):
        used = int((sizes > 0).sum())
        fixed = max(1, used // 4)
        moved = fixed + (places - fixed + turn * (used - fixed)) % max(1, number_of - fixed)
        return jnp.zeros((number_of,), jnp.int32).at[order[jnp.where(places < fixed, places, moved)]].set(jnp.asarray(sizes, jnp.int32))

    sizes = jnp.where(number % 4 == 0, named(packed, number // 4), named(usual, number - number // 4 - 1))
    mixed = jax.random.permutation(jax.random.fold_in(own, 3), number_of)
    source_of, receiver = mixed[0:number_of // 2 * 2:2], mixed[1:number_of // 2 * 2:2]
    slack = jnp.minimum(sizes[source_of] - 1, limit - sizes[receiver]) // 2
    slack = jnp.where((source_of == order[0]) | (receiver == order[0]) | (sizes[receiver] == 0), 0, jnp.maximum(slack, 0))
    moved = jax.random.randint(jax.random.fold_in(own, 4), (number_of // 2,), 0, 1 << 20) % (slack + 1)
    sizes = sizes.at[source_of].add(-moved).at[receiver].add(moved)
    labels = jnp.searchsorted(jnp.cumsum(sizes), jnp.arange(rows * top), side="right").astype(jnp.int32)
    listing = labels.reshape(top, rows).T
    listing = listing[jax.random.permutation(jax.random.fold_in(own, 1), rows)]
    turn = jax.random.randint(jax.random.fold_in(own, 2), (rows, 1), 0, top)
    return jnp.take_along_axis(listing, (jnp.arange(top)[None, :] + turn) % top, axis=1)


def shares(number_of, total, reach, skew, full):
    portions = [(1 << 20) // math.isqrt(rank ** skew) + 1 for rank in range(1, number_of + 1)]
    largest = reach if full else min(reach, max(-(-total // number_of), total * portions[0] // sum(portions)))
    least = 1 if total - largest >= number_of - 1 else 0
    holding, surplus = [largest] + [least] * (number_of - 1), total - largest - least * (number_of - 1)
    while surplus > 0:
        free = [i for i in range(1, number_of) if holding[i] < largest] or [i for i in range(1, number_of) if holding[i] < reach]
        whole, budget = sum([portions[i] for i in free]), surplus
        for i in free:
            addition = min(reach - holding[i], max(1, budget * portions[i] // whole), surplus)
            holding[i] = holding[i] + addition
            surplus = surplus - addition
    return np.array(holding)


def normal_values(key, dims, scale, limit, pieces=(), kind=jnp.bfloat16):
    gain = block_scale(key, dims, pieces, -0.22, 0.18) if pieces else 1.0
    drawn = jax.random.normal(key, dims, jnp.float32) * scale * gain
    return jnp.minimum(jnp.maximum(drawn, -limit), limit).astype(kind)


def gaussian_with(rng, extent, width, limit, cuts, heavy, kind=jnp.bfloat16):
    drawn = width * jax.random.normal(rng, extent, jnp.float32)
    if cuts:
        drawn = drawn * block_scale(rng, extent, cuts, -0.22, 0.18)
    return jnp.clip(raised(drawn, jax.random.fold_in(rng, 3), *heavy), -limit, limit).astype(kind)


def setup_inputs(seed: int = 0) -> dict:
    keys = jax.random.split(jax.random.key(seed), 10)
    node_feats = normal_values(keys[0], (NODES, F), 1.0, 6.0, ((0, 64), (1, 8)))
    band_weights = draw_band_weights(jax.random.fold_in(keys[9], 71), 0)
    far_weights = draw_far_weights(jax.random.fold_in(keys[9], 71), 0)
    far_owner_keys = jax.random.split(jax.random.fold_in(keys[3], 1), NBLK // TB)
    far_owner_turns = jax.random.permutation(jax.random.fold_in(keys[3], 3), NBLK // TB)
    far_owner = jax.vmap(lambda own, number: routed_block(jax.random.fold_in(keys[3], 2), own, number, TB, N_ROWS, KF, CAP, 2))(far_owner_keys, far_owner_turns).reshape((NBLK, KF))
    far_local = with_ends(jax.random.randint(keys[4], (NBLK, KF), 0, TB), jax.random.fold_in(keys[4], 1), 0, TB - 1).astype(jnp.int32)
    w_self = normal_values(keys[5], (F, F), F ** -0.5, 0.375)
    w_neigh = normal_values(keys[6], (F, F), F ** -0.5, 0.375)
    bias = normal_values(keys[7], (F,), 0.5, 3.0, ((0, 8),), jnp.float32)
    cotangent = gaussian_with(keys[8], (NODES, F), 1.0, 16.0, ((0, 64), (1, 8)), (0, 1, 64, 4.0))
    return dict(node_feats=node_feats, band_weights=band_weights, far_weights=far_weights, far_owner=far_owner, far_local=far_local, w_self=w_self, w_neigh=w_neigh, bias=bias, cotangent=cotangent)


def reference(node_feats, band_weights, far_weights, far_owner, far_local, w_self, w_neigh, bias, cotangent):
    blocks = NODES // TILE
    feats = node_feats.reshape(blocks, TILE, F)
    zero_block = jnp.zeros((1, TILE, F), jnp.bfloat16)
    padded = jnp.concatenate([zero_block, feats, zero_block], axis=0)
    windows = jnp.concatenate([padded[0:blocks], padded[1:blocks + 1], padded[2:blocks + 2]], axis=1).astype(jnp.float32)
    band_tiles = band_weights.reshape(blocks, TILE, 3 * TILE).astype(jnp.float32)
    band_sum = jnp.einsum('bij,bjc->bic', band_tiles, windows)
    source = (far_owner * TB + far_local).astype(jnp.int32).reshape(-1)
    fetched = feats[source].reshape(blocks, KF * TILE, F).astype(jnp.float32)
    far_tiles = far_weights.reshape(blocks, TILE, KF * TILE).astype(jnp.float32)
    far_sum = jnp.einsum('bij,bjc->bic', far_tiles, fetched)
    degree = jnp.sum(band_weights.astype(jnp.float32), axis=1) + jnp.sum(far_weights.astype(jnp.float32), axis=1)
    neighbours = ((band_sum + far_sum).reshape(NODES, F) / degree[:, None]).astype(jnp.bfloat16)
    preact = jnp.dot(node_feats, w_self, preferred_element_type=jnp.float32) + jnp.dot(neighbours, w_neigh, preferred_element_type=jnp.float32) + bias
    layer_out = jax.nn.silu(preact).astype(jnp.bfloat16)
    sigmoid_z = jax.nn.sigmoid(preact)
    grad_pre = (cotangent.astype(jnp.float32) * sigmoid_z * (1.0 + preact * (1.0 - sigmoid_z))).astype(jnp.bfloat16)
    grad_scale = NODES ** -0.5
    grad_self = jnp.dot(node_feats.T, grad_pre, preferred_element_type=jnp.float32) * grad_scale
    grad_neigh = jnp.dot(neighbours.T, grad_pre, preferred_element_type=jnp.float32) * grad_scale
    grad_agg = jnp.dot(grad_pre, w_neigh.T, preferred_element_type=jnp.float32)
    grad_neighbours = (grad_agg / degree[:, None]).astype(jnp.bfloat16)
    grad_blocks = grad_neighbours.reshape(blocks, TILE, F).astype(jnp.float32)
    grad_windows = jnp.einsum('bij,bic->bjc', band_tiles, grad_blocks)
    grad_padded = jnp.zeros((blocks + 2, TILE, F), jnp.float32)
    for offset in range(3):
        grad_padded = grad_padded.at[offset:offset + blocks].add(grad_windows[:, offset * TILE:(offset + 1) * TILE, :])
    band_grad = grad_padded[1:blocks + 1].reshape(NODES, F)
    grad_fetched = jnp.einsum('bij,bic->bjc', far_tiles, grad_blocks).reshape(blocks * KF, TILE * F)
    far_grad = jax.ops.segment_sum(grad_fetched, source, num_segments=blocks).reshape(NODES, F)
    grad_feats = jnp.dot(grad_pre, w_self.T, preferred_element_type=jnp.float32) + band_grad + far_grad
    return layer_out, grad_feats, grad_self, grad_neigh
```

```python
import jax
import jax.numpy as jnp
from jax import lax
from jax.sharding import PartitionSpec as P


def extended(block, sides, width):
    for axis, dim in sides:
        count = lax.axis_size(axis)
        forward = [(i, i + 1) for i in range(count - 1)]
        backward = [(target, source) for source, target in forward]
        low = lax.ppermute(
            lax.slice_in_dim(block, block.shape[dim] - width, None, axis=dim), axis, forward
        )
        high = lax.ppermute(lax.slice_in_dim(block, 0, width, axis=dim), axis, backward)
        block = jnp.concatenate([low, block, high], axis=dim)
    return block


def from_behind(block, axis, distance):
    devices = range(lax.axis_size(axis))
    route = [(i - distance, i) for i in devices if i - distance in devices]
    return lax.ppermute(block, axis, route)


def summed_over(parts, axis):
    count = lax.axis_size(axis)
    flat = parts.reshape(count, -1)
    pieces = lax.all_to_all(flat, axis, split_axis=0, concat_axis=0, tiled=True)
    mine = jnp.sum(pieces, axis=0, keepdims=True)
    spread = jnp.broadcast_to(mine, flat.shape)
    whole = lax.all_to_all(spread, axis, split_axis=0, concat_axis=0, tiled=True)
    return whole.reshape(parts.shape)


def on_device(
    node_feats, band_weights, far_weights, far_owner, far_local, w_self, w_neigh, bias, cotangent
):
    rows_dev, col_count = node_feats.shape
    tile_size = band_weights.shape[1] // 3
    blocks = rows_dev // tile_size
    fanout = far_owner.shape[1]
    peer_count = lax.axis_size("rows")
    capacity = max(2, 2 * blocks * fanout // peer_count)
    col_start = lax.axis_index("feat") * col_count
    padded = extended(node_feats, (("rows", 0),), tile_size)
    windows = jnp.concatenate(
        [
            padded[offset * tile_size : offset * tile_size + rows_dev].reshape(
                blocks, tile_size, col_count
            )
            for offset in range(3)
        ],
        axis=1,
    )
    band_tiles = band_weights.reshape(blocks, tile_size, 3 * tile_size)
    band_sum = jnp.einsum("bij,bjc->bic", band_tiles, windows, preferred_element_type=jnp.float32)
    owner_ids = far_owner.reshape(-1)
    local_ids = far_local.reshape(-1)
    entries = owner_ids.shape[0]
    same_owner = owner_ids[:, None] == owner_ids[None, :]
    earlier = jnp.arange(entries)[None, :] < jnp.arange(entries)[:, None]
    slot_rank = jnp.sum(jnp.where(same_owner & earlier, 1, 0), axis=1).astype(jnp.int32)
    slot_ids = owner_ids * capacity + slot_rank
    slot_hit = slot_ids[:, None] == jnp.arange(peer_count * capacity, dtype=jnp.int32)[None, :]
    request = (jnp.sum(jnp.where(slot_hit, local_ids[:, None] + 1, 0), axis=0) - 1).reshape(
        peer_count, capacity
    )
    wanted = lax.all_to_all(request, "rows", split_axis=0, concat_axis=0, tiled=True)
    usable = wanted >= 0
    safe_ids = jnp.maximum(wanted, 0)
    own_blocks = node_feats.reshape(blocks, tile_size, col_count)
    outgoing = jnp.where(
        usable[:, :, None, None], own_blocks[safe_ids], jnp.zeros((), jnp.bfloat16)
    )
    incoming = lax.all_to_all(outgoing, "rows", split_axis=0, concat_axis=0, tiled=True)
    fetched = incoming.reshape(peer_count * capacity, tile_size, col_count)[slot_ids].reshape(
        blocks, fanout * tile_size, col_count
    )
    far_tiles = far_weights.reshape(blocks, tile_size, fanout * tile_size)
    far_sum = jnp.einsum("bij,bjc->bic", far_tiles, fetched, preferred_element_type=jnp.float32)
    degree = jnp.sum(band_weights.astype(jnp.float32), axis=1) + jnp.sum(
        far_weights.astype(jnp.float32), axis=1
    )
    neighbours = ((band_sum + far_sum).reshape(rows_dev, col_count) / degree[:, None]).astype(
        jnp.bfloat16
    )
    rows_self = lax.dynamic_slice_in_dim(w_self, col_start, col_count, 0)
    rows_neigh = lax.dynamic_slice_in_dim(w_neigh, col_start, col_count, 0)
    terms = jnp.dot(node_feats, rows_self, preferred_element_type=jnp.float32) + jnp.dot(
        neighbours, rows_neigh, preferred_element_type=jnp.float32
    )
    preact = lax.psum_scatter(terms, "feat", scatter_dimension=1, tiled=True)
    preact = preact + bias
    layer_out = jax.nn.silu(preact).astype(jnp.bfloat16)
    sigmoid_z = jax.nn.sigmoid(preact)
    grad_pre = (
        cotangent.astype(jnp.float32) * sigmoid_z * (1.0 + preact * (1.0 - sigmoid_z))
    ).astype(jnp.bfloat16)
    full_grad = lax.all_gather(grad_pre, "feat", axis=1, tiled=True)
    grad_scale = float(rows_dev * peer_count) ** (-0.5)
    part_self = jnp.einsum("rc,rf->cf", node_feats, full_grad, preferred_element_type=jnp.float32)
    part_neigh = jnp.einsum("rc,rf->cf", neighbours, full_grad, preferred_element_type=jnp.float32)
    sum_self, sum_neigh = summed_over(jnp.stack([part_self, part_neigh]), "rows")
    grad_self = sum_self * grad_scale
    grad_neigh = sum_neigh * grad_scale
    dense_grad = jnp.einsum("rf,cf->rc", full_grad, rows_self, preferred_element_type=jnp.float32)
    grad_agg = jnp.einsum("rf,cf->rc", full_grad, rows_neigh, preferred_element_type=jnp.float32)
    grad_neighbours = (grad_agg / degree[:, None]).astype(jnp.bfloat16)
    grad_blocks = grad_neighbours.reshape(blocks, tile_size, col_count)
    grad_windows = jnp.einsum(
        "bij,bic->bjc", band_tiles, grad_blocks, preferred_element_type=jnp.float32
    )
    grad_padded = jnp.zeros((rows_dev + 2 * tile_size, col_count), jnp.float32)
    for offset in range(3):
        piece = grad_windows[:, offset * tile_size : (offset + 1) * tile_size, :].reshape(
            rows_dev, col_count
        )
        grad_padded = grad_padded + jnp.pad(
            piece, ((offset * tile_size, (2 - offset) * tile_size), (0, 0))
        )
    top_rim = grad_padded[:tile_size]
    bottom_rim = grad_padded[rows_dev + tile_size :]
    from_below = from_behind(top_rim, "rows", -1)
    from_above = from_behind(bottom_rim, "rows", 1)
    grad_fetched = jnp.einsum(
        "bij,bic->bjc", far_tiles, grad_blocks, preferred_element_type=jnp.float32
    )
    returning = jnp.zeros((peer_count * capacity, tile_size, col_count), jnp.float32)
    returning = returning.at[slot_ids].set(grad_fetched.reshape(entries, tile_size, col_count))
    returned = lax.all_to_all(
        returning.reshape(peer_count, capacity, tile_size, col_count).astype(jnp.bfloat16),
        "rows",
        split_axis=0,
        concat_axis=0,
        tiled=True,
    ).astype(jnp.float32)
    target_block = jnp.where(usable, wanted, blocks).reshape(-1)
    owed = jnp.zeros((blocks, tile_size * col_count), jnp.float32)
    owed = owed.at[target_block].add(
        returned.reshape(peer_count * capacity, tile_size * col_count), mode="drop"
    )
    interior = (
        dense_grad
        + grad_padded[tile_size : tile_size + rows_dev]
        + owed.reshape(rows_dev, col_count)
    )
    interior = interior.at[:tile_size].add(from_above)
    grad_feats = interior.at[rows_dev - tile_size :].add(from_below)
    return (layer_out, grad_feats, grad_self, grad_neigh)


def solution(mesh):
    in_specs = (
        P("rows", "feat"),
        P("rows", None),
        P("rows", None),
        P("rows", None),
        P("rows", None),
        P(),
        P(),
        P("feat"),
        P("rows", "feat"),
    )
    out_specs = (P("rows", "feat"), P("rows", "feat"), P("feat", None), P("feat", None))
    return jax.shard_map(
        on_device, mesh=mesh, in_specs=in_specs, out_specs=out_specs, check_vma=False
    )
```

```python
import jax
import jax.numpy as jnp
from jax import lax
from jax.sharding import PartitionSpec as P


def extended(block, sides, width):
    for axis, dim in sides:
        count = lax.axis_size(axis)
        forward = [(i, i + 1) for i in range(count - 1)]
        backward = [(target, source) for source, target in forward]
        low = lax.ppermute(
            lax.slice_in_dim(block, block.shape[dim] - width, None, axis=dim), axis, forward
        )
        high = lax.ppermute(lax.slice_in_dim(block, 0, width, axis=dim), axis, backward)
        block = jnp.concatenate([low, block, high], axis=dim)
    return block


def from_behind(block, axis, distance):
    devices = range(lax.axis_size(axis))
    route = [(i - distance, i) for i in devices if i - distance in devices]
    return lax.ppermute(block, axis, route)


def on_device(
    node_feats, band_weights, far_weights, far_owner, far_local, w_self, w_neigh, bias, cotangent
):
    rows_dev, col_count = node_feats.shape
    tile_size = band_weights.shape[1] // 3
    blocks = rows_dev // tile_size
    fanout = far_owner.shape[1]
    peer_count = lax.axis_size("rows")
    capacity = max(2, 2 * blocks * fanout // peer_count)
    col_start = lax.axis_index("feat") * col_count
    padded = extended(node_feats, (("rows", 0),), tile_size)
    windows = jnp.concatenate(
        [
            padded[offset * tile_size : offset * tile_size + rows_dev].reshape(
                blocks, tile_size, col_count
            )
            for offset in range(3)
        ],
        axis=1,
    )
    band_tiles = band_weights.reshape(blocks, tile_size, 3 * tile_size)
    band_sum = jnp.einsum("bij,bjc->bic", band_tiles, windows, preferred_element_type=jnp.float32)
    owner_ids = far_owner.reshape(-1)
    local_ids = far_local.reshape(-1)
    entries = owner_ids.shape[0]
    same_owner = owner_ids[:, None] == owner_ids[None, :]
    earlier = jnp.arange(entries)[None, :] < jnp.arange(entries)[:, None]
    slot_rank = jnp.sum(jnp.where(same_owner & earlier, 1, 0), axis=1).astype(jnp.int32)
    slot_ids = owner_ids * capacity + slot_rank
    slot_hit = slot_ids[:, None] == jnp.arange(peer_count * capacity, dtype=jnp.int32)[None, :]
    request = (jnp.sum(jnp.where(slot_hit, local_ids[:, None] + 1, 0), axis=0) - 1).reshape(
        peer_count, capacity
    )
    wanted = lax.all_to_all(request, "rows", split_axis=0, concat_axis=0, tiled=True)
    usable = wanted >= 0
    safe_ids = jnp.maximum(wanted, 0)
    own_blocks = node_feats.reshape(blocks, tile_size, col_count)
    outgoing = jnp.where(
        usable[:, :, None, None], own_blocks[safe_ids], jnp.zeros((), jnp.bfloat16)
    )
    incoming = lax.all_to_all(outgoing, "rows", split_axis=0, concat_axis=0, tiled=True)
    fetched = incoming.reshape(peer_count * capacity, tile_size, col_count)[slot_ids].reshape(
        blocks, fanout * tile_size, col_count
    )
    far_tiles = far_weights.reshape(blocks, tile_size, fanout * tile_size)
    far_sum = jnp.einsum("bij,bjc->bic", far_tiles, fetched, preferred_element_type=jnp.float32)
    degree = jnp.sum(band_weights.astype(jnp.float32), axis=1) + jnp.sum(
        far_weights.astype(jnp.float32), axis=1
    )
    neighbours = ((band_sum + far_sum).reshape(rows_dev, col_count) / degree[:, None]).astype(
        jnp.bfloat16
    )
    rows_self = lax.dynamic_slice_in_dim(w_self, col_start, col_count, 0)
    rows_neigh = lax.dynamic_slice_in_dim(w_neigh, col_start, col_count, 0)
    terms = jnp.dot(node_feats, rows_self, preferred_element_type=jnp.float32) + jnp.dot(
        neighbours, rows_neigh, preferred_element_type=jnp.float32
    )
    preact = lax.psum_scatter(terms, "feat", scatter_dimension=1, tiled=True)
    preact = preact + bias
    layer_out = jax.nn.silu(preact).astype(jnp.bfloat16)
    sigmoid_z = jax.nn.sigmoid(preact)
    grad_pre = (
        cotangent.astype(jnp.float32) * sigmoid_z * (1.0 + preact * (1.0 - sigmoid_z))
    ).astype(jnp.bfloat16)
    full_grad = lax.all_gather(grad_pre, "feat", axis=1, tiled=True)
    grad_scale = float(rows_dev * peer_count) ** (-0.5)
    part_self = jnp.einsum("rc,rf->cf", node_feats, full_grad, preferred_element_type=jnp.float32)
    part_neigh = jnp.einsum("rc,rf->cf", neighbours, full_grad, preferred_element_type=jnp.float32)
    dense_grad = jnp.einsum("rf,cf->rc", full_grad, rows_self, preferred_element_type=jnp.float32)
    grad_agg = jnp.einsum("rf,cf->rc", full_grad, rows_neigh, preferred_element_type=jnp.float32)
    grad_neighbours = (grad_agg / degree[:, None]).astype(jnp.bfloat16)
    grad_blocks = grad_neighbours.reshape(blocks, tile_size, col_count)
    grad_windows = jnp.einsum(
        "bij,bic->bjc", band_tiles, grad_blocks, preferred_element_type=jnp.float32
    )
    grad_padded = jnp.zeros((rows_dev + 2 * tile_size, col_count), jnp.float32)
    for offset in range(3):
        piece = grad_windows[:, offset * tile_size : (offset + 1) * tile_size, :].reshape(
            rows_dev, col_count
        )
        grad_padded = grad_padded + jnp.pad(
            piece, ((offset * tile_size, (2 - offset) * tile_size), (0, 0))
        )
    top_rim = grad_padded[:tile_size]
    bottom_rim = grad_padded[rows_dev + tile_size :]
    from_below = from_behind(top_rim, "rows", -1)
    from_above = from_behind(bottom_rim, "rows", 1)
    grad_fetched = jnp.einsum(
        "bij,bic->bjc", far_tiles, grad_blocks, preferred_element_type=jnp.float32
    )
    returning = jnp.zeros((peer_count * capacity, tile_size, col_count), jnp.float32)
    returning = returning.at[slot_ids].set(grad_fetched.reshape(entries, tile_size, col_count))
    partials = jnp.stack([part_self, part_neigh]).reshape(peer_count, -1)
    payload = jnp.concatenate([returning.reshape(peer_count, -1), partials], axis=1)
    arrived = lax.all_to_all(payload, "rows", split_axis=0, concat_axis=0, tiled=True)
    returned = arrived[:, : capacity * tile_size * col_count]
    mine = jnp.sum(arrived[:, capacity * tile_size * col_count :], axis=0, keepdims=True)
    whole = lax.all_to_all(
        jnp.broadcast_to(mine, partials.shape), "rows", split_axis=0, concat_axis=0, tiled=True
    )
    sum_self, sum_neigh = whole.reshape(2, col_count, -1)
    grad_self = sum_self * grad_scale
    grad_neigh = sum_neigh * grad_scale
    target_block = jnp.where(usable, wanted, blocks).reshape(-1)
    owed = jnp.zeros((blocks, tile_size * col_count), jnp.float32)
    owed = owed.at[target_block].add(
        returned.reshape(peer_count * capacity, tile_size * col_count), mode="drop"
    )
    interior = (
        dense_grad
        + grad_padded[tile_size : tile_size + rows_dev]
        + owed.reshape(rows_dev, col_count)
    )
    interior = interior.at[:tile_size].add(from_above)
    grad_feats = interior.at[rows_dev - tile_size :].add(from_below)
    return (layer_out, grad_feats, grad_self, grad_neigh)


def solution(mesh):
    in_specs = (
        P("rows", "feat"),
        P("rows", None),
        P("rows", None),
        P("rows", None),
        P("rows", None),
        P(),
        P(),
        P("feat"),
        P("rows", "feat"),
    )
    out_specs = (P("rows", "feat"), P("rows", "feat"), P("feat", None), P("feat", None))
    return jax.shard_map(
        on_device, mesh=mesh, in_specs=in_specs, out_specs=out_specs, check_vma=False
    )
```

```python
import jax
import jax.numpy as jnp
from jax import lax
from jax.sharding import PartitionSpec as P


def extended(block, sides, width):
    for axis, dim in sides:
        count = lax.axis_size(axis)
        forward = [(i, i + 1) for i in range(count - 1)]
        backward = [(target, source) for source, target in forward]
        low = lax.ppermute(
            lax.slice_in_dim(block, block.shape[dim] - width, None, axis=dim), axis, forward
        )
        high = lax.ppermute(lax.slice_in_dim(block, 0, width, axis=dim), axis, backward)
        block = jnp.concatenate([low, block, high], axis=dim)
    return block


def from_behind(block, axis, distance):
    devices = range(lax.axis_size(axis))
    route = [(i - distance, i) for i in devices if i - distance in devices]
    return lax.ppermute(block, axis, route)


def on_device(
    node_feats, band_weights, far_weights, far_owner, far_local, w_self, w_neigh, bias, cotangent
):
    rows_dev, col_count = node_feats.shape
    tile_size = band_weights.shape[1] // 3
    blocks = rows_dev // tile_size
    fanout = far_owner.shape[1]
    peer_count = lax.axis_size("rows")
    capacity = max(2, 2 * blocks * fanout // peer_count)
    col_start = lax.axis_index("feat") * col_count
    padded = extended(node_feats, (("rows", 0),), tile_size)
    windows = jnp.concatenate(
        [
            padded[offset * tile_size : offset * tile_size + rows_dev].reshape(
                blocks, tile_size, col_count
            )
            for offset in range(3)
        ],
        axis=1,
    )
    band_tiles = band_weights.reshape(blocks, tile_size, 3 * tile_size)
    band_sum = jnp.einsum("bij,bjc->bic", band_tiles, windows, preferred_element_type=jnp.float32)
    owner_ids = far_owner.reshape(-1)
    local_ids = far_local.reshape(-1)
    entries = owner_ids.shape[0]
    same_owner = owner_ids[:, None] == owner_ids[None, :]
    earlier = jnp.arange(entries)[None, :] < jnp.arange(entries)[:, None]
    slot_rank = jnp.sum(jnp.where(same_owner & earlier, 1, 0), axis=1).astype(jnp.int32)
    slot_ids = owner_ids * capacity + slot_rank
    slot_hit = slot_ids[:, None] == jnp.arange(peer_count * capacity, dtype=jnp.int32)[None, :]
    request = (jnp.sum(jnp.where(slot_hit, local_ids[:, None] + 1, 0), axis=0) - 1).reshape(
        peer_count, capacity
    )
    wanted = lax.all_to_all(request, "rows", split_axis=0, concat_axis=0, tiled=True)
    usable = wanted >= 0
    safe_ids = jnp.maximum(wanted, 0)
    own_blocks = node_feats.reshape(blocks, tile_size, col_count)
    outgoing = jnp.where(
        usable[:, :, None, None], own_blocks[safe_ids], jnp.zeros((), jnp.bfloat16)
    )
    incoming = lax.all_to_all(outgoing, "rows", split_axis=0, concat_axis=0, tiled=True)
    fetched = incoming.reshape(peer_count * capacity, tile_size, col_count)[slot_ids].reshape(
        blocks, fanout * tile_size, col_count
    )
    far_tiles = far_weights.reshape(blocks, tile_size, fanout * tile_size)
    far_sum = jnp.einsum("bij,bjc->bic", far_tiles, fetched, preferred_element_type=jnp.float32)
    degree = jnp.sum(band_weights.astype(jnp.float32), axis=1) + jnp.sum(
        far_weights.astype(jnp.float32), axis=1
    )
    neighbours = ((band_sum + far_sum).reshape(rows_dev, col_count) / degree[:, None]).astype(
        jnp.bfloat16
    )
    rows_self = lax.dynamic_slice_in_dim(w_self, col_start, col_count, 0)
    rows_neigh = lax.dynamic_slice_in_dim(w_neigh, col_start, col_count, 0)
    terms = jnp.dot(node_feats, rows_self, preferred_element_type=jnp.float32) + jnp.dot(
        neighbours, rows_neigh, preferred_element_type=jnp.float32
    )
    preact = lax.psum_scatter(terms, "feat", scatter_dimension=1, tiled=True)
    preact = preact + bias
    layer_out = jax.nn.silu(preact).astype(jnp.bfloat16)
    sigmoid_z = jax.nn.sigmoid(preact)
    grad_pre = (
        cotangent.astype(jnp.float32) * sigmoid_z * (1.0 + preact * (1.0 - sigmoid_z))
    ).astype(jnp.bfloat16)
    full_grad = lax.all_gather(grad_pre, "feat", axis=1, tiled=True)
    grad_scale = float(rows_dev * peer_count) ** (-0.5)
    part_self = jnp.einsum("rc,rf->cf", node_feats, full_grad, preferred_element_type=jnp.float32)
    part_neigh = jnp.einsum("rc,rf->cf", neighbours, full_grad, preferred_element_type=jnp.float32)
    dense_grad = jnp.einsum("rf,cf->rc", full_grad, rows_self, preferred_element_type=jnp.float32)
    grad_agg = jnp.einsum("rf,cf->rc", full_grad, rows_neigh, preferred_element_type=jnp.float32)
    grad_neighbours = (grad_agg / degree[:, None]).astype(jnp.bfloat16)
    grad_blocks = grad_neighbours.reshape(blocks, tile_size, col_count)
    grad_windows = jnp.einsum(
        "bij,bic->bjc", band_tiles, grad_blocks, preferred_element_type=jnp.float32
    )
    grad_padded = jnp.zeros((rows_dev + 2 * tile_size, col_count), jnp.float32)
    for offset in range(3):
        piece = grad_windows[:, offset * tile_size : (offset + 1) * tile_size, :].reshape(
            rows_dev, col_count
        )
        grad_padded = grad_padded + jnp.pad(
            piece, ((offset * tile_size, (2 - offset) * tile_size), (0, 0))
        )
    top_rim = grad_padded[:tile_size]
    bottom_rim = grad_padded[rows_dev + tile_size :]
    from_below = from_behind(top_rim, "rows", -1)
    from_above = from_behind(bottom_rim, "rows", 1)
    grad_fetched = jnp.einsum(
        "bij,bic->bjc", far_tiles, grad_blocks, preferred_element_type=jnp.float32
    )
    returning = jnp.zeros((peer_count * capacity, tile_size, col_count), jnp.float32)
    returning = returning.at[slot_ids].set(grad_fetched.reshape(entries, tile_size, col_count))
    partials = jnp.stack([part_self, part_neigh]).reshape(peer_count, -1)
    high = partials.astype(jnp.bfloat16)
    low = (partials - high.astype(jnp.float32)).astype(jnp.bfloat16)
    span = capacity * tile_size * col_count
    payload = jnp.concatenate(
        [returning.reshape(peer_count, -1).astype(jnp.bfloat16), high, low], axis=1
    )
    arrived = lax.all_to_all(payload, "rows", split_axis=0, concat_axis=0, tiled=True)
    returned = arrived[:, :span].astype(jnp.float32)
    width = partials.shape[1]
    mine = jnp.sum(
        arrived[:, span : span + width].astype(jnp.float32)
        + arrived[:, span + width :].astype(jnp.float32),
        axis=0,
        keepdims=True,
    )
    whole = lax.all_to_all(
        jnp.broadcast_to(mine, partials.shape), "rows", split_axis=0, concat_axis=0, tiled=True
    )
    sum_self, sum_neigh = whole.reshape(2, col_count, -1)
    grad_self = sum_self * grad_scale
    grad_neigh = sum_neigh * grad_scale
    target_block = jnp.where(usable, wanted, blocks).reshape(-1)
    owed = jnp.zeros((blocks, tile_size * col_count), jnp.float32)
    owed = owed.at[target_block].add(
        returned.reshape(peer_count * capacity, tile_size * col_count), mode="drop"
    )
    interior = (
        dense_grad
        + grad_padded[tile_size : tile_size + rows_dev]
        + owed.reshape(rows_dev, col_count)
    )
    interior = interior.at[:tile_size].add(from_above)
    grad_feats = interior.at[rows_dev - tile_size :].add(from_below)
    return (layer_out, grad_feats, grad_self, grad_neigh)


def solution(mesh):
    in_specs = (
        P("rows", "feat"),
        P("rows", None),
        P("rows", None),
        P("rows", None),
        P("rows", None),
        P(),
        P(),
        P("feat"),
        P("rows", "feat"),
    )
    out_specs = (P("rows", "feat"), P("rows", "feat"), P("feat", None), P("feat", None))
    return jax.shard_map(
        on_device, mesh=mesh, in_specs=in_specs, out_specs=out_specs, check_vma=False
    )
```

```python
import jax
import jax.numpy as jnp
from jax import lax
from jax.sharding import PartitionSpec as P


def extended(block, sides, width):
    for axis, dim in sides:
        count = lax.axis_size(axis)
        forward = [(i, i + 1) for i in range(count - 1)]
        backward = [(target, source) for source, target in forward]
        low = lax.ppermute(
            lax.slice_in_dim(block, block.shape[dim] - width, None, axis=dim), axis, forward
        )
        high = lax.ppermute(lax.slice_in_dim(block, 0, width, axis=dim), axis, backward)
        block = jnp.concatenate([low, block, high], axis=dim)
    return block


def from_behind(block, axis, distance):
    devices = range(lax.axis_size(axis))
    route = [(i - distance, i) for i in devices if i - distance in devices]
    return lax.ppermute(block, axis, route)


def summed_over(parts, axis):
    count = lax.axis_size(axis)
    flat = parts.reshape(count, -1)
    pieces = lax.all_to_all(flat, axis, split_axis=0, concat_axis=0, tiled=True)
    mine = jnp.sum(pieces, axis=0, keepdims=True)
    spread = jnp.broadcast_to(mine, flat.shape)
    whole = lax.all_to_all(spread, axis, split_axis=0, concat_axis=0, tiled=True)
    return whole.reshape(parts.shape)


def on_device(
    node_feats, band_weights, far_weights, far_owner, far_local, w_self, w_neigh, bias, cotangent
):
    rows_dev, col_count = node_feats.shape
    tile_size = band_weights.shape[1] // 3
    blocks = rows_dev // tile_size
    fanout = far_owner.shape[1]
    peer_count = lax.axis_size("rows")
    capacity = max(2, 2 * blocks * fanout // peer_count)
    col_start = lax.axis_index("feat") * col_count
    bias_high = lax.reduce_precision(bias, exponent_bits=8, mantissa_bits=7)
    bias_rest = bias - bias_high
    bias_mid = lax.reduce_precision(bias_rest, exponent_bits=8, mantissa_bits=7)
    bias_parts = jnp.zeros((16, col_count), jnp.bfloat16)
    bias_parts = bias_parts.at[:3].set(
        jnp.stack([bias_high, bias_mid, bias_rest - bias_mid]).astype(jnp.bfloat16)
    )
    packed = jnp.concatenate([node_feats, cotangent, bias_parts], axis=0)
    gathered = lax.all_gather(packed, "feat", axis=1, tiled=True)
    feats_all = gathered[:rows_dev]
    cotangent_all = gathered[rows_dev : 2 * rows_dev]
    bias_rows = gathered[2 * rows_dev : 2 * rows_dev + 3].astype(jnp.float32)
    bias_all = (bias_rows[0] + bias_rows[1]) + bias_rows[2]
    padded = extended(node_feats, (("rows", 0),), tile_size)
    windows = jnp.concatenate(
        [
            padded[offset * tile_size : offset * tile_size + rows_dev].reshape(
                blocks, tile_size, col_count
            )
            for offset in range(3)
        ],
        axis=1,
    )
    band_tiles = band_weights.reshape(blocks, tile_size, 3 * tile_size)
    band_sum = jnp.einsum("bij,bjc->bic", band_tiles, windows, preferred_element_type=jnp.float32)
    owner_ids = far_owner.reshape(-1)
    local_ids = far_local.reshape(-1)
    entries = owner_ids.shape[0]
    same_owner = owner_ids[:, None] == owner_ids[None, :]
    earlier = jnp.arange(entries)[None, :] < jnp.arange(entries)[:, None]
    slot_rank = jnp.sum(jnp.where(same_owner & earlier, 1, 0), axis=1).astype(jnp.int32)
    slot_ids = owner_ids * capacity + slot_rank
    slot_hit = slot_ids[:, None] == jnp.arange(peer_count * capacity, dtype=jnp.int32)[None, :]
    request = (jnp.sum(jnp.where(slot_hit, local_ids[:, None] + 1, 0), axis=0) - 1).reshape(
        peer_count, capacity
    )
    wanted = lax.all_to_all(request, "rows", split_axis=0, concat_axis=0, tiled=True)
    usable = wanted >= 0
    safe_ids = jnp.maximum(wanted, 0)
    own_blocks = node_feats.reshape(blocks, tile_size, col_count)
    outgoing = jnp.where(
        usable[:, :, None, None], own_blocks[safe_ids], jnp.zeros((), jnp.bfloat16)
    )
    incoming = lax.all_to_all(outgoing, "rows", split_axis=0, concat_axis=0, tiled=True)
    fetched = incoming.reshape(peer_count * capacity, tile_size, col_count)[slot_ids].reshape(
        blocks, fanout * tile_size, col_count
    )
    far_tiles = far_weights.reshape(blocks, tile_size, fanout * tile_size)
    far_sum = jnp.einsum("bij,bjc->bic", far_tiles, fetched, preferred_element_type=jnp.float32)
    degree = jnp.sum(band_weights.astype(jnp.float32), axis=1) + jnp.sum(
        far_weights.astype(jnp.float32), axis=1
    )
    neighbours = ((band_sum + far_sum).reshape(rows_dev, col_count) / degree[:, None]).astype(
        jnp.bfloat16
    )
    rows_self = lax.dynamic_slice_in_dim(w_self, col_start, col_count, 0)
    rows_neigh = lax.dynamic_slice_in_dim(w_neigh, col_start, col_count, 0)
    neighbours_all = lax.all_gather(neighbours, "feat", axis=1, tiled=True)
    preact_all = (
        jnp.dot(feats_all, w_self, preferred_element_type=jnp.float32)
        + jnp.dot(neighbours_all, w_neigh, preferred_element_type=jnp.float32)
        + bias_all
    )
    preact = lax.dynamic_slice_in_dim(preact_all, col_start, col_count, 1)
    layer_out = jax.nn.silu(preact).astype(jnp.bfloat16)
    sigmoid_z = jax.nn.sigmoid(preact_all)
    full_grad = (
        cotangent_all.astype(jnp.float32) * sigmoid_z * (1.0 + preact_all * (1.0 - sigmoid_z))
    ).astype(jnp.bfloat16)
    grad_scale = float(rows_dev * peer_count) ** (-0.5)
    part_self = jnp.einsum("rc,rf->cf", node_feats, full_grad, preferred_element_type=jnp.float32)
    part_neigh = jnp.einsum("rc,rf->cf", neighbours, full_grad, preferred_element_type=jnp.float32)
    sum_self, sum_neigh = summed_over(jnp.stack([part_self, part_neigh]), "rows")
    grad_self = sum_self * grad_scale
    grad_neigh = sum_neigh * grad_scale
    dense_grad = jnp.einsum("rf,cf->rc", full_grad, rows_self, preferred_element_type=jnp.float32)
    grad_agg = jnp.einsum("rf,cf->rc", full_grad, rows_neigh, preferred_element_type=jnp.float32)
    grad_neighbours = (grad_agg / degree[:, None]).astype(jnp.bfloat16)
    grad_blocks = grad_neighbours.reshape(blocks, tile_size, col_count)
    grad_windows = jnp.einsum(
        "bij,bic->bjc", band_tiles, grad_blocks, preferred_element_type=jnp.float32
    )
    grad_padded = jnp.zeros((rows_dev + 2 * tile_size, col_count), jnp.float32)
    for offset in range(3):
        piece = grad_windows[:, offset * tile_size : (offset + 1) * tile_size, :].reshape(
            rows_dev, col_count
        )
        grad_padded = grad_padded + jnp.pad(
            piece, ((offset * tile_size, (2 - offset) * tile_size), (0, 0))
        )
    top_rim = grad_padded[:tile_size]
    bottom_rim = grad_padded[rows_dev + tile_size :]
    from_below = from_behind(top_rim, "rows", -1)
    from_above = from_behind(bottom_rim, "rows", 1)
    grad_fetched = jnp.einsum(
        "bij,bic->bjc", far_tiles, grad_blocks, preferred_element_type=jnp.float32
    )
    returning = jnp.zeros((peer_count * capacity, tile_size, col_count), jnp.float32)
    returning = returning.at[slot_ids].set(grad_fetched.reshape(entries, tile_size, col_count))
    returned = lax.all_to_all(
        returning.reshape(peer_count, capacity, tile_size, col_count).astype(jnp.bfloat16),
        "rows",
        split_axis=0,
        concat_axis=0,
        tiled=True,
    ).astype(jnp.float32)
    target_block = jnp.where(usable, wanted, blocks).reshape(-1)
    owed = jnp.zeros((blocks, tile_size * col_count), jnp.float32)
    owed = owed.at[target_block].add(
        returned.reshape(peer_count * capacity, tile_size * col_count), mode="drop"
    )
    interior = (
        dense_grad
        + grad_padded[tile_size : tile_size + rows_dev]
        + owed.reshape(rows_dev, col_count)
    )
    interior = interior.at[:tile_size].add(from_above)
    grad_feats = interior.at[rows_dev - tile_size :].add(from_below)
    return (layer_out, grad_feats, grad_self, grad_neigh)


def solution(mesh):
    in_specs = (
        P("rows", "feat"),
        P("rows", None),
        P("rows", None),
        P("rows", None),
        P("rows", None),
        P(),
        P(),
        P("feat"),
        P("rows", "feat"),
    )
    out_specs = (P("rows", "feat"), P("rows", "feat"), P("feat", None), P("feat", None))
    return jax.shard_map(
        on_device, mesh=mesh, in_specs=in_specs, out_specs=out_specs, check_vma=False
    )
```

```python
import jax
import jax.numpy as jnp
from jax import lax
from jax.sharding import PartitionSpec as P


def from_behind(block, axis, distance):
    devices = range(lax.axis_size(axis))
    route = [(i - distance, i) for i in devices if i - distance in devices]
    return lax.ppermute(block, axis, route)


def summed_over(parts, axis):
    count = lax.axis_size(axis)
    flat = parts.reshape(count, -1)
    pieces = lax.all_to_all(flat, axis, split_axis=0, concat_axis=0, tiled=True)
    mine = jnp.sum(pieces, axis=0, keepdims=True)
    spread = jnp.broadcast_to(mine, flat.shape)
    whole = lax.all_to_all(spread, axis, split_axis=0, concat_axis=0, tiled=True)
    return whole.reshape(parts.shape)


def on_device(
    node_feats, band_weights, far_weights, far_owner, far_local, w_self, w_neigh, bias, cotangent
):
    rows_dev, col_count = node_feats.shape
    tile_size = band_weights.shape[1] // 3
    blocks = rows_dev // tile_size
    fanout = far_owner.shape[1]
    peer_count = lax.axis_size("rows")
    capacity = max(2, 2 * blocks * fanout // peer_count)
    row_index = lax.axis_index("rows")
    col_start = lax.axis_index("feat") * col_count
    bias_high = lax.reduce_precision(bias, exponent_bits=8, mantissa_bits=7)
    bias_rest = bias - bias_high
    bias_mid = lax.reduce_precision(bias_rest, exponent_bits=8, mantissa_bits=7)
    bias_parts = jnp.zeros((16, col_count), jnp.bfloat16)
    bias_parts = bias_parts.at[:3].set(
        jnp.stack([bias_high, bias_mid, bias_rest - bias_mid]).astype(jnp.bfloat16)
    )
    packed = jnp.concatenate([node_feats, cotangent, bias_parts], axis=0)
    gathered = lax.all_gather(packed, "feat", axis=1, tiled=True)
    feats_all = gathered[:rows_dev]
    cotangent_all = gathered[rows_dev : 2 * rows_dev]
    bias_rows = gathered[2 * rows_dev : 2 * rows_dev + 3].astype(jnp.float32)
    bias_all = (bias_rows[0] + bias_rows[1]) + bias_rows[2]
    owner_ids = far_owner.reshape(-1)
    local_ids = far_local.reshape(-1)
    entries = owner_ids.shape[0]
    same_owner = owner_ids[:, None] == owner_ids[None, :]
    earlier = jnp.arange(entries)[None, :] < jnp.arange(entries)[:, None]
    slot_rank = jnp.sum(jnp.where(same_owner & earlier, 1, 0), axis=1).astype(jnp.int32)
    slot_ids = owner_ids * capacity + slot_rank
    slot_hit = slot_ids[:, None] == jnp.arange(peer_count * capacity, dtype=jnp.int32)[None, :]
    far_request = (jnp.sum(jnp.where(slot_hit, local_ids[:, None] + 1, 0), axis=0) - 1).reshape(
        peer_count, capacity
    )
    peers = jnp.arange(peer_count, dtype=jnp.int32)
    halo_request = jnp.where(
        peers == row_index - 1, blocks - 1, jnp.where(peers == row_index + 1, 0, -1)
    )
    request = jnp.concatenate([far_request, halo_request[:, None]], axis=1)
    wanted = lax.all_to_all(request, "rows", split_axis=0, concat_axis=0, tiled=True)
    usable = wanted >= 0
    safe_ids = jnp.maximum(wanted, 0)
    own_blocks = node_feats.reshape(blocks, tile_size, col_count)
    outgoing = jnp.where(
        usable[:, :, None, None], own_blocks[safe_ids], jnp.zeros((), jnp.bfloat16)
    )
    incoming = lax.all_to_all(outgoing, "rows", split_axis=0, concat_axis=0, tiled=True)
    low = lax.dynamic_index_in_dim(incoming, jnp.maximum(row_index - 1, 0), 0, keepdims=False)
    high = lax.dynamic_index_in_dim(
        incoming, jnp.minimum(row_index + 1, peer_count - 1), 0, keepdims=False
    )
    padded = jnp.concatenate([low[capacity], node_feats, high[capacity]], axis=0)
    windows = jnp.concatenate(
        [
            padded[offset * tile_size : offset * tile_size + rows_dev].reshape(
                blocks, tile_size, col_count
            )
            for offset in range(3)
        ],
        axis=1,
    )
    band_tiles = band_weights.reshape(blocks, tile_size, 3 * tile_size)
    band_sum = jnp.einsum("bij,bjc->bic", band_tiles, windows, preferred_element_type=jnp.float32)
    far_slots = incoming[:, :capacity].reshape(peer_count * capacity, tile_size, col_count)
    fetched = far_slots[slot_ids].reshape(blocks, fanout * tile_size, col_count)
    far_tiles = far_weights.reshape(blocks, tile_size, fanout * tile_size)
    far_sum = jnp.einsum("bij,bjc->bic", far_tiles, fetched, preferred_element_type=jnp.float32)
    degree = jnp.sum(band_weights.astype(jnp.float32), axis=1) + jnp.sum(
        far_weights.astype(jnp.float32), axis=1
    )
    neighbours = ((band_sum + far_sum).reshape(rows_dev, col_count) / degree[:, None]).astype(
        jnp.bfloat16
    )
    rows_self = lax.dynamic_slice_in_dim(w_self, col_start, col_count, 0)
    rows_neigh = lax.dynamic_slice_in_dim(w_neigh, col_start, col_count, 0)
    neighbours_all = lax.all_gather(neighbours, "feat", axis=1, tiled=True)
    preact_all = (
        jnp.dot(feats_all, w_self, preferred_element_type=jnp.float32)
        + jnp.dot(neighbours_all, w_neigh, preferred_element_type=jnp.float32)
        + bias_all
    )
    preact = lax.dynamic_slice_in_dim(preact_all, col_start, col_count, 1)
    layer_out = jax.nn.silu(preact).astype(jnp.bfloat16)
    sigmoid_z = jax.nn.sigmoid(preact_all)
    full_grad = (
        cotangent_all.astype(jnp.float32) * sigmoid_z * (1.0 + preact_all * (1.0 - sigmoid_z))
    ).astype(jnp.bfloat16)
    grad_scale = float(rows_dev * peer_count) ** (-0.5)
    part_self = jnp.einsum("rc,rf->cf", node_feats, full_grad, preferred_element_type=jnp.float32)
    part_neigh = jnp.einsum("rc,rf->cf", neighbours, full_grad, preferred_element_type=jnp.float32)
    sum_self, sum_neigh = summed_over(jnp.stack([part_self, part_neigh]), "rows")
    grad_self = sum_self * grad_scale
    grad_neigh = sum_neigh * grad_scale
    dense_grad = jnp.einsum("rf,cf->rc", full_grad, rows_self, preferred_element_type=jnp.float32)
    grad_agg = jnp.einsum("rf,cf->rc", full_grad, rows_neigh, preferred_element_type=jnp.float32)
    grad_neighbours = (grad_agg / degree[:, None]).astype(jnp.bfloat16)
    grad_blocks = grad_neighbours.reshape(blocks, tile_size, col_count)
    grad_windows = jnp.einsum(
        "bij,bic->bjc", band_tiles, grad_blocks, preferred_element_type=jnp.float32
    )
    grad_padded = jnp.zeros((rows_dev + 2 * tile_size, col_count), jnp.float32)
    for offset in range(3):
        piece = grad_windows[:, offset * tile_size : (offset + 1) * tile_size, :].reshape(
            rows_dev, col_count
        )
        grad_padded = grad_padded + jnp.pad(
            piece, ((offset * tile_size, (2 - offset) * tile_size), (0, 0))
        )
    top_rim = grad_padded[:tile_size]
    bottom_rim = grad_padded[rows_dev + tile_size :]
    from_below = from_behind(top_rim, "rows", -1)
    from_above = from_behind(bottom_rim, "rows", 1)
    grad_fetched = jnp.einsum(
        "bij,bic->bjc", far_tiles, grad_blocks, preferred_element_type=jnp.float32
    )
    returning = jnp.zeros((peer_count * capacity, tile_size, col_count), jnp.float32)
    returning = returning.at[slot_ids].set(grad_fetched.reshape(entries, tile_size, col_count))
    returned = lax.all_to_all(
        returning.reshape(peer_count, capacity, tile_size, col_count).astype(jnp.bfloat16),
        "rows",
        split_axis=0,
        concat_axis=0,
        tiled=True,
    ).astype(jnp.float32)
    target_block = jnp.where(usable, wanted, blocks)[:, :capacity].reshape(-1)
    owed = jnp.zeros((blocks, tile_size * col_count), jnp.float32)
    owed = owed.at[target_block].add(
        returned.reshape(peer_count * capacity, tile_size * col_count), mode="drop"
    )
    interior = (
        dense_grad
        + grad_padded[tile_size : tile_size + rows_dev]
        + owed.reshape(rows_dev, col_count)
    )
    interior = interior.at[:tile_size].add(from_above)
    grad_feats = interior.at[rows_dev - tile_size :].add(from_below)
    return (layer_out, grad_feats, grad_self, grad_neigh)


def solution(mesh):
    in_specs = (
        P("rows", "feat"),
        P("rows", None),
        P("rows", None),
        P("rows", None),
        P("rows", None),
        P(),
        P(),
        P("feat"),
        P("rows", "feat"),
    )
    out_specs = (P("rows", "feat"), P("rows", "feat"), P("feat", None), P("feat", None))
    return jax.shard_map(
        on_device, mesh=mesh, in_specs=in_specs, out_specs=out_specs, check_vma=False
    )
```

```python
import jax
import jax.numpy as jnp
from jax import lax
from jax.sharding import PartitionSpec as P


def from_behind(block, axis, distance):
    devices = range(lax.axis_size(axis))
    route = [(i - distance, i) for i in devices if i - distance in devices]
    return lax.ppermute(block, axis, route)


def summed_over(parts, axis):
    count = lax.axis_size(axis)
    flat = parts.reshape(count, -1)
    pieces = lax.all_to_all(flat, axis, split_axis=0, concat_axis=0, tiled=True)
    mine = jnp.sum(pieces, axis=0, keepdims=True)
    spread = jnp.broadcast_to(mine, flat.shape)
    whole = lax.all_to_all(spread, axis, split_axis=0, concat_axis=0, tiled=True)
    return whole.reshape(parts.shape)


def on_device(
    node_feats, band_weights, far_weights, far_owner, far_local, w_self, w_neigh, bias, cotangent
):
    rows_dev, col_count = node_feats.shape
    tile_size = band_weights.shape[1] // 3
    blocks = rows_dev // tile_size
    fanout = far_owner.shape[1]
    peer_count = lax.axis_size("rows")
    capacity = max(2, 2 * blocks * fanout // peer_count)
    row_index = lax.axis_index("rows")
    col_start = lax.axis_index("feat") * col_count
    bias_high = lax.reduce_precision(bias, exponent_bits=8, mantissa_bits=7)
    bias_rest = bias - bias_high
    bias_mid = lax.reduce_precision(bias_rest, exponent_bits=8, mantissa_bits=7)
    bias_parts = jnp.zeros((16, col_count), jnp.bfloat16)
    bias_parts = bias_parts.at[:3].set(
        jnp.stack([bias_high, bias_mid, bias_rest - bias_mid]).astype(jnp.bfloat16)
    )
    packed = jnp.concatenate([node_feats, cotangent, bias_parts], axis=0)
    gathered = lax.all_gather(packed, "feat", axis=1, tiled=True)
    feats_all = gathered[:rows_dev]
    cotangent_all = gathered[rows_dev : 2 * rows_dev]
    bias_rows = gathered[2 * rows_dev : 2 * rows_dev + 3].astype(jnp.float32)
    bias_all = (bias_rows[0] + bias_rows[1]) + bias_rows[2]
    owner_ids = far_owner.reshape(-1)
    local_ids = far_local.reshape(-1)
    entries = owner_ids.shape[0]
    same_owner = owner_ids[:, None] == owner_ids[None, :]
    earlier = jnp.arange(entries)[None, :] < jnp.arange(entries)[:, None]
    slot_rank = jnp.sum(jnp.where(same_owner & earlier, 1, 0), axis=1).astype(jnp.int32)
    slot_ids = owner_ids * capacity + slot_rank
    slot_hit = slot_ids[:, None] == jnp.arange(peer_count * capacity, dtype=jnp.int32)[None, :]
    request = (jnp.sum(jnp.where(slot_hit, local_ids[:, None] + 1, 0), axis=0) - 1).reshape(
        peer_count, capacity
    )
    peers = jnp.arange(peer_count, dtype=jnp.int32)[:, None, None]
    own_blocks = node_feats.reshape(blocks, tile_size, col_count)
    halo_out = jnp.where(
        peers == row_index - 1,
        own_blocks[0],
        jnp.where(peers == row_index + 1, own_blocks[blocks - 1], jnp.zeros((), jnp.bfloat16)),
    )
    request_rows = jnp.zeros((peer_count, 1, col_count), jnp.bfloat16)
    request_rows = request_rows.at[:, 0, :capacity].set(request.astype(jnp.bfloat16))
    first = lax.all_to_all(
        jnp.concatenate([halo_out, request_rows], axis=1),
        "rows",
        split_axis=0,
        concat_axis=0,
        tiled=True,
    )
    wanted = first[:, tile_size, :capacity].astype(jnp.int32)
    usable = wanted >= 0
    safe_ids = jnp.maximum(wanted, 0)
    outgoing = jnp.where(
        usable[:, :, None, None], own_blocks[safe_ids], jnp.zeros((), jnp.bfloat16)
    )
    incoming = lax.all_to_all(outgoing, "rows", split_axis=0, concat_axis=0, tiled=True)
    low = lax.dynamic_index_in_dim(first, jnp.maximum(row_index - 1, 0), 0, keepdims=False)
    high = lax.dynamic_index_in_dim(
        first, jnp.minimum(row_index + 1, peer_count - 1), 0, keepdims=False
    )
    padded = jnp.concatenate([low[:tile_size], node_feats, high[:tile_size]], axis=0)
    windows = jnp.concatenate(
        [
            padded[offset * tile_size : offset * tile_size + rows_dev].reshape(
                blocks, tile_size, col_count
            )
            for offset in range(3)
        ],
        axis=1,
    )
    band_tiles = band_weights.reshape(blocks, tile_size, 3 * tile_size)
    band_sum = jnp.einsum("bij,bjc->bic", band_tiles, windows, preferred_element_type=jnp.float32)
    fetched = incoming.reshape(peer_count * capacity, tile_size, col_count)[slot_ids].reshape(
        blocks, fanout * tile_size, col_count
    )
    far_tiles = far_weights.reshape(blocks, tile_size, fanout * tile_size)
    far_sum = jnp.einsum("bij,bjc->bic", far_tiles, fetched, preferred_element_type=jnp.float32)
    degree = jnp.sum(band_weights.astype(jnp.float32), axis=1) + jnp.sum(
        far_weights.astype(jnp.float32), axis=1
    )
    neighbours = ((band_sum + far_sum).reshape(rows_dev, col_count) / degree[:, None]).astype(
        jnp.bfloat16
    )
    rows_self = lax.dynamic_slice_in_dim(w_self, col_start, col_count, 0)
    rows_neigh = lax.dynamic_slice_in_dim(w_neigh, col_start, col_count, 0)
    neighbours_all = lax.all_gather(neighbours, "feat", axis=1, tiled=True)
    preact_all = (
        jnp.dot(feats_all, w_self, preferred_element_type=jnp.float32)
        + jnp.dot(neighbours_all, w_neigh, preferred_element_type=jnp.float32)
        + bias_all
    )
    preact = lax.dynamic_slice_in_dim(preact_all, col_start, col_count, 1)
    layer_out = jax.nn.silu(preact).astype(jnp.bfloat16)
    sigmoid_z = jax.nn.sigmoid(preact_all)
    full_grad = (
        cotangent_all.astype(jnp.float32) * sigmoid_z * (1.0 + preact_all * (1.0 - sigmoid_z))
    ).astype(jnp.bfloat16)
    grad_scale = float(rows_dev * peer_count) ** (-0.5)
    part_self = jnp.einsum("rc,rf->cf", node_feats, full_grad, preferred_element_type=jnp.float32)
    part_neigh = jnp.einsum("rc,rf->cf", neighbours, full_grad, preferred_element_type=jnp.float32)
    sum_self, sum_neigh = summed_over(jnp.stack([part_self, part_neigh]), "rows")
    grad_self = sum_self * grad_scale
    grad_neigh = sum_neigh * grad_scale
    dense_grad = jnp.einsum("rf,cf->rc", full_grad, rows_self, preferred_element_type=jnp.float32)
    grad_agg = jnp.einsum("rf,cf->rc", full_grad, rows_neigh, preferred_element_type=jnp.float32)
    grad_neighbours = (grad_agg / degree[:, None]).astype(jnp.bfloat16)
    grad_blocks = grad_neighbours.reshape(blocks, tile_size, col_count)
    grad_windows = jnp.einsum(
        "bij,bic->bjc", band_tiles, grad_blocks, preferred_element_type=jnp.float32
    )
    grad_padded = jnp.zeros((rows_dev + 2 * tile_size, col_count), jnp.float32)
    for offset in range(3):
        piece = grad_windows[:, offset * tile_size : (offset + 1) * tile_size, :].reshape(
            rows_dev, col_count
        )
        grad_padded = grad_padded + jnp.pad(
            piece, ((offset * tile_size, (2 - offset) * tile_size), (0, 0))
        )
    top_rim = grad_padded[:tile_size]
    bottom_rim = grad_padded[rows_dev + tile_size :]
    from_below = from_behind(top_rim, "rows", -1)
    from_above = from_behind(bottom_rim, "rows", 1)
    grad_fetched = jnp.einsum(
        "bij,bic->bjc", far_tiles, grad_blocks, preferred_element_type=jnp.float32
    )
    returning = jnp.zeros((peer_count * capacity, tile_size, col_count), jnp.float32)
    returning = returning.at[slot_ids].set(grad_fetched.reshape(entries, tile_size, col_count))
    returned = lax.all_to_all(
        returning.reshape(peer_count, capacity, tile_size, col_count).astype(jnp.bfloat16),
        "rows",
        split_axis=0,
        concat_axis=0,
        tiled=True,
    ).astype(jnp.float32)
    target_block = jnp.where(usable, wanted, blocks).reshape(-1)
    owed = jnp.zeros((blocks, tile_size * col_count), jnp.float32)
    owed = owed.at[target_block].add(
        returned.reshape(peer_count * capacity, tile_size * col_count), mode="drop"
    )
    interior = (
        dense_grad
        + grad_padded[tile_size : tile_size + rows_dev]
        + owed.reshape(rows_dev, col_count)
    )
    interior = interior.at[:tile_size].add(from_above)
    grad_feats = interior.at[rows_dev - tile_size :].add(from_below)
    return (layer_out, grad_feats, grad_self, grad_neigh)


def solution(mesh):
    in_specs = (
        P("rows", "feat"),
        P("rows", None),
        P("rows", None),
        P("rows", None),
        P("rows", None),
        P(),
        P(),
        P("feat"),
        P("rows", "feat"),
    )
    out_specs = (P("rows", "feat"), P("rows", "feat"), P("feat", None), P("feat", None))
    return jax.shard_map(
        on_device, mesh=mesh, in_specs=in_specs, out_specs=out_specs, check_vma=False
    )
```

```python
import jax
import jax.numpy as jnp
from jax import lax
from jax.sharding import PartitionSpec as P


def extended(block, sides, width):
    for axis, dim in sides:
        count = lax.axis_size(axis)
        forward = [(i, i + 1) for i in range(count - 1)]
        backward = [(target, source) for source, target in forward]
        low = lax.ppermute(
            lax.slice_in_dim(block, block.shape[dim] - width, None, axis=dim), axis, forward
        )
        high = lax.ppermute(lax.slice_in_dim(block, 0, width, axis=dim), axis, backward)
        block = jnp.concatenate([low, block, high], axis=dim)
    return block


def from_behind(block, axis, distance):
    devices = range(lax.axis_size(axis))
    route = [(i - distance, i) for i in devices if i - distance in devices]
    return lax.ppermute(block, axis, route)


def on_device(
    node_feats, band_weights, far_weights, far_owner, far_local, w_self, w_neigh, bias, cotangent
):
    rows_dev, col_count = node_feats.shape
    tile_size = band_weights.shape[1] // 3
    blocks = rows_dev // tile_size
    fanout = far_owner.shape[1]
    peer_count = lax.axis_size("rows")
    capacity = max(2, 2 * blocks * fanout // peer_count)
    col_start = lax.axis_index("feat") * col_count
    bias_high = lax.reduce_precision(bias, exponent_bits=8, mantissa_bits=7)
    bias_rest = bias - bias_high
    bias_mid = lax.reduce_precision(bias_rest, exponent_bits=8, mantissa_bits=7)
    bias_parts = jnp.zeros((16, col_count), jnp.bfloat16)
    bias_parts = bias_parts.at[:3].set(
        jnp.stack([bias_high, bias_mid, bias_rest - bias_mid]).astype(jnp.bfloat16)
    )
    packed = jnp.concatenate([node_feats, cotangent, bias_parts], axis=0)
    gathered = lax.all_gather(packed, "feat", axis=1, tiled=True)
    feats_all = gathered[:rows_dev]
    cotangent_all = gathered[rows_dev : 2 * rows_dev]
    bias_rows = gathered[2 * rows_dev : 2 * rows_dev + 3].astype(jnp.float32)
    bias_all = (bias_rows[0] + bias_rows[1]) + bias_rows[2]
    padded = extended(node_feats, (("rows", 0),), tile_size)
    windows = jnp.concatenate(
        [
            padded[offset * tile_size : offset * tile_size + rows_dev].reshape(
                blocks, tile_size, col_count
            )
            for offset in range(3)
        ],
        axis=1,
    )
    band_tiles = band_weights.reshape(blocks, tile_size, 3 * tile_size)
    band_sum = jnp.einsum("bij,bjc->bic", band_tiles, windows, preferred_element_type=jnp.float32)
    owner_ids = far_owner.reshape(-1)
    local_ids = far_local.reshape(-1)
    entries = owner_ids.shape[0]
    same_owner = owner_ids[:, None] == owner_ids[None, :]
    earlier = jnp.arange(entries)[None, :] < jnp.arange(entries)[:, None]
    slot_rank = jnp.sum(jnp.where(same_owner & earlier, 1, 0), axis=1).astype(jnp.int32)
    slot_ids = owner_ids * capacity + slot_rank
    slot_hit = slot_ids[:, None] == jnp.arange(peer_count * capacity, dtype=jnp.int32)[None, :]
    request = (jnp.sum(jnp.where(slot_hit, local_ids[:, None] + 1, 0), axis=0) - 1).reshape(
        peer_count, capacity
    )
    wanted = lax.all_to_all(request, "rows", split_axis=0, concat_axis=0, tiled=True)
    usable = wanted >= 0
    safe_ids = jnp.maximum(wanted, 0)
    own_blocks = node_feats.reshape(blocks, tile_size, col_count)
    outgoing = jnp.where(
        usable[:, :, None, None], own_blocks[safe_ids], jnp.zeros((), jnp.bfloat16)
    )
    incoming = lax.all_to_all(outgoing, "rows", split_axis=0, concat_axis=0, tiled=True)
    fetched = incoming.reshape(peer_count * capacity, tile_size, col_count)[slot_ids].reshape(
        blocks, fanout * tile_size, col_count
    )
    far_tiles = far_weights.reshape(blocks, tile_size, fanout * tile_size)
    far_sum = jnp.einsum("bij,bjc->bic", far_tiles, fetched, preferred_element_type=jnp.float32)
    degree = jnp.sum(band_weights.astype(jnp.float32), axis=1) + jnp.sum(
        far_weights.astype(jnp.float32), axis=1
    )
    neighbours = ((band_sum + far_sum).reshape(rows_dev, col_count) / degree[:, None]).astype(
        jnp.bfloat16
    )
    rows_self = lax.dynamic_slice_in_dim(w_self, col_start, col_count, 0)
    rows_neigh = lax.dynamic_slice_in_dim(w_neigh, col_start, col_count, 0)
    neighbours_all = lax.all_gather(neighbours, "feat", axis=1, tiled=True)
    preact_all = (
        jnp.dot(feats_all, w_self, preferred_element_type=jnp.float32)
        + jnp.dot(neighbours_all, w_neigh, preferred_element_type=jnp.float32)
        + bias_all
    )
    preact = lax.dynamic_slice_in_dim(preact_all, col_start, col_count, 1)
    layer_out = jax.nn.silu(preact).astype(jnp.bfloat16)
    sigmoid_z = jax.nn.sigmoid(preact_all)
    full_grad = (
        cotangent_all.astype(jnp.float32) * sigmoid_z * (1.0 + preact_all * (1.0 - sigmoid_z))
    ).astype(jnp.bfloat16)
    grad_scale = float(rows_dev * peer_count) ** (-0.5)
    part_self = jnp.einsum("rc,rf->cf", node_feats, full_grad, preferred_element_type=jnp.float32)
    part_neigh = jnp.einsum("rc,rf->cf", neighbours, full_grad, preferred_element_type=jnp.float32)
    dense_grad = jnp.einsum("rf,cf->rc", full_grad, rows_self, preferred_element_type=jnp.float32)
    grad_agg = jnp.einsum("rf,cf->rc", full_grad, rows_neigh, preferred_element_type=jnp.float32)
    grad_neighbours = (grad_agg / degree[:, None]).astype(jnp.bfloat16)
    grad_blocks = grad_neighbours.reshape(blocks, tile_size, col_count)
    grad_windows = jnp.einsum(
        "bij,bic->bjc", band_tiles, grad_blocks, preferred_element_type=jnp.float32
    )
    grad_padded = jnp.zeros((rows_dev + 2 * tile_size, col_count), jnp.float32)
    for offset in range(3):
        piece = grad_windows[:, offset * tile_size : (offset + 1) * tile_size, :].reshape(
            rows_dev, col_count
        )
        grad_padded = grad_padded + jnp.pad(
            piece, ((offset * tile_size, (2 - offset) * tile_size), (0, 0))
        )
    top_rim = grad_padded[:tile_size]
    bottom_rim = grad_padded[rows_dev + tile_size :]
    from_below = from_behind(top_rim, "rows", -1)
    from_above = from_behind(bottom_rim, "rows", 1)
    grad_fetched = jnp.einsum(
        "bij,bic->bjc", far_tiles, grad_blocks, preferred_element_type=jnp.float32
    )
    returning = jnp.zeros((peer_count * capacity, tile_size, col_count), jnp.float32)
    returning = returning.at[slot_ids].set(grad_fetched.reshape(entries, tile_size, col_count))
    partials = jnp.stack([part_self, part_neigh]).reshape(peer_count, -1)
    high = lax.reduce_precision(partials, exponent_bits=8, mantissa_bits=7)
    coded = jnp.stack(
        [high.astype(jnp.bfloat16), (partials - high).astype(jnp.bfloat16)], axis=1
    ).reshape(peer_count, 1, -1, col_count)
    coded_rows = coded.shape[2]
    coded = jnp.pad(coded, ((0, 0), (0, 0), (0, tile_size - coded_rows), (0, 0)))
    payload = jnp.concatenate(
        [
            returning.reshape(peer_count, capacity, tile_size, col_count).astype(jnp.bfloat16),
            coded,
        ],
        axis=1,
    )
    arrived = lax.all_to_all(payload, "rows", split_axis=0, concat_axis=0, tiled=True)
    returned = arrived[:, :capacity].astype(jnp.float32)
    codes = arrived[:, capacity, :coded_rows].reshape(peer_count, 2, -1).astype(jnp.float32)
    mine = jnp.sum(codes[:, 0] + codes[:, 1], axis=0, keepdims=True)
    whole = lax.all_to_all(
        jnp.broadcast_to(mine, partials.shape), "rows", split_axis=0, concat_axis=0, tiled=True
    )
    sum_self, sum_neigh = whole.reshape(2, col_count, -1)
    grad_self = sum_self * grad_scale
    grad_neigh = sum_neigh * grad_scale
    target_block = jnp.where(usable, wanted, blocks).reshape(-1)
    owed = jnp.zeros((blocks, tile_size * col_count), jnp.float32)
    owed = owed.at[target_block].add(
        returned.reshape(peer_count * capacity, tile_size * col_count), mode="drop"
    )
    interior = (
        dense_grad
        + grad_padded[tile_size : tile_size + rows_dev]
        + owed.reshape(rows_dev, col_count)
    )
    interior = interior.at[:tile_size].add(from_above)
    grad_feats = interior.at[rows_dev - tile_size :].add(from_below)
    return (layer_out, grad_feats, grad_self, grad_neigh)


def solution(mesh):
    in_specs = (
        P("rows", "feat"),
        P("rows", None),
        P("rows", None),
        P("rows", None),
        P("rows", None),
        P(),
        P(),
        P("feat"),
        P("rows", "feat"),
    )
    out_specs = (P("rows", "feat"), P("rows", "feat"), P("feat", None), P("feat", None))
    return jax.shard_map(
        on_device, mesh=mesh, in_specs=in_specs, out_specs=out_specs, check_vma=False
    )
```

```python
import jax
import jax.numpy as jnp
from jax import lax
from jax.sharding import PartitionSpec as P


def extended(block, sides, width):
    for axis, dim in sides:
        count = lax.axis_size(axis)
        forward = [(i, i + 1) for i in range(count - 1)]
        backward = [(target, source) for source, target in forward]
        low = lax.ppermute(
            lax.slice_in_dim(block, block.shape[dim] - width, None, axis=dim), axis, forward
        )
        high = lax.ppermute(lax.slice_in_dim(block, 0, width, axis=dim), axis, backward)
        block = jnp.concatenate([low, block, high], axis=dim)
    return block


def from_behind(block, axis, distance):
    devices = range(lax.axis_size(axis))
    route = [(i - distance, i) for i in devices if i - distance in devices]
    return lax.ppermute(block, axis, route)


def on_device(
    node_feats, band_weights, far_weights, far_owner, far_local, w_self, w_neigh, bias, cotangent
):
    rows_dev, col_count = node_feats.shape
    tile_size = band_weights.shape[1] // 3
    blocks = rows_dev // tile_size
    fanout = far_owner.shape[1]
    peer_count = lax.axis_size("rows")
    capacity = max(2, 2 * blocks * fanout // peer_count)
    col_start = lax.axis_index("feat") * col_count
    bias_high = lax.reduce_precision(bias, exponent_bits=8, mantissa_bits=7)
    bias_rest = bias - bias_high
    bias_mid = lax.reduce_precision(bias_rest, exponent_bits=8, mantissa_bits=7)
    bias_parts = jnp.zeros((16, col_count), jnp.bfloat16)
    bias_parts = bias_parts.at[:3].set(
        jnp.stack([bias_high, bias_mid, bias_rest - bias_mid]).astype(jnp.bfloat16)
    )
    packed = jnp.concatenate([node_feats, cotangent, bias_parts], axis=0)
    gathered = lax.all_gather(packed, "feat", axis=1, tiled=True)
    feats_all = gathered[:rows_dev]
    cotangent_all = gathered[rows_dev : 2 * rows_dev]
    bias_rows = gathered[2 * rows_dev : 2 * rows_dev + 3].astype(jnp.float32)
    bias_all = (bias_rows[0] + bias_rows[1]) + bias_rows[2]
    padded = extended(node_feats, (("rows", 0),), tile_size)
    windows = jnp.concatenate(
        [
            padded[offset * tile_size : offset * tile_size + rows_dev].reshape(
                blocks, tile_size, col_count
            )
            for offset in range(3)
        ],
        axis=1,
    )
    band_tiles = band_weights.reshape(blocks, tile_size, 3 * tile_size)
    band_sum = jnp.einsum("bij,bjc->bic", band_tiles, windows, preferred_element_type=jnp.float32)
    owner_ids = far_owner.reshape(-1)
    local_ids = far_local.reshape(-1)
    entries = owner_ids.shape[0]
    same_owner = owner_ids[:, None] == owner_ids[None, :]
    earlier = jnp.arange(entries)[None, :] < jnp.arange(entries)[:, None]
    slot_rank = jnp.sum(jnp.where(same_owner & earlier, 1, 0), axis=1).astype(jnp.int32)
    slot_ids = owner_ids * capacity + slot_rank
    slot_hit = slot_ids[:, None] == jnp.arange(peer_count * capacity, dtype=jnp.int32)[None, :]
    request = (jnp.sum(jnp.where(slot_hit, local_ids[:, None] + 1, 0), axis=0) - 1).reshape(
        peer_count, capacity
    )
    wanted = lax.all_to_all(request, "rows", split_axis=0, concat_axis=0, tiled=True)
    usable = wanted >= 0
    safe_ids = jnp.maximum(wanted, 0)
    own_blocks = node_feats.reshape(blocks, tile_size, col_count)
    outgoing = jnp.where(
        usable[:, :, None, None], own_blocks[safe_ids], jnp.zeros((), jnp.bfloat16)
    )
    incoming = lax.all_to_all(outgoing, "rows", split_axis=0, concat_axis=0, tiled=True)
    fetched = incoming.reshape(peer_count * capacity, tile_size, col_count)[slot_ids].reshape(
        blocks, fanout * tile_size, col_count
    )
    far_tiles = far_weights.reshape(blocks, tile_size, fanout * tile_size)
    far_sum = jnp.einsum("bij,bjc->bic", far_tiles, fetched, preferred_element_type=jnp.float32)
    degree = jnp.sum(band_weights.astype(jnp.float32), axis=1) + jnp.sum(
        far_weights.astype(jnp.float32), axis=1
    )
    neighbours = ((band_sum + far_sum).reshape(rows_dev, col_count) / degree[:, None]).astype(
        jnp.bfloat16
    )
    rows_self = lax.dynamic_slice_in_dim(w_self, col_start, col_count, 0)
    rows_neigh = lax.dynamic_slice_in_dim(w_neigh, col_start, col_count, 0)
    neighbours_all = lax.all_gather(neighbours, "feat", axis=1, tiled=True)
    preact_all = (
        jnp.dot(feats_all, w_self, preferred_element_type=jnp.float32)
        + jnp.dot(neighbours_all, w_neigh, preferred_element_type=jnp.float32)
        + bias_all
    )
    preact = lax.dynamic_slice_in_dim(preact_all, col_start, col_count, 1)
    layer_out = jax.nn.silu(preact).astype(jnp.bfloat16)
    sigmoid_z = jax.nn.sigmoid(preact_all)
    full_grad = (
        cotangent_all.astype(jnp.float32) * sigmoid_z * (1.0 + preact_all * (1.0 - sigmoid_z))
    ).astype(jnp.bfloat16)
    grad_scale = float(rows_dev * peer_count) ** (-0.5)
    part_self = jnp.einsum("rc,rf->cf", node_feats, full_grad, preferred_element_type=jnp.float32)
    part_neigh = jnp.einsum("rc,rf->cf", neighbours, full_grad, preferred_element_type=jnp.float32)
    dense_grad = jnp.einsum("rf,cf->rc", full_grad, rows_self, preferred_element_type=jnp.float32)
    grad_agg = jnp.einsum("rf,cf->rc", full_grad, rows_neigh, preferred_element_type=jnp.float32)
    grad_neighbours = (grad_agg / degree[:, None]).astype(jnp.bfloat16)
    grad_blocks = grad_neighbours.reshape(blocks, tile_size, col_count)
    grad_windows = jnp.einsum(
        "bij,bic->bjc", band_tiles, grad_blocks, preferred_element_type=jnp.float32
    )
    grad_padded = jnp.zeros((rows_dev + 2 * tile_size, col_count), jnp.float32)
    for offset in range(3):
        piece = grad_windows[:, offset * tile_size : (offset + 1) * tile_size, :].reshape(
            rows_dev, col_count
        )
        grad_padded = grad_padded + jnp.pad(
            piece, ((offset * tile_size, (2 - offset) * tile_size), (0, 0))
        )
    top_rim = grad_padded[:tile_size]
    bottom_rim = grad_padded[rows_dev + tile_size :]
    from_below = from_behind(top_rim, "rows", -1)
    from_above = from_behind(bottom_rim, "rows", 1)
    grad_fetched = jnp.einsum(
        "bij,bic->bjc", far_tiles, grad_blocks, preferred_element_type=jnp.float32
    )
    returning = jnp.zeros((peer_count * capacity, tile_size, col_count), jnp.float32)
    returning = returning.at[slot_ids].set(grad_fetched.reshape(entries, tile_size, col_count))
    partials = jnp.stack([part_self, part_neigh]).reshape(peer_count, -1)
    high = lax.reduce_precision(partials, exponent_bits=8, mantissa_bits=7)
    coded = jnp.stack(
        [high.astype(jnp.bfloat16), (partials - high).astype(jnp.bfloat16)], axis=1
    ).reshape(peer_count, 1, -1, col_count)
    coded_rows = coded.shape[2]
    span = capacity * tile_size
    payload = jnp.concatenate(
        [
            returning.reshape(peer_count, span, col_count).astype(jnp.bfloat16),
            coded.reshape(peer_count, coded_rows, col_count),
        ],
        axis=1,
    )
    arrived = lax.all_to_all(payload, "rows", split_axis=0, concat_axis=0, tiled=True)
    returned = arrived[:, :span].reshape(peer_count * capacity, tile_size, col_count)
    codes = arrived[:, span:].reshape(peer_count, 2, -1).astype(jnp.float32)
    mine = jnp.sum(codes[:, 0] + codes[:, 1], axis=0, keepdims=True)
    whole = lax.all_to_all(
        jnp.broadcast_to(mine, partials.shape), "rows", split_axis=0, concat_axis=0, tiled=True
    )
    sum_self, sum_neigh = whole.reshape(2, col_count, -1)
    grad_self = sum_self * grad_scale
    grad_neigh = sum_neigh * grad_scale
    target_block = jnp.where(usable, wanted, blocks).reshape(-1)
    routing = (target_block[None, :] == jnp.arange(blocks, dtype=jnp.int32)[:, None]).astype(
        jnp.bfloat16
    )
    owed = jnp.einsum("bs,sjc->bjc", routing, returned, preferred_element_type=jnp.float32)
    interior = (
        dense_grad
        + grad_padded[tile_size : tile_size + rows_dev]
        + owed.reshape(rows_dev, col_count)
    )
    interior = interior.at[:tile_size].add(from_above)
    grad_feats = interior.at[rows_dev - tile_size :].add(from_below)
    return (layer_out, grad_feats, grad_self, grad_neigh)


def solution(mesh):
    in_specs = (
        P("rows", "feat"),
        P("rows", None),
        P("rows", None),
        P("rows", None),
        P("rows", None),
        P(),
        P(),
        P("feat"),
        P("rows", "feat"),
    )
    out_specs = (P("rows", "feat"), P("rows", "feat"), P("feat", None), P("feat", None))
    return jax.shard_map(
        on_device, mesh=mesh, in_specs=in_specs, out_specs=out_specs, check_vma=False
    )
```

```python
import jax
import jax.numpy as jnp
from jax import lax
from jax.sharding import PartitionSpec as P


def extended(block, sides, width):
    for axis, dim in sides:
        count = lax.axis_size(axis)
        forward = [(i, i + 1) for i in range(count - 1)]
        backward = [(target, source) for source, target in forward]
        low = lax.ppermute(
            lax.slice_in_dim(block, block.shape[dim] - width, None, axis=dim), axis, forward
        )
        high = lax.ppermute(lax.slice_in_dim(block, 0, width, axis=dim), axis, backward)
        block = jnp.concatenate([low, block, high], axis=dim)
    return block


def from_behind(block, axis, distance):
    devices = range(lax.axis_size(axis))
    route = [(i - distance, i) for i in devices if i - distance in devices]
    return lax.ppermute(block, axis, route)


def on_device(
    node_feats, band_weights, far_weights, far_owner, far_local, w_self, w_neigh, bias, cotangent
):
    rows_dev, col_count = node_feats.shape
    tile_size = band_weights.shape[1] // 3
    blocks = rows_dev // tile_size
    fanout = far_owner.shape[1]
    peer_count = lax.axis_size("rows")
    capacity = max(2, 2 * blocks * fanout // peer_count)
    col_start = lax.axis_index("feat") * col_count
    bias_high = lax.reduce_precision(bias, exponent_bits=8, mantissa_bits=7)
    bias_rest = bias - bias_high
    bias_mid = lax.reduce_precision(bias_rest, exponent_bits=8, mantissa_bits=7)
    bias_parts = jnp.zeros((16, col_count), jnp.bfloat16)
    bias_parts = bias_parts.at[:3].set(
        jnp.stack([bias_high, bias_mid, bias_rest - bias_mid]).astype(jnp.bfloat16)
    )
    packed = jnp.concatenate([node_feats, cotangent, bias_parts], axis=0)
    gathered = lax.all_gather(packed, "feat", axis=1, tiled=True)
    feats_all = gathered[:rows_dev]
    cotangent_all = gathered[rows_dev : 2 * rows_dev]
    bias_rows = gathered[2 * rows_dev : 2 * rows_dev + 3].astype(jnp.float32)
    bias_all = (bias_rows[0] + bias_rows[1]) + bias_rows[2]
    padded = extended(node_feats, (("rows", 0),), tile_size)
    windows = jnp.concatenate(
        [
            padded[offset * tile_size : offset * tile_size + rows_dev].reshape(
                blocks, tile_size, col_count
            )
            for offset in range(3)
        ],
        axis=1,
    )
    band_tiles = band_weights.reshape(blocks, tile_size, 3 * tile_size)
    band_sum = jnp.einsum("bij,bjc->bic", band_tiles, windows, preferred_element_type=jnp.float32)
    owner_ids = far_owner.reshape(-1)
    local_ids = far_local.reshape(-1)
    entries = owner_ids.shape[0]
    same_owner = owner_ids[:, None] == owner_ids[None, :]
    earlier = jnp.arange(entries)[None, :] < jnp.arange(entries)[:, None]
    slot_rank = jnp.sum(jnp.where(same_owner & earlier, 1, 0), axis=1).astype(jnp.int32)
    slot_ids = owner_ids * capacity + slot_rank
    slot_hit = slot_ids[:, None] == jnp.arange(peer_count * capacity, dtype=jnp.int32)[None, :]
    request = (jnp.sum(jnp.where(slot_hit, local_ids[:, None] + 1, 0), axis=0) - 1).reshape(
        peer_count, capacity
    )
    wanted = lax.all_to_all(request, "rows", split_axis=0, concat_axis=0, tiled=True)
    usable = wanted >= 0
    safe_ids = jnp.maximum(wanted, 0)
    own_blocks = node_feats.reshape(blocks, tile_size, col_count)
    outgoing = jnp.where(
        usable[:, :, None, None], own_blocks[safe_ids], jnp.zeros((), jnp.bfloat16)
    )
    incoming = lax.all_to_all(outgoing, "rows", split_axis=0, concat_axis=0, tiled=True)
    fetched = incoming.reshape(peer_count * capacity, tile_size, col_count)[slot_ids].reshape(
        blocks, fanout * tile_size, col_count
    )
    far_tiles = far_weights.reshape(blocks, tile_size, fanout * tile_size)
    far_sum = jnp.einsum("bij,bjc->bic", far_tiles, fetched, preferred_element_type=jnp.float32)
    degree = jnp.sum(band_weights.astype(jnp.float32), axis=1) + jnp.sum(
        far_weights.astype(jnp.float32), axis=1
    )
    neighbours = ((band_sum + far_sum).reshape(rows_dev, col_count) / degree[:, None]).astype(
        jnp.bfloat16
    )
    rows_self = lax.dynamic_slice_in_dim(w_self, col_start, col_count, 0)
    rows_neigh = lax.dynamic_slice_in_dim(w_neigh, col_start, col_count, 0)
    neighbours_all = lax.all_gather(neighbours, "feat", axis=1, tiled=True)
    preact_all = (
        jnp.dot(feats_all, w_self, preferred_element_type=jnp.float32)
        + jnp.dot(neighbours_all, w_neigh, preferred_element_type=jnp.float32)
        + bias_all
    )
    preact = lax.dynamic_slice_in_dim(preact_all, col_start, col_count, 1)
    layer_out = jax.nn.silu(preact).astype(jnp.bfloat16)
    sigmoid_z = jax.nn.sigmoid(preact_all)
    full_grad = (
        cotangent_all.astype(jnp.float32) * sigmoid_z * (1.0 + preact_all * (1.0 - sigmoid_z))
    ).astype(jnp.bfloat16)
    grad_scale = float(rows_dev * peer_count) ** (-0.5)
    part_self = jnp.einsum("rc,rf->cf", node_feats, full_grad, preferred_element_type=jnp.float32)
    part_neigh = jnp.einsum("rc,rf->cf", neighbours, full_grad, preferred_element_type=jnp.float32)
    dense_grad = jnp.einsum("rf,cf->rc", full_grad, rows_self, preferred_element_type=jnp.float32)
    grad_agg = jnp.einsum("rf,cf->rc", full_grad, rows_neigh, preferred_element_type=jnp.float32)
    grad_neighbours = (grad_agg / degree[:, None]).astype(jnp.bfloat16)
    grad_blocks = grad_neighbours.reshape(blocks, tile_size, col_count)
    grad_windows = jnp.einsum(
        "bij,bic->bjc", band_tiles, grad_blocks, preferred_element_type=jnp.float32
    )
    grad_padded = jnp.zeros((rows_dev + 2 * tile_size, col_count), jnp.float32)
    for offset in range(3):
        piece = grad_windows[:, offset * tile_size : (offset + 1) * tile_size, :].reshape(
            rows_dev, col_count
        )
        grad_padded = grad_padded + jnp.pad(
            piece, ((offset * tile_size, (2 - offset) * tile_size), (0, 0))
        )
    top_rim = grad_padded[:tile_size]
    bottom_rim = grad_padded[rows_dev + tile_size :]
    from_below = from_behind(top_rim, "rows", -1)
    from_above = from_behind(bottom_rim, "rows", 1)
    grad_fetched = jnp.einsum(
        "bij,bic->bjc", far_tiles, grad_blocks, preferred_element_type=jnp.float32
    )
    returning = jnp.zeros((peer_count * capacity, tile_size, col_count), jnp.float32)
    returning = returning.at[slot_ids].set(grad_fetched.reshape(entries, tile_size, col_count))
    feat_count = lax.axis_size("feat")
    feat_index = lax.axis_index("feat")
    slotted = jnp.zeros((2, feat_count, col_count, feat_count * col_count), jnp.float32)
    slotted = lax.dynamic_update_index_in_dim(
        slotted, jnp.stack([part_self, part_neigh])[:, None], feat_index, 1
    )
    summed = lax.psum(slotted, ("rows", "feat"))
    sum_self, sum_neigh = lax.dynamic_index_in_dim(summed, feat_index, 1, keepdims=False)
    grad_self = sum_self * grad_scale
    grad_neigh = sum_neigh * grad_scale
    returned = lax.all_to_all(
        returning.reshape(peer_count, capacity, tile_size, col_count).astype(jnp.bfloat16),
        "rows",
        split_axis=0,
        concat_axis=0,
        tiled=True,
    ).astype(jnp.float32)
    target_block = jnp.where(usable, wanted, blocks).reshape(-1)
    owed = jnp.zeros((blocks, tile_size * col_count), jnp.float32)
    owed = owed.at[target_block].add(
        returned.reshape(peer_count * capacity, tile_size * col_count), mode="drop"
    )
    interior = (
        dense_grad
        + grad_padded[tile_size : tile_size + rows_dev]
        + owed.reshape(rows_dev, col_count)
    )
    interior = interior.at[:tile_size].add(from_above)
    grad_feats = interior.at[rows_dev - tile_size :].add(from_below)
    return (layer_out, grad_feats, grad_self, grad_neigh)


def solution(mesh):
    in_specs = (
        P("rows", "feat"),
        P("rows", None),
        P("rows", None),
        P("rows", None),
        P("rows", None),
        P(),
        P(),
        P("feat"),
        P("rows", "feat"),
    )
    out_specs = (P("rows", "feat"), P("rows", "feat"), P("feat", None), P("feat", None))
    return jax.shard_map(
        on_device, mesh=mesh, in_specs=in_specs, out_specs=out_specs, check_vma=False
    )
```

```python
import jax
import jax.numpy as jnp
from jax import lax
from jax.sharding import PartitionSpec as P


def extended(block, sides, width):
    for axis, dim in sides:
        count = lax.axis_size(axis)
        forward = [(i, i + 1) for i in range(count - 1)]
        backward = [(target, source) for source, target in forward]
        low = lax.ppermute(
            lax.slice_in_dim(block, block.shape[dim] - width, None, axis=dim), axis, forward
        )
        high = lax.ppermute(lax.slice_in_dim(block, 0, width, axis=dim), axis, backward)
        block = jnp.concatenate([low, block, high], axis=dim)
    return block


def from_behind(block, axis, distance):
    devices = range(lax.axis_size(axis))
    route = [(i - distance, i) for i in devices if i - distance in devices]
    return lax.ppermute(block, axis, route)


def on_device(
    node_feats, band_weights, far_weights, far_owner, far_local, w_self, w_neigh, bias, cotangent
):
    rows_dev, col_count = node_feats.shape
    tile_size = band_weights.shape[1] // 3
    blocks = rows_dev // tile_size
    fanout = far_owner.shape[1]
    peer_count = lax.axis_size("rows")
    capacity = max(2, 2 * blocks * fanout // peer_count)
    col_start = lax.axis_index("feat") * col_count
    bias_high = lax.reduce_precision(bias, exponent_bits=8, mantissa_bits=7)
    bias_rest = bias - bias_high
    bias_mid = lax.reduce_precision(bias_rest, exponent_bits=8, mantissa_bits=7)
    bias_parts = jnp.zeros((16, col_count), jnp.bfloat16)
    bias_parts = bias_parts.at[:3].set(
        jnp.stack([bias_high, bias_mid, bias_rest - bias_mid]).astype(jnp.bfloat16)
    )
    packed = jnp.concatenate([node_feats, cotangent, bias_parts], axis=0)
    gathered = lax.all_gather(packed, "feat", axis=1, tiled=True)
    feats_all = gathered[:rows_dev]
    cotangent_all = gathered[rows_dev : 2 * rows_dev]
    bias_rows = gathered[2 * rows_dev : 2 * rows_dev + 3].astype(jnp.float32)
    bias_all = (bias_rows[0] + bias_rows[1]) + bias_rows[2]
    padded = extended(node_feats, (("rows", 0),), tile_size)
    windows = jnp.concatenate(
        [
            padded[offset * tile_size : offset * tile_size + rows_dev].reshape(
                blocks, tile_size, col_count
            )
            for offset in range(3)
        ],
        axis=1,
    )
    band_tiles = band_weights.reshape(blocks, tile_size, 3 * tile_size)
    band_sum = jnp.einsum("bij,bjc->bic", band_tiles, windows, preferred_element_type=jnp.float32)
    owner_ids = far_owner.reshape(-1)
    local_ids = far_local.reshape(-1)
    entries = owner_ids.shape[0]
    same_owner = owner_ids[:, None] == owner_ids[None, :]
    earlier = jnp.arange(entries)[None, :] < jnp.arange(entries)[:, None]
    slot_rank = jnp.sum(jnp.where(same_owner & earlier, 1, 0), axis=1).astype(jnp.int32)
    slot_ids = owner_ids * capacity + slot_rank
    table = lax.all_gather(jnp.stack([far_owner, far_local]), "rows", axis=1, tiled=True)
    every_owner = table[0].reshape(peer_count, entries)
    every_local = table[1].reshape(peer_count, entries)
    peer_same = every_owner[:, :, None] == every_owner[:, None, :]
    peer_rank = jnp.sum(jnp.where(peer_same & earlier[None], 1, 0), axis=2)
    to_me = every_owner == lax.axis_index("rows")
    wanted = (
        jnp.sum(
            jnp.where(
                to_me[:, :, None]
                & (peer_rank[:, :, None] == jnp.arange(capacity, dtype=jnp.int32)[None, None, :]),
                every_local[:, :, None] + 1,
                0,
            ),
            axis=1,
        )
        - 1
    )
    usable = wanted >= 0
    safe_ids = jnp.maximum(wanted, 0)
    own_blocks = node_feats.reshape(blocks, tile_size, col_count)
    outgoing = jnp.where(
        usable[:, :, None, None], own_blocks[safe_ids], jnp.zeros((), jnp.bfloat16)
    )
    incoming = lax.all_to_all(outgoing, "rows", split_axis=0, concat_axis=0, tiled=True)
    fetched = incoming.reshape(peer_count * capacity, tile_size, col_count)[slot_ids].reshape(
        blocks, fanout * tile_size, col_count
    )
    far_tiles = far_weights.reshape(blocks, tile_size, fanout * tile_size)
    far_sum = jnp.einsum("bij,bjc->bic", far_tiles, fetched, preferred_element_type=jnp.float32)
    degree = jnp.sum(band_weights.astype(jnp.float32), axis=1) + jnp.sum(
        far_weights.astype(jnp.float32), axis=1
    )
    neighbours = ((band_sum + far_sum).reshape(rows_dev, col_count) / degree[:, None]).astype(
        jnp.bfloat16
    )
    rows_self = lax.dynamic_slice_in_dim(w_self, col_start, col_count, 0)
    rows_neigh = lax.dynamic_slice_in_dim(w_neigh, col_start, col_count, 0)
    neighbours_all = lax.all_gather(neighbours, "feat", axis=1, tiled=True)
    preact_all = (
        jnp.dot(feats_all, w_self, preferred_element_type=jnp.float32)
        + jnp.dot(neighbours_all, w_neigh, preferred_element_type=jnp.float32)
        + bias_all
    )
    preact = lax.dynamic_slice_in_dim(preact_all, col_start, col_count, 1)
    layer_out = jax.nn.silu(preact).astype(jnp.bfloat16)
    sigmoid_z = jax.nn.sigmoid(preact_all)
    full_grad = (
        cotangent_all.astype(jnp.float32) * sigmoid_z * (1.0 + preact_all * (1.0 - sigmoid_z))
    ).astype(jnp.bfloat16)
    grad_scale = float(rows_dev * peer_count) ** (-0.5)
    part_self = jnp.einsum("rc,rf->cf", node_feats, full_grad, preferred_element_type=jnp.float32)
    part_neigh = jnp.einsum("rc,rf->cf", neighbours, full_grad, preferred_element_type=jnp.float32)
    dense_grad = jnp.einsum("rf,cf->rc", full_grad, rows_self, preferred_element_type=jnp.float32)
    grad_agg = jnp.einsum("rf,cf->rc", full_grad, rows_neigh, preferred_element_type=jnp.float32)
    grad_neighbours = (grad_agg / degree[:, None]).astype(jnp.bfloat16)
    grad_blocks = grad_neighbours.reshape(blocks, tile_size, col_count)
    grad_windows = jnp.einsum(
        "bij,bic->bjc", band_tiles, grad_blocks, preferred_element_type=jnp.float32
    )
    grad_padded = jnp.zeros((rows_dev + 2 * tile_size, col_count), jnp.float32)
    for offset in range(3):
        piece = grad_windows[:, offset * tile_size : (offset + 1) * tile_size, :].reshape(
            rows_dev, col_count
        )
        grad_padded = grad_padded + jnp.pad(
            piece, ((offset * tile_size, (2 - offset) * tile_size), (0, 0))
        )
    top_rim = grad_padded[:tile_size]
    bottom_rim = grad_padded[rows_dev + tile_size :]
    from_below = from_behind(top_rim, "rows", -1)
    from_above = from_behind(bottom_rim, "rows", 1)
    grad_fetched = jnp.einsum(
        "bij,bic->bjc", far_tiles, grad_blocks, preferred_element_type=jnp.float32
    )
    returning = jnp.zeros((peer_count * capacity, tile_size, col_count), jnp.float32)
    returning = returning.at[slot_ids].set(grad_fetched.reshape(entries, tile_size, col_count))
    partials = jnp.stack([part_self, part_neigh]).reshape(peer_count, -1)
    high = lax.reduce_precision(partials, exponent_bits=8, mantissa_bits=7)
    coded = jnp.stack(
        [high.astype(jnp.bfloat16), (partials - high).astype(jnp.bfloat16)], axis=1
    ).reshape(peer_count, 1, -1, col_count)
    coded_rows = coded.shape[2]
    coded = jnp.pad(coded, ((0, 0), (0, 0), (0, tile_size - coded_rows), (0, 0)))
    payload = jnp.concatenate(
        [
            returning.reshape(peer_count, capacity, tile_size, col_count).astype(jnp.bfloat16),
            coded,
        ],
        axis=1,
    )
    arrived = lax.all_to_all(payload, "rows", split_axis=0, concat_axis=0, tiled=True)
    returned = arrived[:, :capacity].astype(jnp.float32)
    codes = arrived[:, capacity, :coded_rows].reshape(peer_count, 2, -1).astype(jnp.float32)
    mine = jnp.sum(codes[:, 0] + codes[:, 1], axis=0, keepdims=True)
    whole = lax.all_to_all(
        jnp.broadcast_to(mine, partials.shape), "rows", split_axis=0, concat_axis=0, tiled=True
    )
    sum_self, sum_neigh = whole.reshape(2, col_count, -1)
    grad_self = sum_self * grad_scale
    grad_neigh = sum_neigh * grad_scale
    target_block = jnp.where(usable, wanted, blocks).reshape(-1)
    owed = jnp.zeros((blocks, tile_size * col_count), jnp.float32)
    owed = owed.at[target_block].add(
        returned.reshape(peer_count * capacity, tile_size * col_count), mode="drop"
    )
    interior = (
        dense_grad
        + grad_padded[tile_size : tile_size + rows_dev]
        + owed.reshape(rows_dev, col_count)
    )
    interior = interior.at[:tile_size].add(from_above)
    grad_feats = interior.at[rows_dev - tile_size :].add(from_below)
    return (layer_out, grad_feats, grad_self, grad_neigh)


def solution(mesh):
    in_specs = (
        P("rows", "feat"),
        P("rows", None),
        P("rows", None),
        P("rows", None),
        P("rows", None),
        P(),
        P(),
        P("feat"),
        P("rows", "feat"),
    )
    out_specs = (P("rows", "feat"), P("rows", "feat"), P("feat", None), P("feat", None))
    return jax.shard_map(
        on_device, mesh=mesh, in_specs=in_specs, out_specs=out_specs, check_vma=False
    )
```

```python
import jax
import jax.numpy as jnp
from jax import lax
from jax.sharding import PartitionSpec as P


def extended(block, sides, width):
    for axis, dim in sides:
        count = lax.axis_size(axis)
        forward = [(i, i + 1) for i in range(count - 1)]
        backward = [(target, source) for source, target in forward]
        low = lax.ppermute(
            lax.slice_in_dim(block, block.shape[dim] - width, None, axis=dim), axis, forward
        )
        high = lax.ppermute(lax.slice_in_dim(block, 0, width, axis=dim), axis, backward)
        block = jnp.concatenate([low, block, high], axis=dim)
    return block


def from_behind(block, axis, distance):
    devices = range(lax.axis_size(axis))
    route = [(i - distance, i) for i in devices if i - distance in devices]
    return lax.ppermute(block, axis, route)


def on_device(
    node_feats, band_weights, far_weights, far_owner, far_local, w_self, w_neigh, bias, cotangent
):
    rows_dev, col_count = node_feats.shape
    tile_size = band_weights.shape[1] // 3
    blocks = rows_dev // tile_size
    fanout = far_owner.shape[1]
    peer_count = lax.axis_size("rows")
    capacity = max(2, 2 * blocks * fanout // peer_count)
    col_start = lax.axis_index("feat") * col_count
    bias_high = lax.reduce_precision(bias, exponent_bits=8, mantissa_bits=7)
    bias_rest = bias - bias_high
    bias_mid = lax.reduce_precision(bias_rest, exponent_bits=8, mantissa_bits=7)
    bias_parts = jnp.zeros((16, col_count), jnp.bfloat16)
    bias_parts = bias_parts.at[:3].set(
        jnp.stack([bias_high, bias_mid, bias_rest - bias_mid]).astype(jnp.bfloat16)
    )
    packed = jnp.concatenate([node_feats, cotangent, bias_parts], axis=0)
    gathered = lax.all_gather(packed, "feat", axis=1, tiled=True)
    feats_all = gathered[:rows_dev]
    cotangent_all = gathered[rows_dev : 2 * rows_dev]
    bias_rows = gathered[2 * rows_dev : 2 * rows_dev + 3].astype(jnp.float32)
    bias_all = (bias_rows[0] + bias_rows[1]) + bias_rows[2]
    padded = extended(node_feats, (("rows", 0),), tile_size)
    windows = jnp.concatenate(
        [
            padded[offset * tile_size : offset * tile_size + rows_dev].reshape(
                blocks, tile_size, col_count
            )
            for offset in range(3)
        ],
        axis=1,
    )
    band_tiles = band_weights.reshape(blocks, tile_size, 3 * tile_size)
    band_sum = jnp.einsum("bij,bjc->bic", band_tiles, windows, preferred_element_type=jnp.float32)
    owner_ids = far_owner.reshape(-1)
    local_ids = far_local.reshape(-1)
    entries = owner_ids.shape[0]
    same_owner = owner_ids[:, None] == owner_ids[None, :]
    earlier = jnp.arange(entries)[None, :] < jnp.arange(entries)[:, None]
    slot_rank = jnp.sum(jnp.where(same_owner & earlier, 1, 0), axis=1).astype(jnp.int32)
    slot_ids = owner_ids * capacity + slot_rank
    slot_hit = slot_ids[:, None] == jnp.arange(peer_count * capacity, dtype=jnp.int32)[None, :]
    request = (jnp.sum(jnp.where(slot_hit, local_ids[:, None] + 1, 0), axis=0) - 1).reshape(
        peer_count, capacity
    )
    wanted = lax.all_to_all(request, "rows", split_axis=0, concat_axis=0, tiled=True)
    usable = wanted >= 0
    safe_ids = jnp.maximum(wanted, 0)
    own_blocks = node_feats.reshape(blocks, tile_size, col_count)
    outgoing = jnp.where(
        usable[:, :, None, None], own_blocks[safe_ids], jnp.zeros((), jnp.bfloat16)
    )
    incoming = lax.all_to_all(outgoing, "rows", split_axis=0, concat_axis=0, tiled=True)
    fetched = incoming.reshape(peer_count * capacity, tile_size, col_count)[slot_ids].reshape(
        blocks, fanout * tile_size, col_count
    )
    far_tiles = far_weights.reshape(blocks, tile_size, fanout * tile_size)
    far_sum = jnp.einsum("bij,bjc->bic", far_tiles, fetched, preferred_element_type=jnp.float32)
    degree = jnp.sum(band_weights.astype(jnp.float32), axis=1) + jnp.sum(
        far_weights.astype(jnp.float32), axis=1
    )
    neighbours = ((band_sum + far_sum).reshape(rows_dev, col_count) / degree[:, None]).astype(
        jnp.bfloat16
    )
    rows_self = lax.dynamic_slice_in_dim(w_self, col_start, col_count, 0)
    rows_neigh = lax.dynamic_slice_in_dim(w_neigh, col_start, col_count, 0)
    neighbours_all = lax.all_gather(neighbours, "feat", axis=1, tiled=True)
    preact_all = (
        jnp.dot(feats_all, w_self, preferred_element_type=jnp.float32)
        + jnp.dot(neighbours_all, w_neigh, preferred_element_type=jnp.float32)
        + bias_all
    )
    preact = lax.dynamic_slice_in_dim(preact_all, col_start, col_count, 1)
    layer_out = jax.nn.silu(preact).astype(jnp.bfloat16)
    sigmoid_z = jax.nn.sigmoid(preact_all)
    full_grad = (
        cotangent_all.astype(jnp.float32) * sigmoid_z * (1.0 + preact_all * (1.0 - sigmoid_z))
    ).astype(jnp.bfloat16)
    grad_scale = float(rows_dev * peer_count) ** (-0.5)
    part_self = jnp.einsum("rc,rf->cf", node_feats, full_grad, preferred_element_type=jnp.float32)
    part_neigh = jnp.einsum("rc,rf->cf", neighbours, full_grad, preferred_element_type=jnp.float32)
    dense_grad = jnp.einsum("rf,cf->rc", full_grad, rows_self, preferred_element_type=jnp.float32)
    grad_agg = jnp.einsum("rf,cf->rc", full_grad, rows_neigh, preferred_element_type=jnp.float32)
    grad_neighbours = (grad_agg / degree[:, None]).astype(jnp.bfloat16)
    grad_blocks = grad_neighbours.reshape(blocks, tile_size, col_count)
    grad_windows = jnp.einsum(
        "bij,bic->bjc", band_tiles, grad_blocks, preferred_element_type=jnp.float32
    )
    grad_padded = jnp.zeros((rows_dev + 2 * tile_size, col_count), jnp.float32)
    for offset in range(3):
        piece = grad_windows[:, offset * tile_size : (offset + 1) * tile_size, :].reshape(
            rows_dev, col_count
        )
        grad_padded = grad_padded + jnp.pad(
            piece, ((offset * tile_size, (2 - offset) * tile_size), (0, 0))
        )
    top_rim = grad_padded[:tile_size]
    bottom_rim = grad_padded[rows_dev + tile_size :]
    from_below = from_behind(top_rim, "rows", -1)
    from_above = from_behind(bottom_rim, "rows", 1)
    grad_fetched = jnp.einsum(
        "bij,bic->bjc", far_tiles, grad_blocks, preferred_element_type=jnp.float32
    )
    returning = jnp.zeros((peer_count * capacity, tile_size, col_count), jnp.float32)
    returning = returning.at[slot_ids].set(grad_fetched.reshape(entries, tile_size, col_count))
    partials = jnp.stack([part_self, part_neigh]).reshape(peer_count, -1)
    high = lax.reduce_precision(partials, exponent_bits=8, mantissa_bits=7)
    coded = jnp.stack(
        [high.astype(jnp.bfloat16), (partials - high).astype(jnp.bfloat16)], axis=1
    ).reshape(peer_count, capacity, tile_size, -1)
    payload = jnp.concatenate(
        [
            returning.reshape(peer_count, capacity, tile_size, col_count).astype(jnp.bfloat16),
            coded,
        ],
        axis=3,
    )
    arrived = lax.all_to_all(payload, "rows", split_axis=0, concat_axis=0, tiled=True)
    returned = arrived[..., :col_count].astype(jnp.float32)
    codes = arrived[..., col_count:].reshape(peer_count, 2, -1).astype(jnp.float32)
    mine = jnp.sum(codes[:, 0] + codes[:, 1], axis=0, keepdims=True)
    whole = lax.all_to_all(
        jnp.broadcast_to(mine, partials.shape), "rows", split_axis=0, concat_axis=0, tiled=True
    )
    sum_self, sum_neigh = whole.reshape(2, col_count, -1)
    grad_self = sum_self * grad_scale
    grad_neigh = sum_neigh * grad_scale
    target_block = jnp.where(usable, wanted, blocks).reshape(-1)
    owed = jnp.zeros((blocks, tile_size * col_count), jnp.float32)
    owed = owed.at[target_block].add(
        returned.reshape(peer_count * capacity, tile_size * col_count), mode="drop"
    )
    interior = (
        dense_grad
        + grad_padded[tile_size : tile_size + rows_dev]
        + owed.reshape(rows_dev, col_count)
    )
    interior = interior.at[:tile_size].add(from_above)
    grad_feats = interior.at[rows_dev - tile_size :].add(from_below)
    return (layer_out, grad_feats, grad_self, grad_neigh)


def solution(mesh):
    in_specs = (
        P("rows", "feat"),
        P("rows", None),
        P("rows", None),
        P("rows", None),
        P("rows", None),
        P(),
        P(),
        P("feat"),
        P("rows", "feat"),
    )
    out_specs = (P("rows", "feat"), P("rows", "feat"), P("feat", None), P("feat", None))
    return jax.shard_map(
        on_device, mesh=mesh, in_specs=in_specs, out_specs=out_specs, check_vma=False
    )
```

```python
import jax
import jax.numpy as jnp
from jax import lax
from jax.sharding import PartitionSpec as P


def extended(block, sides, width):
    for axis, dim in sides:
        count = lax.axis_size(axis)
        forward = [(i, i + 1) for i in range(count - 1)]
        backward = [(target, source) for source, target in forward]
        low = lax.ppermute(
            lax.slice_in_dim(block, block.shape[dim] - width, None, axis=dim), axis, forward
        )
        high = lax.ppermute(lax.slice_in_dim(block, 0, width, axis=dim), axis, backward)
        block = jnp.concatenate([low, block, high], axis=dim)
    return block


def from_behind(block, axis, distance):
    devices = range(lax.axis_size(axis))
    route = [(i - distance, i) for i in devices if i - distance in devices]
    return lax.ppermute(block, axis, route)


def on_device(
    node_feats, band_weights, far_weights, far_owner, far_local, w_self, w_neigh, bias, cotangent
):
    rows_dev, col_count = node_feats.shape
    tile_size = band_weights.shape[1] // 3
    blocks = rows_dev // tile_size
    fanout = far_owner.shape[1]
    peer_count = lax.axis_size("rows")
    capacity = max(2, 2 * blocks * fanout // peer_count)
    col_start = lax.axis_index("feat") * col_count
    bias_high = lax.reduce_precision(bias, exponent_bits=8, mantissa_bits=7)
    bias_rest = bias - bias_high
    bias_mid = lax.reduce_precision(bias_rest, exponent_bits=8, mantissa_bits=7)
    bias_parts = jnp.zeros((16, col_count), jnp.bfloat16)
    bias_parts = bias_parts.at[:3].set(
        jnp.stack([bias_high, bias_mid, bias_rest - bias_mid]).astype(jnp.bfloat16)
    )
    packed = jnp.concatenate([node_feats, cotangent, bias_parts], axis=0)
    gathered = lax.all_gather(packed, "feat", axis=1, tiled=True)
    feats_all = gathered[:rows_dev]
    cotangent_all = gathered[rows_dev : 2 * rows_dev]
    bias_rows = gathered[2 * rows_dev : 2 * rows_dev + 3].astype(jnp.float32)
    bias_all = (bias_rows[0] + bias_rows[1]) + bias_rows[2]
    padded = extended(node_feats, (("rows", 0),), tile_size)
    windows = jnp.concatenate(
        [
            padded[offset * tile_size : offset * tile_size + rows_dev].reshape(
                blocks, tile_size, col_count
            )
            for offset in range(3)
        ],
        axis=1,
    )
    band_tiles = band_weights.reshape(blocks, tile_size, 3 * tile_size)
    band_sum = jnp.einsum("bij,bjc->bic", band_tiles, windows, preferred_element_type=jnp.float32)
    owner_ids = far_owner.reshape(-1)
    local_ids = far_local.reshape(-1)
    entries = owner_ids.shape[0]
    same_owner = owner_ids[:, None] == owner_ids[None, :]
    earlier = jnp.arange(entries)[None, :] < jnp.arange(entries)[:, None]
    slot_rank = jnp.sum(jnp.where(same_owner & earlier, 1, 0), axis=1).astype(jnp.int32)
    slot_ids = owner_ids * capacity + slot_rank
    slot_hit = slot_ids[:, None] == jnp.arange(peer_count * capacity, dtype=jnp.int32)[None, :]
    request = (jnp.sum(jnp.where(slot_hit, local_ids[:, None] + 1, 0), axis=0) - 1).reshape(
        peer_count, capacity
    )
    wanted = lax.all_to_all(request, "rows", split_axis=0, concat_axis=0, tiled=True)
    usable = wanted >= 0
    safe_ids = jnp.maximum(wanted, 0)
    own_blocks = node_feats.reshape(blocks, tile_size, col_count)
    outgoing = jnp.where(
        usable[:, :, None, None], own_blocks[safe_ids], jnp.zeros((), jnp.bfloat16)
    )
    incoming = lax.all_to_all(outgoing, "rows", split_axis=0, concat_axis=0, tiled=True)
    fetched = incoming.reshape(peer_count * capacity, tile_size, col_count)[slot_ids].reshape(
        blocks, fanout * tile_size, col_count
    )
    far_tiles = far_weights.reshape(blocks, tile_size, fanout * tile_size)
    far_sum = jnp.einsum("bij,bjc->bic", far_tiles, fetched, preferred_element_type=jnp.float32)
    degree = jnp.sum(band_weights.astype(jnp.float32), axis=1) + jnp.sum(
        far_weights.astype(jnp.float32), axis=1
    )
    neighbours = ((band_sum + far_sum).reshape(rows_dev, col_count) / degree[:, None]).astype(
        jnp.bfloat16
    )
    rows_self = lax.dynamic_slice_in_dim(w_self, col_start, col_count, 0)
    rows_neigh = lax.dynamic_slice_in_dim(w_neigh, col_start, col_count, 0)
    neighbours_all = lax.all_gather(neighbours, "feat", axis=1, tiled=True)
    preact_all = (
        jnp.dot(feats_all, w_self, preferred_element_type=jnp.float32)
        + jnp.dot(neighbours_all, w_neigh, preferred_element_type=jnp.float32)
        + bias_all
    )
    preact = lax.dynamic_slice_in_dim(preact_all, col_start, col_count, 1)
    layer_out = jax.nn.silu(preact).astype(jnp.bfloat16)
    sigmoid_z = jax.nn.sigmoid(preact_all)
    full_grad = (
        cotangent_all.astype(jnp.float32) * sigmoid_z * (1.0 + preact_all * (1.0 - sigmoid_z))
    ).astype(jnp.bfloat16)
    grad_scale = float(rows_dev * peer_count) ** (-0.5)
    part_self = jnp.einsum("rc,rf->cf", node_feats, full_grad, preferred_element_type=jnp.float32)
    part_neigh = jnp.einsum("rc,rf->cf", neighbours, full_grad, preferred_element_type=jnp.float32)
    dense_grad = jnp.einsum("rf,cf->rc", full_grad, rows_self, preferred_element_type=jnp.float32)
    grad_agg = jnp.einsum("rf,cf->rc", full_grad, rows_neigh, preferred_element_type=jnp.float32)
    grad_neighbours = (grad_agg / degree[:, None]).astype(jnp.bfloat16)
    grad_blocks = grad_neighbours.reshape(blocks, tile_size, col_count)
    grad_windows = jnp.einsum(
        "bij,bic->bjc", band_tiles, grad_blocks, preferred_element_type=jnp.float32
    )
    grad_padded = jnp.zeros((rows_dev + 2 * tile_size, col_count), jnp.float32)
    for offset in range(3):
        piece = grad_windows[:, offset * tile_size : (offset + 1) * tile_size, :].reshape(
            rows_dev, col_count
        )
        grad_padded = grad_padded + jnp.pad(
            piece, ((offset * tile_size, (2 - offset) * tile_size), (0, 0))
        )
    top_rim = grad_padded[:tile_size]
    bottom_rim = grad_padded[rows_dev + tile_size :]
    from_below = from_behind(top_rim, "rows", -1)
    from_above = from_behind(bottom_rim, "rows", 1)
    grad_fetched = jnp.einsum(
        "bij,bic->bjc", far_tiles, grad_blocks, preferred_element_type=jnp.float32
    )
    returning = jnp.zeros((peer_count * capacity, tile_size, col_count), jnp.float32)
    returning = returning.at[slot_ids].set(grad_fetched.reshape(entries, tile_size, col_count))
    partials = jnp.stack([part_self, part_neigh]).reshape(peer_count, -1)
    high = lax.reduce_precision(partials, exponent_bits=8, mantissa_bits=7)
    coded = jnp.stack(
        [high.astype(jnp.bfloat16), (partials - high).astype(jnp.bfloat16)], axis=1
    ).reshape(peer_count, capacity, tile_size, -1)
    payload = jnp.concatenate(
        [
            returning.reshape(peer_count, capacity, tile_size, col_count).astype(jnp.bfloat16),
            coded,
        ],
        axis=3,
    )
    arrived = lax.all_to_all(payload, "rows", split_axis=0, concat_axis=0, tiled=True)
    returned = arrived[..., :col_count]
    codes = arrived[..., col_count:].reshape(peer_count, 2, -1).astype(jnp.float32)
    mine = jnp.sum(codes[:, 0] + codes[:, 1], axis=0, keepdims=True)
    whole = lax.all_to_all(
        jnp.broadcast_to(mine, partials.shape), "rows", split_axis=0, concat_axis=0, tiled=True
    )
    sum_self, sum_neigh = whole.reshape(2, col_count, -1)
    grad_self = sum_self * grad_scale
    grad_neigh = sum_neigh * grad_scale
    target_block = jnp.where(usable, wanted, blocks)
    routing = (
        target_block[None] == jnp.arange(blocks, dtype=jnp.int32)[:, None, None]
    ).astype(jnp.bfloat16)
    owed = jnp.einsum("bps,psjc->bjc", routing, returned, preferred_element_type=jnp.float32)
    interior = (
        dense_grad
        + grad_padded[tile_size : tile_size + rows_dev]
        + owed.reshape(rows_dev, col_count)
    )
    interior = interior.at[:tile_size].add(from_above)
    grad_feats = interior.at[rows_dev - tile_size :].add(from_below)
    return (layer_out, grad_feats, grad_self, grad_neigh)


def solution(mesh):
    in_specs = (
        P("rows", "feat"),
        P("rows", None),
        P("rows", None),
        P("rows", None),
        P("rows", None),
        P(),
        P(),
        P("feat"),
        P("rows", "feat"),
    )
    out_specs = (P("rows", "feat"), P("rows", "feat"), P("feat", None), P("feat", None))
    return jax.shard_map(
        on_device, mesh=mesh, in_specs=in_specs, out_specs=out_specs, check_vma=False
    )
```

```python
import jax
import jax.numpy as jnp
from jax import lax
from jax.sharding import PartitionSpec as P


def extended(block, sides, width):
    for axis, dim in sides:
        count = lax.axis_size(axis)
        forward = [(i, i + 1) for i in range(count - 1)]
        backward = [(target, source) for source, target in forward]
        low = lax.ppermute(
            lax.slice_in_dim(block, block.shape[dim] - width, None, axis=dim), axis, forward
        )
        high = lax.ppermute(lax.slice_in_dim(block, 0, width, axis=dim), axis, backward)
        block = jnp.concatenate([low, block, high], axis=dim)
    return block


def from_behind(block, axis, distance):
    devices = range(lax.axis_size(axis))
    route = [(i - distance, i) for i in devices if i - distance in devices]
    return lax.ppermute(block, axis, route)


def on_device(
    node_feats, band_weights, far_weights, far_owner, far_local, w_self, w_neigh, bias, cotangent
):
    rows_dev, col_count = node_feats.shape
    tile_size = band_weights.shape[1] // 3
    blocks = rows_dev // tile_size
    fanout = far_owner.shape[1]
    peer_count = lax.axis_size("rows")
    capacity = max(2, 2 * blocks * fanout // peer_count)
    col_start = lax.axis_index("feat") * col_count
    bias_high = lax.reduce_precision(bias, exponent_bits=8, mantissa_bits=7)
    bias_rest = bias - bias_high
    bias_mid = lax.reduce_precision(bias_rest, exponent_bits=8, mantissa_bits=7)
    bias_parts = jnp.zeros((16, col_count), jnp.bfloat16)
    bias_parts = bias_parts.at[:3].set(
        jnp.stack([bias_high, bias_mid, bias_rest - bias_mid]).astype(jnp.bfloat16)
    )
    packed = jnp.concatenate([node_feats, cotangent, bias_parts], axis=0)
    gathered = lax.all_gather(packed, "feat", axis=1, tiled=True)
    feats_all = gathered[:rows_dev]
    cotangent_all = gathered[rows_dev : 2 * rows_dev]
    bias_rows = gathered[2 * rows_dev : 2 * rows_dev + 3].astype(jnp.float32)
    bias_all = (bias_rows[0] + bias_rows[1]) + bias_rows[2]
    padded = extended(node_feats, (("rows", 0),), tile_size)
    windows = jnp.concatenate(
        [
            padded[offset * tile_size : offset * tile_size + rows_dev].reshape(
                blocks, tile_size, col_count
            )
            for offset in range(3)
        ],
        axis=1,
    )
    band_tiles = band_weights.reshape(blocks, tile_size, 3 * tile_size)
    band_sum = jnp.einsum("bij,bjc->bic", band_tiles, windows, preferred_element_type=jnp.float32)
    owner_ids = far_owner.reshape(-1)
    local_ids = far_local.reshape(-1)
    entries = owner_ids.shape[0]
    same_owner = owner_ids[:, None] == owner_ids[None, :]
    earlier = jnp.arange(entries)[None, :] < jnp.arange(entries)[:, None]
    slot_rank = jnp.sum(jnp.where(same_owner & earlier, 1, 0), axis=1).astype(jnp.int32)
    slot_ids = owner_ids * capacity + slot_rank
    slot_hit = slot_ids[:, None] == jnp.arange(peer_count * capacity, dtype=jnp.int32)[None, :]
    request = (jnp.sum(jnp.where(slot_hit, local_ids[:, None] + 1, 0), axis=0) - 1).reshape(
        peer_count, capacity
    )
    wanted = lax.all_to_all(request, "rows", split_axis=0, concat_axis=0, tiled=True)
    usable = wanted >= 0
    safe_ids = jnp.maximum(wanted, 0)
    own_blocks = node_feats.reshape(blocks, tile_size, col_count)
    outgoing = jnp.where(
        usable[:, :, None, None], own_blocks[safe_ids], jnp.zeros((), jnp.bfloat16)
    )
    incoming = lax.all_to_all(outgoing, "rows", split_axis=0, concat_axis=0, tiled=True)
    fetched = incoming.reshape(peer_count * capacity, tile_size, col_count)[slot_ids].reshape(
        blocks, fanout * tile_size, col_count
    )
    far_tiles = far_weights.reshape(blocks, tile_size, fanout * tile_size)
    far_sum = jnp.einsum("bij,bjc->bic", far_tiles, fetched, preferred_element_type=jnp.float32)
    degree = jnp.sum(band_weights.astype(jnp.float32), axis=1) + jnp.sum(
        far_weights.astype(jnp.float32), axis=1
    )
    neighbours = ((band_sum + far_sum).reshape(rows_dev, col_count) / degree[:, None]).astype(
        jnp.bfloat16
    )
    rows_self = lax.dynamic_slice_in_dim(w_self, col_start, col_count, 0)
    rows_neigh = lax.dynamic_slice_in_dim(w_neigh, col_start, col_count, 0)
    neighbours_all = lax.all_gather(neighbours, "feat", axis=1, tiled=True)
    preact_all = (
        jnp.dot(feats_all, w_self, preferred_element_type=jnp.float32)
        + jnp.dot(neighbours_all, w_neigh, preferred_element_type=jnp.float32)
        + bias_all
    )
    preact = lax.dynamic_slice_in_dim(preact_all, col_start, col_count, 1)
    layer_out = jax.nn.silu(preact).astype(jnp.bfloat16)
    sigmoid_z = jax.nn.sigmoid(preact_all)
    full_grad = (
        cotangent_all.astype(jnp.float32) * sigmoid_z * (1.0 + preact_all * (1.0 - sigmoid_z))
    ).astype(jnp.bfloat16)
    grad_scale = float(rows_dev * peer_count) ** (-0.5)
    part_self = jnp.einsum("rc,rf->cf", node_feats, full_grad, preferred_element_type=jnp.float32)
    part_neigh = jnp.einsum("rc,rf->cf", neighbours, full_grad, preferred_element_type=jnp.float32)
    dense_grad = jnp.einsum("rf,cf->rc", full_grad, rows_self, preferred_element_type=jnp.float32)
    grad_agg = jnp.einsum("rf,cf->rc", full_grad, rows_neigh, preferred_element_type=jnp.float32)
    grad_neighbours = (grad_agg / degree[:, None]).astype(jnp.bfloat16)
    grad_blocks = grad_neighbours.reshape(blocks, tile_size, col_count)
    grad_windows = jnp.einsum(
        "bij,bic->bjc", band_tiles, grad_blocks, preferred_element_type=jnp.float32
    )
    grad_padded = jnp.zeros((rows_dev + 2 * tile_size, col_count), jnp.float32)
    for offset in range(3):
        piece = grad_windows[:, offset * tile_size : (offset + 1) * tile_size, :].reshape(
            rows_dev, col_count
        )
        grad_padded = grad_padded + jnp.pad(
            piece, ((offset * tile_size, (2 - offset) * tile_size), (0, 0))
        )
    top_rim = grad_padded[:tile_size]
    bottom_rim = grad_padded[rows_dev + tile_size :]
    from_below = from_behind(top_rim, "rows", -1)
    from_above = from_behind(bottom_rim, "rows", 1)
    grad_fetched = jnp.einsum(
        "bij,bic->bjc", far_tiles, grad_blocks, preferred_element_type=jnp.float32
    )
    placing = (
        slot_ids[None, None, :]
        == (jnp.arange(peer_count, dtype=jnp.int32)[:, None, None] * capacity
            + jnp.arange(capacity, dtype=jnp.int32)[None, :, None])
    ).astype(jnp.bfloat16)
    returning = jnp.einsum(
        "pse,ejc->psjc",
        placing,
        grad_fetched.reshape(entries, tile_size, col_count).astype(jnp.bfloat16),
        preferred_element_type=jnp.float32,
    )
    partials = jnp.stack([part_self, part_neigh]).reshape(peer_count, -1)
    high = lax.reduce_precision(partials, exponent_bits=8, mantissa_bits=7)
    coded = jnp.stack(
        [high.astype(jnp.bfloat16), (partials - high).astype(jnp.bfloat16)], axis=1
    ).reshape(peer_count, capacity, tile_size, -1)
    payload = jnp.concatenate(
        [
            returning.reshape(peer_count, capacity, tile_size, col_count).astype(jnp.bfloat16),
            coded,
        ],
        axis=3,
    )
    arrived = lax.all_to_all(payload, "rows", split_axis=0, concat_axis=0, tiled=True)
    returned = arrived[..., :col_count]
    codes = arrived[..., col_count:].reshape(peer_count, 2, -1).astype(jnp.float32)
    mine = jnp.sum(codes[:, 0] + codes[:, 1], axis=0, keepdims=True)
    whole = lax.all_to_all(
        jnp.broadcast_to(mine, partials.shape), "rows", split_axis=0, concat_axis=0, tiled=True
    )
    sum_self, sum_neigh = whole.reshape(2, col_count, -1)
    grad_self = sum_self * grad_scale
    grad_neigh = sum_neigh * grad_scale
    target_block = jnp.where(usable, wanted, blocks)
    routing = (
        target_block[None] == jnp.arange(blocks, dtype=jnp.int32)[:, None, None]
    ).astype(jnp.bfloat16)
    owed = jnp.einsum("bps,psjc->bjc", routing, returned, preferred_element_type=jnp.float32)
    interior = (
        dense_grad
        + grad_padded[tile_size : tile_size + rows_dev]
        + owed.reshape(rows_dev, col_count)
    )
    interior = interior.at[:tile_size].add(from_above)
    grad_feats = interior.at[rows_dev - tile_size :].add(from_below)
    return (layer_out, grad_feats, grad_self, grad_neigh)


def solution(mesh):
    in_specs = (
        P("rows", "feat"),
        P("rows", None),
        P("rows", None),
        P("rows", None),
        P("rows", None),
        P(),
        P(),
        P("feat"),
        P("rows", "feat"),
    )
    out_specs = (P("rows", "feat"), P("rows", "feat"), P("feat", None), P("feat", None))
    return jax.shard_map(
        on_device, mesh=mesh, in_specs=in_specs, out_specs=out_specs, check_vma=False
    )
```

```python
import jax
import jax.numpy as jnp
from jax import lax
from jax.sharding import PartitionSpec as P


def extended(block, sides, width):
    for axis, dim in sides:
        count = lax.axis_size(axis)
        forward = [(i, i + 1) for i in range(count - 1)]
        backward = [(target, source) for source, target in forward]
        low = lax.ppermute(
            lax.slice_in_dim(block, block.shape[dim] - width, None, axis=dim), axis, forward
        )
        high = lax.ppermute(lax.slice_in_dim(block, 0, width, axis=dim), axis, backward)
        block = jnp.concatenate([low, block, high], axis=dim)
    return block


def from_behind(block, axis, distance):
    devices = range(lax.axis_size(axis))
    route = [(i - distance, i) for i in devices if i - distance in devices]
    return lax.ppermute(block, axis, route)


def on_device(
    node_feats, band_weights, far_weights, far_owner, far_local, w_self, w_neigh, bias, cotangent
):
    rows_dev, col_count = node_feats.shape
    tile_size = band_weights.shape[1] // 3
    blocks = rows_dev // tile_size
    fanout = far_owner.shape[1]
    peer_count = lax.axis_size("rows")
    capacity = max(2, 2 * blocks * fanout // peer_count)
    col_start = lax.axis_index("feat") * col_count
    bias_high = lax.reduce_precision(bias, exponent_bits=8, mantissa_bits=7)
    bias_rest = bias - bias_high
    bias_mid = lax.reduce_precision(bias_rest, exponent_bits=8, mantissa_bits=7)
    bias_parts = jnp.zeros((16, col_count), jnp.bfloat16)
    bias_parts = bias_parts.at[:3].set(
        jnp.stack([bias_high, bias_mid, bias_rest - bias_mid]).astype(jnp.bfloat16)
    )
    packed = jnp.concatenate([node_feats, cotangent, bias_parts], axis=0)
    gathered = lax.all_gather(packed, "feat", axis=1, tiled=True)
    feats_all = gathered[:rows_dev]
    cotangent_all = gathered[rows_dev : 2 * rows_dev]
    bias_rows = gathered[2 * rows_dev : 2 * rows_dev + 3].astype(jnp.float32)
    bias_all = (bias_rows[0] + bias_rows[1]) + bias_rows[2]
    padded = extended(node_feats, (("rows", 0),), tile_size)
    windows = jnp.concatenate(
        [
            padded[offset * tile_size : offset * tile_size + rows_dev].reshape(
                blocks, tile_size, col_count
            )
            for offset in range(3)
        ],
        axis=1,
    )
    band_tiles = band_weights.reshape(blocks, tile_size, 3 * tile_size)
    band_sum = jnp.einsum("bij,bjc->bic", band_tiles, windows, preferred_element_type=jnp.float32)
    owner_ids = far_owner.reshape(-1)
    local_ids = far_local.reshape(-1)
    entries = owner_ids.shape[0]
    same_owner = owner_ids[:, None] == owner_ids[None, :]
    earlier = jnp.arange(entries)[None, :] < jnp.arange(entries)[:, None]
    slot_rank = jnp.sum(jnp.where(same_owner & earlier, 1, 0), axis=1).astype(jnp.int32)
    slot_ids = owner_ids * capacity + slot_rank
    slot_hit = slot_ids[:, None] == jnp.arange(peer_count * capacity, dtype=jnp.int32)[None, :]
    request = (jnp.sum(jnp.where(slot_hit, local_ids[:, None] + 1, 0), axis=0) - 1).reshape(
        peer_count, capacity
    )
    wanted = lax.all_to_all(request, "rows", split_axis=0, concat_axis=0, tiled=True)
    usable = wanted >= 0
    safe_ids = jnp.maximum(wanted, 0)
    own_blocks = node_feats.reshape(blocks, tile_size, col_count)
    outgoing = jnp.where(
        usable[:, :, None, None], own_blocks[safe_ids], jnp.zeros((), jnp.bfloat16)
    )
    incoming = lax.all_to_all(outgoing, "rows", split_axis=0, concat_axis=0, tiled=True)
    fetched = incoming.reshape(peer_count * capacity, tile_size, col_count)[slot_ids].reshape(
        blocks, fanout * tile_size, col_count
    )
    far_tiles = far_weights.reshape(blocks, tile_size, fanout * tile_size)
    far_sum = jnp.einsum("bij,bjc->bic", far_tiles, fetched, preferred_element_type=jnp.float32)
    degree = jnp.sum(band_weights.astype(jnp.float32), axis=1) + jnp.sum(
        far_weights.astype(jnp.float32), axis=1
    )
    neighbours = ((band_sum + far_sum).reshape(rows_dev, col_count) / degree[:, None]).astype(
        jnp.bfloat16
    )
    rows_self = lax.dynamic_slice_in_dim(w_self, col_start, col_count, 0)
    rows_neigh = lax.dynamic_slice_in_dim(w_neigh, col_start, col_count, 0)
    feat_count = lax.axis_size("feat")
    neighbours_each = lax.all_to_all(
        jnp.broadcast_to(neighbours[None], (feat_count, rows_dev, col_count)),
        "feat",
        split_axis=0,
        concat_axis=0,
        tiled=True,
    )
    preact_all = (
        jnp.dot(feats_all, w_self, preferred_element_type=jnp.float32)
        + jnp.einsum(
            "frc,fcd->rd",
            neighbours_each,
            w_neigh.reshape(feat_count, col_count, -1),
            preferred_element_type=jnp.float32,
        )
        + bias_all
    )
    preact = lax.dynamic_slice_in_dim(preact_all, col_start, col_count, 1)
    layer_out = jax.nn.silu(preact).astype(jnp.bfloat16)
    sigmoid_z = jax.nn.sigmoid(preact_all)
    full_grad = (
        cotangent_all.astype(jnp.float32) * sigmoid_z * (1.0 + preact_all * (1.0 - sigmoid_z))
    ).astype(jnp.bfloat16)
    grad_scale = float(rows_dev * peer_count) ** (-0.5)
    part_self = jnp.einsum("rc,rf->cf", node_feats, full_grad, preferred_element_type=jnp.float32)
    part_neigh = jnp.einsum("rc,rf->cf", neighbours, full_grad, preferred_element_type=jnp.float32)
    dense_grad = jnp.einsum("rf,cf->rc", full_grad, rows_self, preferred_element_type=jnp.float32)
    grad_agg = jnp.einsum("rf,cf->rc", full_grad, rows_neigh, preferred_element_type=jnp.float32)
    grad_neighbours = (grad_agg / degree[:, None]).astype(jnp.bfloat16)
    grad_blocks = grad_neighbours.reshape(blocks, tile_size, col_count)
    grad_windows = jnp.einsum(
        "bij,bic->bjc", band_tiles, grad_blocks, preferred_element_type=jnp.float32
    )
    grad_padded = jnp.zeros((rows_dev + 2 * tile_size, col_count), jnp.float32)
    for offset in range(3):
        piece = grad_windows[:, offset * tile_size : (offset + 1) * tile_size, :].reshape(
            rows_dev, col_count
        )
        grad_padded = grad_padded + jnp.pad(
            piece, ((offset * tile_size, (2 - offset) * tile_size), (0, 0))
        )
    top_rim = grad_padded[:tile_size]
    bottom_rim = grad_padded[rows_dev + tile_size :]
    from_below = from_behind(top_rim, "rows", -1)
    from_above = from_behind(bottom_rim, "rows", 1)
    grad_fetched = jnp.einsum(
        "bij,bic->bjc", far_tiles, grad_blocks, preferred_element_type=jnp.float32
    )
    returning = jnp.zeros((peer_count * capacity, tile_size, col_count), jnp.float32)
    returning = returning.at[slot_ids].set(grad_fetched.reshape(entries, tile_size, col_count))
    partials = jnp.stack([part_self, part_neigh]).reshape(peer_count, -1)
    high = lax.reduce_precision(partials, exponent_bits=8, mantissa_bits=7)
    coded = jnp.stack(
        [high.astype(jnp.bfloat16), (partials - high).astype(jnp.bfloat16)], axis=1
    ).reshape(peer_count, capacity, tile_size, -1)
    payload = jnp.concatenate(
        [
            returning.reshape(peer_count, capacity, tile_size, col_count).astype(jnp.bfloat16),
            coded,
        ],
        axis=3,
    )
    arrived = lax.all_to_all(payload, "rows", split_axis=0, concat_axis=0, tiled=True)
    returned = arrived[..., :col_count]
    codes = arrived[..., col_count:].reshape(peer_count, 2, -1).astype(jnp.float32)
    mine = jnp.sum(codes[:, 0] + codes[:, 1], axis=0, keepdims=True)
    whole = lax.all_to_all(
        jnp.broadcast_to(mine, partials.shape), "rows", split_axis=0, concat_axis=0, tiled=True
    )
    sum_self, sum_neigh = whole.reshape(2, col_count, -1)
    grad_self = sum_self * grad_scale
    grad_neigh = sum_neigh * grad_scale
    target_block = jnp.where(usable, wanted, blocks)
    routing = (
        target_block[None] == jnp.arange(blocks, dtype=jnp.int32)[:, None, None]
    ).astype(jnp.bfloat16)
    owed = jnp.einsum("bps,psjc->bjc", routing, returned, preferred_element_type=jnp.float32)
    interior = (
        dense_grad
        + grad_padded[tile_size : tile_size + rows_dev]
        + owed.reshape(rows_dev, col_count)
    )
    interior = interior.at[:tile_size].add(from_above)
    grad_feats = interior.at[rows_dev - tile_size :].add(from_below)
    return (layer_out, grad_feats, grad_self, grad_neigh)


def solution(mesh):
    in_specs = (
        P("rows", "feat"),
        P("rows", None),
        P("rows", None),
        P("rows", None),
        P("rows", None),
        P(),
        P(),
        P("feat"),
        P("rows", "feat"),
    )
    out_specs = (P("rows", "feat"), P("rows", "feat"), P("feat", None), P("feat", None))
    return jax.shard_map(
        on_device, mesh=mesh, in_specs=in_specs, out_specs=out_specs, check_vma=False
    )
```

```python
import jax
import jax.numpy as jnp
from jax import lax
from jax.sharding import PartitionSpec as P


def extended(block, sides, width):
    for axis, dim in sides:
        count = lax.axis_size(axis)
        forward = [(i, i + 1) for i in range(count - 1)]
        backward = [(target, source) for source, target in forward]
        low = lax.ppermute(
            lax.slice_in_dim(block, block.shape[dim] - width, None, axis=dim), axis, forward
        )
        high = lax.ppermute(lax.slice_in_dim(block, 0, width, axis=dim), axis, backward)
        block = jnp.concatenate([low, block, high], axis=dim)
    return block


def from_behind(block, axis, distance):
    devices = range(lax.axis_size(axis))
    route = [(i - distance, i) for i in devices if i - distance in devices]
    return lax.ppermute(block, axis, route)


def on_device(
    node_feats, band_weights, far_weights, far_owner, far_local, w_self, w_neigh, bias, cotangent
):
    rows_dev, col_count = node_feats.shape
    tile_size = band_weights.shape[1] // 3
    blocks = rows_dev // tile_size
    fanout = far_owner.shape[1]
    peer_count = lax.axis_size("rows")
    capacity = max(2, 2 * blocks * fanout // peer_count)
    col_start = lax.axis_index("feat") * col_count
    bias_high = lax.reduce_precision(bias, exponent_bits=8, mantissa_bits=7)
    bias_rest = bias - bias_high
    bias_mid = lax.reduce_precision(bias_rest, exponent_bits=8, mantissa_bits=7)
    bias_parts = jnp.zeros((16, col_count), jnp.bfloat16)
    bias_parts = bias_parts.at[:3].set(
        jnp.stack([bias_high, bias_mid, bias_rest - bias_mid]).astype(jnp.bfloat16)
    )
    packed = jnp.concatenate([node_feats, cotangent, bias_parts], axis=0)
    feat_count = lax.axis_size("feat")
    gathered = lax.all_to_all(
        jnp.broadcast_to(packed[None], (feat_count,) + packed.shape),
        "feat",
        split_axis=0,
        concat_axis=0,
        tiled=True,
    )
    feats_each = gathered[:, :rows_dev]
    cotangent_all = gathered[:, rows_dev : 2 * rows_dev].transpose(1, 0, 2).reshape(rows_dev, -1)
    bias_rows = gathered[:, 2 * rows_dev : 2 * rows_dev + 3].astype(jnp.float32)
    bias_rows = bias_rows.transpose(1, 0, 2).reshape(3, -1)
    bias_all = (bias_rows[0] + bias_rows[1]) + bias_rows[2]
    padded = extended(node_feats, (("rows", 0),), tile_size)
    windows = jnp.concatenate(
        [
            padded[offset * tile_size : offset * tile_size + rows_dev].reshape(
                blocks, tile_size, col_count
            )
            for offset in range(3)
        ],
        axis=1,
    )
    band_tiles = band_weights.reshape(blocks, tile_size, 3 * tile_size)
    band_sum = jnp.einsum("bij,bjc->bic", band_tiles, windows, preferred_element_type=jnp.float32)
    owner_ids = far_owner.reshape(-1)
    local_ids = far_local.reshape(-1)
    entries = owner_ids.shape[0]
    same_owner = owner_ids[:, None] == owner_ids[None, :]
    earlier = jnp.arange(entries)[None, :] < jnp.arange(entries)[:, None]
    slot_rank = jnp.sum(jnp.where(same_owner & earlier, 1, 0), axis=1).astype(jnp.int32)
    slot_ids = owner_ids * capacity + slot_rank
    slot_hit = slot_ids[:, None] == jnp.arange(peer_count * capacity, dtype=jnp.int32)[None, :]
    request = (jnp.sum(jnp.where(slot_hit, local_ids[:, None] + 1, 0), axis=0) - 1).reshape(
        peer_count, capacity
    )
    wanted = lax.all_to_all(request, "rows", split_axis=0, concat_axis=0, tiled=True)
    usable = wanted >= 0
    safe_ids = jnp.maximum(wanted, 0)
    own_blocks = node_feats.reshape(blocks, tile_size, col_count)
    outgoing = jnp.where(
        usable[:, :, None, None], own_blocks[safe_ids], jnp.zeros((), jnp.bfloat16)
    )
    incoming = lax.all_to_all(outgoing, "rows", split_axis=0, concat_axis=0, tiled=True)
    fetched = incoming.reshape(peer_count * capacity, tile_size, col_count)[slot_ids].reshape(
        blocks, fanout * tile_size, col_count
    )
    far_tiles = far_weights.reshape(blocks, tile_size, fanout * tile_size)
    far_sum = jnp.einsum("bij,bjc->bic", far_tiles, fetched, preferred_element_type=jnp.float32)
    degree = jnp.sum(band_weights.astype(jnp.float32), axis=1) + jnp.sum(
        far_weights.astype(jnp.float32), axis=1
    )
    neighbours = ((band_sum + far_sum).reshape(rows_dev, col_count) / degree[:, None]).astype(
        jnp.bfloat16
    )
    rows_self = lax.dynamic_slice_in_dim(w_self, col_start, col_count, 0)
    rows_neigh = lax.dynamic_slice_in_dim(w_neigh, col_start, col_count, 0)
    neighbours_each = lax.all_to_all(
        jnp.broadcast_to(neighbours[None], (feat_count, rows_dev, col_count)),
        "feat",
        split_axis=0,
        concat_axis=0,
        tiled=True,
    )
    preact_all = (
        jnp.einsum(
            "frc,fcd->rd",
            feats_each,
            w_self.reshape(feat_count, col_count, -1),
            preferred_element_type=jnp.float32,
        )
        + jnp.einsum(
            "frc,fcd->rd",
            neighbours_each,
            w_neigh.reshape(feat_count, col_count, -1),
            preferred_element_type=jnp.float32,
        )
        + bias_all
    )
    preact = lax.dynamic_slice_in_dim(preact_all, col_start, col_count, 1)
    layer_out = jax.nn.silu(preact).astype(jnp.bfloat16)
    sigmoid_z = jax.nn.sigmoid(preact_all)
    full_grad = (
        cotangent_all.astype(jnp.float32) * sigmoid_z * (1.0 + preact_all * (1.0 - sigmoid_z))
    ).astype(jnp.bfloat16)
    grad_scale = float(rows_dev * peer_count) ** (-0.5)
    part_self = jnp.einsum("rc,rf->cf", node_feats, full_grad, preferred_element_type=jnp.float32)
    part_neigh = jnp.einsum("rc,rf->cf", neighbours, full_grad, preferred_element_type=jnp.float32)
    dense_grad = jnp.einsum("rf,cf->rc", full_grad, rows_self, preferred_element_type=jnp.float32)
    grad_agg = jnp.einsum("rf,cf->rc", full_grad, rows_neigh, preferred_element_type=jnp.float32)
    grad_neighbours = (grad_agg / degree[:, None]).astype(jnp.bfloat16)
    grad_blocks = grad_neighbours.reshape(blocks, tile_size, col_count)
    grad_windows = jnp.einsum(
        "bij,bic->bjc", band_tiles, grad_blocks, preferred_element_type=jnp.float32
    )
    grad_padded = jnp.zeros((rows_dev + 2 * tile_size, col_count), jnp.float32)
    for offset in range(3):
        piece = grad_windows[:, offset * tile_size : (offset + 1) * tile_size, :].reshape(
            rows_dev, col_count
        )
        grad_padded = grad_padded + jnp.pad(
            piece, ((offset * tile_size, (2 - offset) * tile_size), (0, 0))
        )
    top_rim = grad_padded[:tile_size]
    bottom_rim = grad_padded[rows_dev + tile_size :]
    from_below = from_behind(top_rim, "rows", -1)
    from_above = from_behind(bottom_rim, "rows", 1)
    grad_fetched = jnp.einsum(
        "bij,bic->bjc", far_tiles, grad_blocks, preferred_element_type=jnp.float32
    )
    returning = jnp.zeros((peer_count * capacity, tile_size, col_count), jnp.float32)
    returning = returning.at[slot_ids].set(grad_fetched.reshape(entries, tile_size, col_count))
    partials = jnp.stack([part_self, part_neigh]).reshape(peer_count, -1)
    high = lax.reduce_precision(partials, exponent_bits=8, mantissa_bits=7)
    coded = jnp.stack(
        [high.astype(jnp.bfloat16), (partials - high).astype(jnp.bfloat16)], axis=1
    ).reshape(peer_count, capacity, tile_size, -1)
    payload = jnp.concatenate(
        [
            returning.reshape(peer_count, capacity, tile_size, col_count).astype(jnp.bfloat16),
            coded,
        ],
        axis=3,
    )
    arrived = lax.all_to_all(payload, "rows", split_axis=0, concat_axis=0, tiled=True)
    returned = arrived[..., :col_count]
    codes = arrived[..., col_count:].reshape(peer_count, 2, -1).astype(jnp.float32)
    mine = jnp.sum(codes[:, 0] + codes[:, 1], axis=0, keepdims=True)
    whole = lax.all_to_all(
        jnp.broadcast_to(mine, partials.shape), "rows", split_axis=0, concat_axis=0, tiled=True
    )
    sum_self, sum_neigh = whole.reshape(2, col_count, -1)
    grad_self = sum_self * grad_scale
    grad_neigh = sum_neigh * grad_scale
    target_block = jnp.where(usable, wanted, blocks)
    routing = (
        target_block[None] == jnp.arange(blocks, dtype=jnp.int32)[:, None, None]
    ).astype(jnp.bfloat16)
    owed = jnp.einsum("bps,psjc->bjc", routing, returned, preferred_element_type=jnp.float32)
    interior = (
        dense_grad
        + grad_padded[tile_size : tile_size + rows_dev]
        + owed.reshape(rows_dev, col_count)
    )
    interior = interior.at[:tile_size].add(from_above)
    grad_feats = interior.at[rows_dev - tile_size :].add(from_below)
    return (layer_out, grad_feats, grad_self, grad_neigh)


def solution(mesh):
    in_specs = (
        P("rows", "feat"),
        P("rows", None),
        P("rows", None),
        P("rows", None),
        P("rows", None),
        P(),
        P(),
        P("feat"),
        P("rows", "feat"),
    )
    out_specs = (P("rows", "feat"), P("rows", "feat"), P("feat", None), P("feat", None))
    return jax.shard_map(
        on_device, mesh=mesh, in_specs=in_specs, out_specs=out_specs, check_vma=False
    )
```

```python
import jax
import jax.numpy as jnp
from jax import lax
from jax.sharding import PartitionSpec as P


def extended(block, sides, width):
    for axis, dim in sides:
        count = lax.axis_size(axis)
        forward = [(i, i + 1) for i in range(count - 1)]
        backward = [(target, source) for source, target in forward]
        low = lax.ppermute(
            lax.slice_in_dim(block, block.shape[dim] - width, None, axis=dim), axis, forward
        )
        high = lax.ppermute(lax.slice_in_dim(block, 0, width, axis=dim), axis, backward)
        block = jnp.concatenate([low, block, high], axis=dim)
    return block


def from_behind(block, axis, distance):
    devices = range(lax.axis_size(axis))
    route = [(i - distance, i) for i in devices if i - distance in devices]
    return lax.ppermute(block, axis, route)


def on_device(
    node_feats, band_weights, far_weights, far_owner, far_local, w_self, w_neigh, bias, cotangent
):
    rows_dev, col_count = node_feats.shape
    tile_size = band_weights.shape[1] // 3
    blocks = rows_dev // tile_size
    fanout = far_owner.shape[1]
    peer_count = lax.axis_size("rows")
    capacity = max(2, 2 * blocks * fanout // peer_count)
    col_start = lax.axis_index("feat") * col_count
    bias_high = lax.reduce_precision(bias, exponent_bits=8, mantissa_bits=7)
    bias_rest = bias - bias_high
    bias_mid = lax.reduce_precision(bias_rest, exponent_bits=8, mantissa_bits=7)
    bias_parts = jnp.zeros((16, col_count), jnp.bfloat16)
    bias_parts = bias_parts.at[:3].set(
        jnp.stack([bias_high, bias_mid, bias_rest - bias_mid]).astype(jnp.bfloat16)
    )
    packed = jnp.concatenate([node_feats, cotangent, bias_parts], axis=0)
    feat_count = lax.axis_size("feat")
    padded = extended(node_feats, (("rows", 0),), tile_size)
    windows = jnp.concatenate(
        [
            padded[offset * tile_size : offset * tile_size + rows_dev].reshape(
                blocks, tile_size, col_count
            )
            for offset in range(3)
        ],
        axis=1,
    )
    band_tiles = band_weights.reshape(blocks, tile_size, 3 * tile_size)
    band_sum = jnp.einsum("bij,bjc->bic", band_tiles, windows, preferred_element_type=jnp.float32)
    owner_ids = far_owner.reshape(-1)
    local_ids = far_local.reshape(-1)
    entries = owner_ids.shape[0]
    same_owner = owner_ids[:, None] == owner_ids[None, :]
    earlier = jnp.arange(entries)[None, :] < jnp.arange(entries)[:, None]
    slot_rank = jnp.sum(jnp.where(same_owner & earlier, 1, 0), axis=1).astype(jnp.int32)
    slot_ids = owner_ids * capacity + slot_rank
    slot_hit = slot_ids[:, None] == jnp.arange(peer_count * capacity, dtype=jnp.int32)[None, :]
    request = (jnp.sum(jnp.where(slot_hit, local_ids[:, None] + 1, 0), axis=0) - 1).reshape(
        peer_count, capacity
    )
    wanted = lax.all_to_all(request, "rows", split_axis=0, concat_axis=0, tiled=True)
    usable = wanted >= 0
    safe_ids = jnp.maximum(wanted, 0)
    own_blocks = node_feats.reshape(blocks, tile_size, col_count)
    outgoing = jnp.where(
        usable[:, :, None, None], own_blocks[safe_ids], jnp.zeros((), jnp.bfloat16)
    )
    incoming = lax.all_to_all(outgoing, "rows", split_axis=0, concat_axis=0, tiled=True)
    fetched = incoming.reshape(peer_count * capacity, tile_size, col_count)[slot_ids].reshape(
        blocks, fanout * tile_size, col_count
    )
    far_tiles = far_weights.reshape(blocks, tile_size, fanout * tile_size)
    far_sum = jnp.einsum("bij,bjc->bic", far_tiles, fetched, preferred_element_type=jnp.float32)
    degree = jnp.sum(band_weights.astype(jnp.float32), axis=1) + jnp.sum(
        far_weights.astype(jnp.float32), axis=1
    )
    neighbours = ((band_sum + far_sum).reshape(rows_dev, col_count) / degree[:, None]).astype(
        jnp.bfloat16
    )
    rows_self = lax.dynamic_slice_in_dim(w_self, col_start, col_count, 0)
    rows_neigh = lax.dynamic_slice_in_dim(w_neigh, col_start, col_count, 0)
    joined = jnp.concatenate([neighbours, packed], axis=0)
    gathered = lax.all_to_all(
        jnp.broadcast_to(joined[None], (feat_count,) + joined.shape),
        "feat",
        split_axis=0,
        concat_axis=0,
        tiled=True,
    )
    neighbours_each = gathered[:, :rows_dev]
    feats_each = gathered[:, rows_dev : 2 * rows_dev]
    cotangent_all = (
        gathered[:, 2 * rows_dev : 3 * rows_dev].transpose(1, 0, 2).reshape(rows_dev, -1)
    )
    bias_rows = gathered[:, 3 * rows_dev : 3 * rows_dev + 3].astype(jnp.float32)
    bias_rows = bias_rows.transpose(1, 0, 2).reshape(3, -1)
    bias_all = (bias_rows[0] + bias_rows[1]) + bias_rows[2]
    preact_all = (
        jnp.einsum(
            "frc,fcd->rd",
            feats_each,
            w_self.reshape(feat_count, col_count, -1),
            preferred_element_type=jnp.float32,
        )
        + jnp.einsum(
            "frc,fcd->rd",
            neighbours_each,
            w_neigh.reshape(feat_count, col_count, -1),
            preferred_element_type=jnp.float32,
        )
        + bias_all
    )
    preact = lax.dynamic_slice_in_dim(preact_all, col_start, col_count, 1)
    layer_out = jax.nn.silu(preact).astype(jnp.bfloat16)
    sigmoid_z = jax.nn.sigmoid(preact_all)
    full_grad = (
        cotangent_all.astype(jnp.float32) * sigmoid_z * (1.0 + preact_all * (1.0 - sigmoid_z))
    ).astype(jnp.bfloat16)
    grad_scale = float(rows_dev * peer_count) ** (-0.5)
    part_self = jnp.einsum("rc,rf->cf", node_feats, full_grad, preferred_element_type=jnp.float32)
    part_neigh = jnp.einsum("rc,rf->cf", neighbours, full_grad, preferred_element_type=jnp.float32)
    dense_grad = jnp.einsum("rf,cf->rc", full_grad, rows_self, preferred_element_type=jnp.float32)
    grad_agg = jnp.einsum("rf,cf->rc", full_grad, rows_neigh, preferred_element_type=jnp.float32)
    grad_neighbours = (grad_agg / degree[:, None]).astype(jnp.bfloat16)
    grad_blocks = grad_neighbours.reshape(blocks, tile_size, col_count)
    grad_windows = jnp.einsum(
        "bij,bic->bjc", band_tiles, grad_blocks, preferred_element_type=jnp.float32
    )
    grad_padded = jnp.zeros((rows_dev + 2 * tile_size, col_count), jnp.float32)
    for offset in range(3):
        piece = grad_windows[:, offset * tile_size : (offset + 1) * tile_size, :].reshape(
            rows_dev, col_count
        )
        grad_padded = grad_padded + jnp.pad(
            piece, ((offset * tile_size, (2 - offset) * tile_size), (0, 0))
        )
    top_rim = grad_padded[:tile_size]
    bottom_rim = grad_padded[rows_dev + tile_size :]
    from_below = from_behind(top_rim, "rows", -1)
    from_above = from_behind(bottom_rim, "rows", 1)
    grad_fetched = jnp.einsum(
        "bij,bic->bjc", far_tiles, grad_blocks, preferred_element_type=jnp.float32
    )
    returning = jnp.zeros((peer_count * capacity, tile_size, col_count), jnp.float32)
    returning = returning.at[slot_ids].set(grad_fetched.reshape(entries, tile_size, col_count))
    partials = jnp.stack([part_self, part_neigh]).reshape(peer_count, -1)
    high = lax.reduce_precision(partials, exponent_bits=8, mantissa_bits=7)
    coded = jnp.stack(
        [high.astype(jnp.bfloat16), (partials - high).astype(jnp.bfloat16)], axis=1
    ).reshape(peer_count, capacity, tile_size, -1)
    payload = jnp.concatenate(
        [
            returning.reshape(peer_count, capacity, tile_size, col_count).astype(jnp.bfloat16),
            coded,
        ],
        axis=3,
    )
    arrived = lax.all_to_all(payload, "rows", split_axis=0, concat_axis=0, tiled=True)
    returned = arrived[..., :col_count]
    codes = arrived[..., col_count:].reshape(peer_count, 2, -1).astype(jnp.float32)
    mine = jnp.sum(codes[:, 0] + codes[:, 1], axis=0, keepdims=True)
    whole = lax.all_to_all(
        jnp.broadcast_to(mine, partials.shape), "rows", split_axis=0, concat_axis=0, tiled=True
    )
    sum_self, sum_neigh = whole.reshape(2, col_count, -1)
    grad_self = sum_self * grad_scale
    grad_neigh = sum_neigh * grad_scale
    target_block = jnp.where(usable, wanted, blocks)
    routing = (
        target_block[None] == jnp.arange(blocks, dtype=jnp.int32)[:, None, None]
    ).astype(jnp.bfloat16)
    owed = jnp.einsum("bps,psjc->bjc", routing, returned, preferred_element_type=jnp.float32)
    interior = (
        dense_grad
        + grad_padded[tile_size : tile_size + rows_dev]
        + owed.reshape(rows_dev, col_count)
    )
    interior = interior.at[:tile_size].add(from_above)
    grad_feats = interior.at[rows_dev - tile_size :].add(from_below)
    return (layer_out, grad_feats, grad_self, grad_neigh)


def solution(mesh):
    in_specs = (
        P("rows", "feat"),
        P("rows", None),
        P("rows", None),
        P("rows", None),
        P("rows", None),
        P(),
        P(),
        P("feat"),
        P("rows", "feat"),
    )
    out_specs = (P("rows", "feat"), P("rows", "feat"), P("feat", None), P("feat", None))
    return jax.shard_map(
        on_device, mesh=mesh, in_specs=in_specs, out_specs=out_specs, check_vma=False
    )
```

```python
import jax
import jax.numpy as jnp
from jax import lax
from jax.sharding import PartitionSpec as P


def extended(block, sides, width):
    for axis, dim in sides:
        count = lax.axis_size(axis)
        forward = [(i, i + 1) for i in range(count - 1)]
        backward = [(target, source) for source, target in forward]
        low = lax.ppermute(
            lax.slice_in_dim(block, block.shape[dim] - width, None, axis=dim), axis, forward
        )
        high = lax.ppermute(lax.slice_in_dim(block, 0, width, axis=dim), axis, backward)
        block = jnp.concatenate([low, block, high], axis=dim)
    return block


def from_behind(block, axis, distance):
    devices = range(lax.axis_size(axis))
    route = [(i - distance, i) for i in devices if i - distance in devices]
    return lax.ppermute(block, axis, route)


def on_device(
    node_feats, band_weights, far_weights, far_owner, far_local, w_self, w_neigh, bias, cotangent
):
    rows_dev, col_count = node_feats.shape
    tile_size = band_weights.shape[1] // 3
    blocks = rows_dev // tile_size
    fanout = far_owner.shape[1]
    peer_count = lax.axis_size("rows")
    capacity = max(2, 2 * blocks * fanout // peer_count)
    col_start = lax.axis_index("feat") * col_count
    bias_high = lax.reduce_precision(bias, exponent_bits=8, mantissa_bits=7)
    bias_rest = bias - bias_high
    bias_mid = lax.reduce_precision(bias_rest, exponent_bits=8, mantissa_bits=7)
    bias_parts = jnp.zeros((16, col_count), jnp.bfloat16)
    bias_parts = bias_parts.at[:3].set(
        jnp.stack([bias_high, bias_mid, bias_rest - bias_mid]).astype(jnp.bfloat16)
    )
    packed = jnp.concatenate([node_feats, cotangent, bias_parts], axis=0)
    feat_count = lax.axis_size("feat")
    padded = extended(node_feats, (("rows", 0),), tile_size)
    windows = jnp.concatenate(
        [
            padded[offset * tile_size : offset * tile_size + rows_dev].reshape(
                blocks, tile_size, col_count
            )
            for offset in range(3)
        ],
        axis=1,
    )
    band_tiles = band_weights.reshape(blocks, tile_size, 3 * tile_size)
    band_sum = jnp.einsum("bij,bjc->bic", band_tiles, windows, preferred_element_type=jnp.float32)
    owner_ids = far_owner.reshape(-1)
    local_ids = far_local.reshape(-1)
    entries = owner_ids.shape[0]
    same_owner = owner_ids[:, None] == owner_ids[None, :]
    earlier = jnp.arange(entries)[None, :] < jnp.arange(entries)[:, None]
    slot_rank = jnp.sum(jnp.where(same_owner & earlier, 1, 0), axis=1).astype(jnp.int32)
    slot_ids = owner_ids * capacity + slot_rank
    slot_hit = slot_ids[:, None] == jnp.arange(peer_count * capacity, dtype=jnp.int32)[None, :]
    request = (jnp.sum(jnp.where(slot_hit, local_ids[:, None] + 1, 0), axis=0) - 1).reshape(
        peer_count, capacity
    )
    wanted = lax.all_to_all(request, "rows", split_axis=0, concat_axis=0, tiled=True)
    usable = wanted >= 0
    safe_ids = jnp.maximum(wanted, 0)
    own_blocks = node_feats.reshape(blocks, tile_size, col_count)
    outgoing = jnp.where(
        usable[:, :, None, None], own_blocks[safe_ids], jnp.zeros((), jnp.bfloat16)
    )
    incoming = lax.all_to_all(outgoing, "rows", split_axis=0, concat_axis=0, tiled=True)
    fetched = incoming.reshape(peer_count * capacity, tile_size, col_count)[slot_ids].reshape(
        blocks, fanout * tile_size, col_count
    )
    far_tiles = far_weights.reshape(blocks, tile_size, fanout * tile_size)
    far_sum = jnp.einsum("bij,bjc->bic", far_tiles, fetched, preferred_element_type=jnp.float32)
    degree = jnp.sum(band_weights.astype(jnp.float32), axis=1) + jnp.sum(
        far_weights.astype(jnp.float32), axis=1
    )
    neighbours = ((band_sum + far_sum).reshape(rows_dev, col_count) / degree[:, None]).astype(
        jnp.bfloat16
    )
    rows_self = lax.dynamic_slice_in_dim(w_self, col_start, col_count, 0)
    rows_neigh = lax.dynamic_slice_in_dim(w_neigh, col_start, col_count, 0)
    joined = jnp.concatenate([neighbours, packed], axis=0)
    gathered = lax.all_to_all(
        jnp.broadcast_to(joined[None], (feat_count,) + joined.shape),
        "feat",
        split_axis=0,
        concat_axis=0,
        tiled=True,
    )
    neighbours_each = gathered[:, :rows_dev]
    feats_each = gathered[:, rows_dev : 2 * rows_dev]
    cotangent_each = gathered[:, 2 * rows_dev : 3 * rows_dev]
    bias_rows = gathered[:, 3 * rows_dev : 3 * rows_dev + 3].astype(jnp.float32)
    bias_each = (bias_rows[:, 0:1] + bias_rows[:, 1:2]) + bias_rows[:, 2:3]
    blocked = (feat_count, col_count, feat_count, col_count)
    preact_each = (
        jnp.einsum(
            "frc,fcgd->grd",
            feats_each,
            w_self.reshape(blocked),
            preferred_element_type=jnp.float32,
        )
        + jnp.einsum(
            "frc,fcgd->grd",
            neighbours_each,
            w_neigh.reshape(blocked),
            preferred_element_type=jnp.float32,
        )
        + bias_each
    )
    preact = lax.dynamic_index_in_dim(preact_each, lax.axis_index("feat"), 0, keepdims=False)
    layer_out = jax.nn.silu(preact).astype(jnp.bfloat16)
    sigmoid_z = jax.nn.sigmoid(preact_each)
    grad_each = (
        cotangent_each.astype(jnp.float32) * sigmoid_z * (1.0 + preact_each * (1.0 - sigmoid_z))
    ).astype(jnp.bfloat16)
    grad_scale = float(rows_dev * peer_count) ** (-0.5)
    part_self = jnp.einsum(
        "rc,grd->cgd", node_feats, grad_each, preferred_element_type=jnp.float32
    ).reshape(col_count, -1)
    part_neigh = jnp.einsum(
        "rc,grd->cgd", neighbours, grad_each, preferred_element_type=jnp.float32
    ).reshape(col_count, -1)
    dense_grad = jnp.einsum(
        "grd,cgd->rc",
        grad_each,
        rows_self.reshape(col_count, feat_count, col_count),
        preferred_element_type=jnp.float32,
    )
    grad_agg = jnp.einsum(
        "grd,cgd->rc",
        grad_each,
        rows_neigh.reshape(col_count, feat_count, col_count),
        preferred_element_type=jnp.float32,
    )
    grad_neighbours = (grad_agg / degree[:, None]).astype(jnp.bfloat16)
    grad_blocks = grad_neighbours.reshape(blocks, tile_size, col_count)
    grad_windows = jnp.einsum(
        "bij,bic->bjc", band_tiles, grad_blocks, preferred_element_type=jnp.float32
    )
    grad_padded = jnp.zeros((rows_dev + 2 * tile_size, col_count), jnp.float32)
    for offset in range(3):
        piece = grad_windows[:, offset * tile_size : (offset + 1) * tile_size, :].reshape(
            rows_dev, col_count
        )
        grad_padded = grad_padded + jnp.pad(
            piece, ((offset * tile_size, (2 - offset) * tile_size), (0, 0))
        )
    top_rim = grad_padded[:tile_size]
    bottom_rim = grad_padded[rows_dev + tile_size :]
    from_below = from_behind(top_rim, "rows", -1)
    from_above = from_behind(bottom_rim, "rows", 1)
    grad_fetched = jnp.einsum(
        "bij,bic->bjc", far_tiles, grad_blocks, preferred_element_type=jnp.float32
    )
    returning = jnp.zeros((peer_count * capacity, tile_size, col_count), jnp.float32)
    returning = returning.at[slot_ids].set(grad_fetched.reshape(entries, tile_size, col_count))
    partials = jnp.stack([part_self, part_neigh]).reshape(peer_count, -1)
    high = lax.reduce_precision(partials, exponent_bits=8, mantissa_bits=7)
    coded = jnp.stack(
        [high.astype(jnp.bfloat16), (partials - high).astype(jnp.bfloat16)], axis=1
    ).reshape(peer_count, capacity, tile_size, -1)
    payload = jnp.concatenate(
        [
            returning.reshape(peer_count, capacity, tile_size, col_count).astype(jnp.bfloat16),
            coded,
        ],
        axis=3,
    )
    arrived = lax.all_to_all(payload, "rows", split_axis=0, concat_axis=0, tiled=True)
    returned = arrived[..., :col_count]
    codes = arrived[..., col_count:].reshape(peer_count, 2, -1).astype(jnp.float32)
    mine = jnp.sum(codes[:, 0] + codes[:, 1], axis=0, keepdims=True)
    whole = lax.all_to_all(
        jnp.broadcast_to(mine, partials.shape), "rows", split_axis=0, concat_axis=0, tiled=True
    )
    sum_self, sum_neigh = whole.reshape(2, col_count, -1)
    grad_self = sum_self * grad_scale
    grad_neigh = sum_neigh * grad_scale
    target_block = jnp.where(usable, wanted, blocks)
    routing = (
        target_block[None] == jnp.arange(blocks, dtype=jnp.int32)[:, None, None]
    ).astype(jnp.bfloat16)
    owed = jnp.einsum("bps,psjc->bjc", routing, returned, preferred_element_type=jnp.float32)
    interior = (
        dense_grad
        + grad_padded[tile_size : tile_size + rows_dev]
        + owed.reshape(rows_dev, col_count)
    )
    interior = interior.at[:tile_size].add(from_above)
    grad_feats = interior.at[rows_dev - tile_size :].add(from_below)
    return (layer_out, grad_feats, grad_self, grad_neigh)


def solution(mesh):
    in_specs = (
        P("rows", "feat"),
        P("rows", None),
        P("rows", None),
        P("rows", None),
        P("rows", None),
        P(),
        P(),
        P("feat"),
        P("rows", "feat"),
    )
    out_specs = (P("rows", "feat"), P("rows", "feat"), P("feat", None), P("feat", None))
    return jax.shard_map(
        on_device, mesh=mesh, in_specs=in_specs, out_specs=out_specs, check_vma=False
    )
```

```python
import jax
import jax.numpy as jnp
from jax import lax
from jax.sharding import PartitionSpec as P


def extended(block, sides, width):
    for axis, dim in sides:
        count = lax.axis_size(axis)
        forward = [(i, i + 1) for i in range(count - 1)]
        backward = [(target, source) for source, target in forward]
        low = lax.ppermute(
            lax.slice_in_dim(block, block.shape[dim] - width, None, axis=dim), axis, forward
        )
        high = lax.ppermute(lax.slice_in_dim(block, 0, width, axis=dim), axis, backward)
        block = jnp.concatenate([low, block, high], axis=dim)
    return block


def from_behind(block, axis, distance):
    devices = range(lax.axis_size(axis))
    route = [(i - distance, i) for i in devices if i - distance in devices]
    return lax.ppermute(block, axis, route)


def on_device(
    node_feats, band_weights, far_weights, far_owner, far_local, w_self, w_neigh, bias, cotangent
):
    rows_dev, col_count = node_feats.shape
    tile_size = band_weights.shape[1] // 3
    blocks = rows_dev // tile_size
    fanout = far_owner.shape[1]
    peer_count = lax.axis_size("rows")
    capacity = max(2, 2 * blocks * fanout // peer_count)
    col_start = lax.axis_index("feat") * col_count
    bias_high = lax.reduce_precision(bias, exponent_bits=8, mantissa_bits=7)
    bias_rest = bias - bias_high
    bias_mid = lax.reduce_precision(bias_rest, exponent_bits=8, mantissa_bits=7)
    bias_parts = jnp.zeros((16, col_count), jnp.bfloat16)
    bias_parts = bias_parts.at[:3].set(
        jnp.stack([bias_high, bias_mid, bias_rest - bias_mid]).astype(jnp.bfloat16)
    )
    packed = jnp.concatenate([node_feats, cotangent, bias_parts], axis=0)
    feat_count = lax.axis_size("feat")
    shifted_packed = [
        lax.ppermute(packed, "feat", [(i, (i + k) % feat_count) for i in range(feat_count)])
        for k in range(1, feat_count)
    ]
    padded = extended(node_feats, (("rows", 0),), tile_size)
    windows = jnp.concatenate(
        [
            padded[offset * tile_size : offset * tile_size + rows_dev].reshape(
                blocks, tile_size, col_count
            )
            for offset in range(3)
        ],
        axis=1,
    )
    band_tiles = band_weights.reshape(blocks, tile_size, 3 * tile_size)
    band_sum = jnp.einsum("bij,bjc->bic", band_tiles, windows, preferred_element_type=jnp.float32)
    owner_ids = far_owner.reshape(-1)
    local_ids = far_local.reshape(-1)
    entries = owner_ids.shape[0]
    same_owner = owner_ids[:, None] == owner_ids[None, :]
    earlier = jnp.arange(entries)[None, :] < jnp.arange(entries)[:, None]
    slot_rank = jnp.sum(jnp.where(same_owner & earlier, 1, 0), axis=1).astype(jnp.int32)
    slot_ids = owner_ids * capacity + slot_rank
    slot_hit = slot_ids[:, None] == jnp.arange(peer_count * capacity, dtype=jnp.int32)[None, :]
    request = (jnp.sum(jnp.where(slot_hit, local_ids[:, None] + 1, 0), axis=0) - 1).reshape(
        peer_count, capacity
    )
    wanted = lax.all_to_all(request, "rows", split_axis=0, concat_axis=0, tiled=True)
    usable = wanted >= 0
    safe_ids = jnp.maximum(wanted, 0)
    own_blocks = node_feats.reshape(blocks, tile_size, col_count)
    outgoing = jnp.where(
        usable[:, :, None, None], own_blocks[safe_ids], jnp.zeros((), jnp.bfloat16)
    )
    incoming = lax.all_to_all(outgoing, "rows", split_axis=0, concat_axis=0, tiled=True)
    fetched = incoming.reshape(peer_count * capacity, tile_size, col_count)[slot_ids].reshape(
        blocks, fanout * tile_size, col_count
    )
    far_tiles = far_weights.reshape(blocks, tile_size, fanout * tile_size)
    far_sum = jnp.einsum("bij,bjc->bic", far_tiles, fetched, preferred_element_type=jnp.float32)
    degree = jnp.sum(band_weights.astype(jnp.float32), axis=1) + jnp.sum(
        far_weights.astype(jnp.float32), axis=1
    )
    neighbours = ((band_sum + far_sum).reshape(rows_dev, col_count) / degree[:, None]).astype(
        jnp.bfloat16
    )
    rows_self = lax.dynamic_slice_in_dim(w_self, col_start, col_count, 0)
    rows_neigh = lax.dynamic_slice_in_dim(w_neigh, col_start, col_count, 0)
    neighbours_each = lax.all_to_all(
        jnp.broadcast_to(neighbours[None], (feat_count, rows_dev, col_count)),
        "feat",
        split_axis=0,
        concat_axis=0,
        tiled=True,
    )
    by_shift = jnp.stack([packed] + shifted_packed)
    by_source = by_shift[(lax.axis_index("feat") - jnp.arange(feat_count)) % feat_count]
    feats_each = by_source[:, :rows_dev]
    cotangent_each = by_source[:, rows_dev : 2 * rows_dev]
    bias_rows = by_source[:, 2 * rows_dev : 2 * rows_dev + 3].astype(jnp.float32)
    bias_each = (bias_rows[:, 0:1] + bias_rows[:, 1:2]) + bias_rows[:, 2:3]
    blocked = (feat_count, col_count, feat_count, col_count)
    preact_each = (
        jnp.einsum(
            "frc,fcgd->grd",
            feats_each,
            w_self.reshape(blocked),
            preferred_element_type=jnp.float32,
        )
        + jnp.einsum(
            "frc,fcgd->grd",
            neighbours_each,
            w_neigh.reshape(blocked),
            preferred_element_type=jnp.float32,
        )
        + bias_each
    )
    preact = lax.dynamic_index_in_dim(preact_each, lax.axis_index("feat"), 0, keepdims=False)
    layer_out = jax.nn.silu(preact).astype(jnp.bfloat16)
    sigmoid_z = jax.nn.sigmoid(preact_each)
    grad_each = (
        cotangent_each.astype(jnp.float32) * sigmoid_z * (1.0 + preact_each * (1.0 - sigmoid_z))
    ).astype(jnp.bfloat16)
    grad_scale = float(rows_dev * peer_count) ** (-0.5)
    part_self = jnp.einsum(
        "rc,grd->cgd", node_feats, grad_each, preferred_element_type=jnp.float32
    ).reshape(col_count, -1)
    part_neigh = jnp.einsum(
        "rc,grd->cgd", neighbours, grad_each, preferred_element_type=jnp.float32
    ).reshape(col_count, -1)
    dense_grad = jnp.einsum(
        "grd,cgd->rc",
        grad_each,
        rows_self.reshape(col_count, feat_count, col_count),
        preferred_element_type=jnp.float32,
    )
    grad_agg = jnp.einsum(
        "grd,cgd->rc",
        grad_each,
        rows_neigh.reshape(col_count, feat_count, col_count),
        preferred_element_type=jnp.float32,
    )
    grad_neighbours = (grad_agg / degree[:, None]).astype(jnp.bfloat16)
    grad_blocks = grad_neighbours.reshape(blocks, tile_size, col_count)
    grad_windows = jnp.einsum(
        "bij,bic->bjc", band_tiles, grad_blocks, preferred_element_type=jnp.float32
    )
    grad_padded = jnp.zeros((rows_dev + 2 * tile_size, col_count), jnp.float32)
    for offset in range(3):
        piece = grad_windows[:, offset * tile_size : (offset + 1) * tile_size, :].reshape(
            rows_dev, col_count
        )
        grad_padded = grad_padded + jnp.pad(
            piece, ((offset * tile_size, (2 - offset) * tile_size), (0, 0))
        )
    top_rim = grad_padded[:tile_size]
    bottom_rim = grad_padded[rows_dev + tile_size :]
    from_below = from_behind(top_rim, "rows", -1)
    from_above = from_behind(bottom_rim, "rows", 1)
    grad_fetched = jnp.einsum(
        "bij,bic->bjc", far_tiles, grad_blocks, preferred_element_type=jnp.float32
    )
    returning = jnp.zeros((peer_count * capacity, tile_size, col_count), jnp.float32)
    returning = returning.at[slot_ids].set(grad_fetched.reshape(entries, tile_size, col_count))
    partials = jnp.stack([part_self, part_neigh]).reshape(peer_count, -1)
    high = lax.reduce_precision(partials, exponent_bits=8, mantissa_bits=7)
    coded = jnp.stack(
        [high.astype(jnp.bfloat16), (partials - high).astype(jnp.bfloat16)], axis=1
    ).reshape(peer_count, capacity, tile_size, -1)
    payload = jnp.concatenate(
        [
            returning.reshape(peer_count, capacity, tile_size, col_count).astype(jnp.bfloat16),
            coded,
        ],
        axis=3,
    )
    arrived = lax.all_to_all(payload, "rows", split_axis=0, concat_axis=0, tiled=True)
    returned = arrived[..., :col_count]
    codes = arrived[..., col_count:].reshape(peer_count, 2, -1).astype(jnp.float32)
    mine = jnp.sum(codes[:, 0] + codes[:, 1], axis=0, keepdims=True)
    whole = lax.all_to_all(
        jnp.broadcast_to(mine, partials.shape), "rows", split_axis=0, concat_axis=0, tiled=True
    )
    sum_self, sum_neigh = whole.reshape(2, col_count, -1)
    grad_self = sum_self * grad_scale
    grad_neigh = sum_neigh * grad_scale
    target_block = jnp.where(usable, wanted, blocks)
    routing = (
        target_block[None] == jnp.arange(blocks, dtype=jnp.int32)[:, None, None]
    ).astype(jnp.bfloat16)
    owed = jnp.einsum("bps,psjc->bjc", routing, returned, preferred_element_type=jnp.float32)
    interior = (
        dense_grad
        + grad_padded[tile_size : tile_size + rows_dev]
        + owed.reshape(rows_dev, col_count)
    )
    interior = interior.at[:tile_size].add(from_above)
    grad_feats = interior.at[rows_dev - tile_size :].add(from_below)
    return (layer_out, grad_feats, grad_self, grad_neigh)


def solution(mesh):
    in_specs = (
        P("rows", "feat"),
        P("rows", None),
        P("rows", None),
        P("rows", None),
        P("rows", None),
        P(),
        P(),
        P("feat"),
        P("rows", "feat"),
    )
    out_specs = (P("rows", "feat"), P("rows", "feat"), P("feat", None), P("feat", None))
    return jax.shard_map(
        on_device, mesh=mesh, in_specs=in_specs, out_specs=out_specs, check_vma=False
    )
```

```python
import jax
import jax.numpy as jnp
from jax import lax
from jax.sharding import PartitionSpec as P


def extended(block, sides, width):
    for axis, dim in sides:
        count = lax.axis_size(axis)
        forward = [(i, i + 1) for i in range(count - 1)]
        backward = [(target, source) for source, target in forward]
        low = lax.ppermute(
            lax.slice_in_dim(block, block.shape[dim] - width, None, axis=dim), axis, forward
        )
        high = lax.ppermute(lax.slice_in_dim(block, 0, width, axis=dim), axis, backward)
        block = jnp.concatenate([low, block, high], axis=dim)
    return block


def from_behind(block, axis, distance):
    devices = range(lax.axis_size(axis))
    route = [(i - distance, i) for i in devices if i - distance in devices]
    return lax.ppermute(block, axis, route)


def on_device(
    node_feats, band_weights, far_weights, far_owner, far_local, w_self, w_neigh, bias, cotangent
):
    rows_dev, col_count = node_feats.shape
    tile_size = band_weights.shape[1] // 3
    blocks = rows_dev // tile_size
    fanout = far_owner.shape[1]
    peer_count = lax.axis_size("rows")
    capacity = max(2, 2 * blocks * fanout // peer_count)
    col_start = lax.axis_index("feat") * col_count
    bias_high = lax.reduce_precision(bias, exponent_bits=8, mantissa_bits=7)
    bias_rest = bias - bias_high
    bias_mid = lax.reduce_precision(bias_rest, exponent_bits=8, mantissa_bits=7)
    bias_parts = jnp.zeros((16, col_count), jnp.bfloat16)
    bias_parts = bias_parts.at[:3].set(
        jnp.stack([bias_high, bias_mid, bias_rest - bias_mid]).astype(jnp.bfloat16)
    )
    packed = jnp.concatenate([node_feats, cotangent, bias_parts], axis=0)
    feat_count = lax.axis_size("feat")
    padded = extended(node_feats, (("rows", 0),), tile_size)
    windows = jnp.concatenate(
        [
            padded[offset * tile_size : offset * tile_size + rows_dev].reshape(
                blocks, tile_size, col_count
            )
            for offset in range(3)
        ],
        axis=1,
    )
    band_tiles = band_weights.reshape(blocks, tile_size, 3 * tile_size)
    band_sum = jnp.einsum("bij,bjc->bic", band_tiles, windows, preferred_element_type=jnp.float32)
    owner_ids = far_owner.reshape(-1)
    local_ids = far_local.reshape(-1)
    entries = owner_ids.shape[0]
    same_owner = owner_ids[:, None] == owner_ids[None, :]
    earlier = jnp.arange(entries)[None, :] < jnp.arange(entries)[:, None]
    slot_rank = jnp.sum(jnp.where(same_owner & earlier, 1, 0), axis=1).astype(jnp.int32)
    slot_ids = owner_ids * capacity + slot_rank
    slot_hit = slot_ids[:, None] == jnp.arange(peer_count * capacity, dtype=jnp.int32)[None, :]
    request = (jnp.sum(jnp.where(slot_hit, local_ids[:, None] + 1, 0), axis=0) - 1).reshape(
        peer_count, capacity
    )
    wanted = lax.all_to_all(request, "rows", split_axis=0, concat_axis=0, tiled=True)
    usable = wanted >= 0
    safe_ids = jnp.maximum(wanted, 0)
    own_blocks = node_feats.reshape(blocks, tile_size, col_count)
    outgoing = jnp.where(
        usable[:, :, None, None], own_blocks[safe_ids], jnp.zeros((), jnp.bfloat16)
    )
    incoming = lax.all_to_all(outgoing, "rows", split_axis=0, concat_axis=0, tiled=True)
    fetched = incoming.reshape(peer_count * capacity, tile_size, col_count)[slot_ids].reshape(
        blocks, fanout * tile_size, col_count
    )
    far_tiles = far_weights.reshape(blocks, tile_size, fanout * tile_size)
    far_sum = jnp.einsum("bij,bjc->bic", far_tiles, fetched, preferred_element_type=jnp.float32)
    degree = jnp.sum(band_weights.astype(jnp.float32), axis=1) + jnp.sum(
        far_weights.astype(jnp.float32), axis=1
    )
    neighbours = ((band_sum + far_sum).reshape(rows_dev, col_count) / degree[:, None]).astype(
        jnp.bfloat16
    )
    rows_self = lax.dynamic_slice_in_dim(w_self, col_start, col_count, 0)
    rows_neigh = lax.dynamic_slice_in_dim(w_neigh, col_start, col_count, 0)
    joined = jnp.concatenate([neighbours, packed], axis=0)
    gathered = lax.all_to_all(
        jnp.broadcast_to(joined[None], (feat_count,) + joined.shape),
        "feat",
        split_axis=0,
        concat_axis=0,
        tiled=True,
    )
    neighbours_each = gathered[:, :rows_dev]
    feats_each = gathered[:, rows_dev : 2 * rows_dev]
    cotangent_each = gathered[:, 2 * rows_dev : 3 * rows_dev]
    bias_rows = gathered[:, 3 * rows_dev : 3 * rows_dev + 3].astype(jnp.float32)
    bias_each = (bias_rows[:, 0:1] + bias_rows[:, 1:2]) + bias_rows[:, 2:3]
    blocked = (feat_count, col_count, feat_count, col_count)
    preact_each = (
        jnp.einsum(
            "frc,fcgd->grd",
            feats_each,
            w_self.reshape(blocked),
            preferred_element_type=jnp.float32,
        )
        + jnp.einsum(
            "frc,fcgd->grd",
            neighbours_each,
            w_neigh.reshape(blocked),
            preferred_element_type=jnp.float32,
        )
        + bias_each
    )
    preact = lax.dynamic_index_in_dim(preact_each, lax.axis_index("feat"), 0, keepdims=False)
    layer_out = jax.nn.silu(preact).astype(jnp.bfloat16)
    sigmoid_z = jax.nn.sigmoid(preact_each)
    grad_each = (
        cotangent_each.astype(jnp.float32) * sigmoid_z * (1.0 + preact_each * (1.0 - sigmoid_z))
    ).astype(jnp.bfloat16)
    grad_scale = float(rows_dev * peer_count) ** (-0.5)
    part_self = jnp.einsum(
        "rc,grd->cgd", node_feats, grad_each, preferred_element_type=jnp.float32
    ).reshape(col_count, -1)
    part_neigh = jnp.einsum(
        "rc,grd->cgd", neighbours, grad_each, preferred_element_type=jnp.float32
    ).reshape(col_count, -1)
    dense_grad = jnp.einsum(
        "grd,cgd->rc",
        grad_each,
        rows_self.reshape(col_count, feat_count, col_count),
        preferred_element_type=jnp.float32,
    )
    grad_agg = jnp.einsum(
        "grd,cgd->rc",
        grad_each,
        rows_neigh.reshape(col_count, feat_count, col_count),
        preferred_element_type=jnp.float32,
    )
    grad_neighbours = (grad_agg / degree[:, None]).astype(jnp.bfloat16)
    grad_blocks = grad_neighbours.reshape(blocks, tile_size, col_count)
    grad_windows = jnp.einsum(
        "bij,bic->bjc", band_tiles, grad_blocks, preferred_element_type=jnp.float32
    )
    grad_padded = jnp.zeros((rows_dev + 2 * tile_size, col_count), jnp.float32)
    for offset in range(3):
        piece = grad_windows[:, offset * tile_size : (offset + 1) * tile_size, :].reshape(
            rows_dev, col_count
        )
        grad_padded = grad_padded + jnp.pad(
            piece, ((offset * tile_size, (2 - offset) * tile_size), (0, 0))
        )
    top_rim = grad_padded[:tile_size]
    bottom_rim = grad_padded[rows_dev + tile_size :]
    from_below = from_behind(top_rim, "rows", -1)
    from_above = from_behind(bottom_rim, "rows", 1)
    grad_fetched = jnp.einsum(
        "bij,bic->bjc", far_tiles, grad_blocks, preferred_element_type=jnp.float32
    )
    placing = (
        slot_ids[None, None, :]
        == (jnp.arange(peer_count, dtype=jnp.int32)[:, None, None] * capacity
            + jnp.arange(capacity, dtype=jnp.int32)[None, :, None])
    ).astype(jnp.bfloat16)
    returning = jnp.einsum(
        "pse,ejc->psjc",
        placing,
        grad_fetched.reshape(entries, tile_size, col_count).astype(jnp.bfloat16),
        preferred_element_type=jnp.float32,
    )
    partials = jnp.stack([part_self, part_neigh]).reshape(peer_count, -1)
    high = lax.reduce_precision(partials, exponent_bits=8, mantissa_bits=7)
    coded = jnp.stack(
        [high.astype(jnp.bfloat16), (partials - high).astype(jnp.bfloat16)], axis=1
    ).reshape(peer_count, capacity, tile_size, -1)
    payload = jnp.concatenate(
        [
            returning.reshape(peer_count, capacity, tile_size, col_count).astype(jnp.bfloat16),
            coded,
        ],
        axis=3,
    )
    arrived = lax.all_to_all(payload, "rows", split_axis=0, concat_axis=0, tiled=True)
    returned = arrived[..., :col_count]
    codes = arrived[..., col_count:].reshape(peer_count, 2, -1).astype(jnp.float32)
    mine = jnp.sum(codes[:, 0] + codes[:, 1], axis=0, keepdims=True)
    whole = lax.all_to_all(
        jnp.broadcast_to(mine, partials.shape), "rows", split_axis=0, concat_axis=0, tiled=True
    )
    sum_self, sum_neigh = whole.reshape(2, col_count, -1)
    grad_self = sum_self * grad_scale
    grad_neigh = sum_neigh * grad_scale
    target_block = jnp.where(usable, wanted, blocks)
    routing = (
        target_block[None] == jnp.arange(blocks, dtype=jnp.int32)[:, None, None]
    ).astype(jnp.bfloat16)
    owed = jnp.einsum("bps,psjc->bjc", routing, returned, preferred_element_type=jnp.float32)
    interior = (
        dense_grad
        + grad_padded[tile_size : tile_size + rows_dev]
        + owed.reshape(rows_dev, col_count)
    )
    interior = interior.at[:tile_size].add(from_above)
    grad_feats = interior.at[rows_dev - tile_size :].add(from_below)
    return (layer_out, grad_feats, grad_self, grad_neigh)


def solution(mesh):
    in_specs = (
        P("rows", "feat"),
        P("rows", None),
        P("rows", None),
        P("rows", None),
        P("rows", None),
        P(),
        P(),
        P("feat"),
        P("rows", "feat"),
    )
    out_specs = (P("rows", "feat"), P("rows", "feat"), P("feat", None), P("feat", None))
    return jax.shard_map(
        on_device, mesh=mesh, in_specs=in_specs, out_specs=out_specs, check_vma=False
    )
```

```python
import jax
import jax.numpy as jnp
from jax import lax
from jax.sharding import PartitionSpec as P


def extended(block, sides, width):
    for axis, dim in sides:
        count = lax.axis_size(axis)
        forward = [(i, i + 1) for i in range(count - 1)]
        backward = [(target, source) for source, target in forward]
        low = lax.ppermute(
            lax.slice_in_dim(block, block.shape[dim] - width, None, axis=dim), axis, forward
        )
        high = lax.ppermute(lax.slice_in_dim(block, 0, width, axis=dim), axis, backward)
        block = jnp.concatenate([low, block, high], axis=dim)
    return block


def from_behind(block, axis, distance):
    devices = range(lax.axis_size(axis))
    route = [(i - distance, i) for i in devices if i - distance in devices]
    return lax.ppermute(block, axis, route)


def on_device(
    node_feats, band_weights, far_weights, far_owner, far_local, w_self, w_neigh, bias, cotangent
):
    rows_dev, col_count = node_feats.shape
    tile_size = band_weights.shape[1] // 3
    blocks = rows_dev // tile_size
    fanout = far_owner.shape[1]
    peer_count = lax.axis_size("rows")
    capacity = max(2, 2 * blocks * fanout // peer_count)
    col_start = lax.axis_index("feat") * col_count
    bias_high = lax.reduce_precision(bias, exponent_bits=8, mantissa_bits=7)
    bias_rest = bias - bias_high
    bias_mid = lax.reduce_precision(bias_rest, exponent_bits=8, mantissa_bits=7)
    bias_parts = jnp.zeros((16, col_count), jnp.bfloat16)
    bias_parts = bias_parts.at[:3].set(
        jnp.stack([bias_high, bias_mid, bias_rest - bias_mid]).astype(jnp.bfloat16)
    )
    packed = jnp.concatenate([node_feats, cotangent, bias_parts], axis=0)
    feat_count = lax.axis_size("feat")
    padded = extended(node_feats, (("rows", 0),), tile_size)
    windows = jnp.concatenate(
        [
            padded[offset * tile_size : offset * tile_size + rows_dev].reshape(
                blocks, tile_size, col_count
            )
            for offset in range(3)
        ],
        axis=1,
    )
    band_tiles = band_weights.reshape(blocks, tile_size, 3 * tile_size)
    band_sum = jnp.einsum("bij,bjc->bic", band_tiles, windows, preferred_element_type=jnp.float32)
    owner_ids = far_owner.reshape(-1)
    local_ids = far_local.reshape(-1)
    entries = owner_ids.shape[0]
    same_owner = owner_ids[:, None] == owner_ids[None, :]
    earlier = jnp.arange(entries)[None, :] < jnp.arange(entries)[:, None]
    slot_rank = jnp.sum(jnp.where(same_owner & earlier, 1, 0), axis=1).astype(jnp.int32)
    slot_ids = owner_ids * capacity + slot_rank
    slot_hit = slot_ids[:, None] == jnp.arange(peer_count * capacity, dtype=jnp.int32)[None, :]
    request = (jnp.sum(jnp.where(slot_hit, local_ids[:, None] + 1, 0), axis=0) - 1).reshape(
        peer_count, capacity
    )
    wanted = lax.all_to_all(request, "rows", split_axis=0, concat_axis=0, tiled=True)
    usable = wanted >= 0
    safe_ids = jnp.maximum(wanted, 0)
    own_blocks = node_feats.reshape(blocks, tile_size, col_count)
    choosing = (wanted[:, :, None] == jnp.arange(blocks, dtype=jnp.int32)[None, None, :]).astype(
        jnp.bfloat16
    )
    outgoing = jnp.einsum(
        "psb,bjc->psjc", choosing, own_blocks, preferred_element_type=jnp.float32
    ).astype(jnp.bfloat16)
    incoming = lax.all_to_all(outgoing, "rows", split_axis=0, concat_axis=0, tiled=True)
    picking = (
        slot_ids[:, None] == jnp.arange(peer_count * capacity, dtype=jnp.int32)[None, :]
    ).astype(jnp.bfloat16)
    fetched = jnp.einsum(
        "ek,kjc->ejc",
        picking,
        incoming.reshape(peer_count * capacity, tile_size, col_count),
        preferred_element_type=jnp.float32,
    ).astype(jnp.bfloat16).reshape(blocks, fanout * tile_size, col_count)
    far_tiles = far_weights.reshape(blocks, tile_size, fanout * tile_size)
    far_sum = jnp.einsum("bij,bjc->bic", far_tiles, fetched, preferred_element_type=jnp.float32)
    degree = jnp.sum(band_weights.astype(jnp.float32), axis=1) + jnp.sum(
        far_weights.astype(jnp.float32), axis=1
    )
    neighbours = ((band_sum + far_sum).reshape(rows_dev, col_count) / degree[:, None]).astype(
        jnp.bfloat16
    )
    rows_self = lax.dynamic_slice_in_dim(w_self, col_start, col_count, 0)
    rows_neigh = lax.dynamic_slice_in_dim(w_neigh, col_start, col_count, 0)
    joined = jnp.concatenate([neighbours, packed], axis=0)
    gathered = lax.all_to_all(
        jnp.broadcast_to(joined[None], (feat_count,) + joined.shape),
        "feat",
        split_axis=0,
        concat_axis=0,
        tiled=True,
    )
    neighbours_each = gathered[:, :rows_dev]
    feats_each = gathered[:, rows_dev : 2 * rows_dev]
    cotangent_each = gathered[:, 2 * rows_dev : 3 * rows_dev]
    bias_rows = gathered[:, 3 * rows_dev : 3 * rows_dev + 3].astype(jnp.float32)
    bias_each = (bias_rows[:, 0:1] + bias_rows[:, 1:2]) + bias_rows[:, 2:3]
    blocked = (feat_count, col_count, feat_count, col_count)
    preact_each = (
        jnp.einsum(
            "frc,fcgd->grd",
            feats_each,
            w_self.reshape(blocked),
            preferred_element_type=jnp.float32,
        )
        + jnp.einsum(
            "frc,fcgd->grd",
            neighbours_each,
            w_neigh.reshape(blocked),
            preferred_element_type=jnp.float32,
        )
        + bias_each
    )
    preact = lax.dynamic_index_in_dim(preact_each, lax.axis_index("feat"), 0, keepdims=False)
    layer_out = jax.nn.silu(preact).astype(jnp.bfloat16)
    sigmoid_z = jax.nn.sigmoid(preact_each)
    grad_each = (
        cotangent_each.astype(jnp.float32) * sigmoid_z * (1.0 + preact_each * (1.0 - sigmoid_z))
    ).astype(jnp.bfloat16)
    grad_scale = float(rows_dev * peer_count) ** (-0.5)
    part_self = jnp.einsum(
        "rc,grd->cgd", node_feats, grad_each, preferred_element_type=jnp.float32
    ).reshape(col_count, -1)
    part_neigh = jnp.einsum(
        "rc,grd->cgd", neighbours, grad_each, preferred_element_type=jnp.float32
    ).reshape(col_count, -1)
    dense_grad = jnp.einsum(
        "grd,cgd->rc",
        grad_each,
        rows_self.reshape(col_count, feat_count, col_count),
        preferred_element_type=jnp.float32,
    )
    grad_agg = jnp.einsum(
        "grd,cgd->rc",
        grad_each,
        rows_neigh.reshape(col_count, feat_count, col_count),
        preferred_element_type=jnp.float32,
    )
    grad_neighbours = (grad_agg / degree[:, None]).astype(jnp.bfloat16)
    grad_blocks = grad_neighbours.reshape(blocks, tile_size, col_count)
    grad_windows = jnp.einsum(
        "bij,bic->bjc", band_tiles, grad_blocks, preferred_element_type=jnp.float32
    )
    grad_padded = jnp.zeros((rows_dev + 2 * tile_size, col_count), jnp.float32)
    for offset in range(3):
        piece = grad_windows[:, offset * tile_size : (offset + 1) * tile_size, :].reshape(
            rows_dev, col_count
        )
        grad_padded = grad_padded + jnp.pad(
            piece, ((offset * tile_size, (2 - offset) * tile_size), (0, 0))
        )
    top_rim = grad_padded[:tile_size]
    bottom_rim = grad_padded[rows_dev + tile_size :]
    from_below = from_behind(top_rim, "rows", -1)
    from_above = from_behind(bottom_rim, "rows", 1)
    grad_fetched = jnp.einsum(
        "bij,bic->bjc", far_tiles, grad_blocks, preferred_element_type=jnp.float32
    )
    placing = (
        slot_ids[None, None, :]
        == (jnp.arange(peer_count, dtype=jnp.int32)[:, None, None] * capacity
            + jnp.arange(capacity, dtype=jnp.int32)[None, :, None])
    ).astype(jnp.bfloat16)
    returning = jnp.einsum(
        "pse,ejc->psjc",
        placing,
        grad_fetched.reshape(entries, tile_size, col_count).astype(jnp.bfloat16),
        preferred_element_type=jnp.float32,
    )
    partials = jnp.stack([part_self, part_neigh]).reshape(peer_count, -1)
    high = lax.reduce_precision(partials, exponent_bits=8, mantissa_bits=7)
    coded = jnp.stack(
        [high.astype(jnp.bfloat16), (partials - high).astype(jnp.bfloat16)], axis=1
    ).reshape(peer_count, capacity, tile_size, -1)
    payload = jnp.concatenate(
        [
            returning.reshape(peer_count, capacity, tile_size, col_count).astype(jnp.bfloat16),
            coded,
        ],
        axis=3,
    )
    arrived = lax.all_to_all(payload, "rows", split_axis=0, concat_axis=0, tiled=True)
    returned = arrived[..., :col_count]
    codes = arrived[..., col_count:].reshape(peer_count, 2, -1).astype(jnp.float32)
    mine = jnp.sum(codes[:, 0] + codes[:, 1], axis=0, keepdims=True)
    whole = lax.all_to_all(
        jnp.broadcast_to(mine, partials.shape), "rows", split_axis=0, concat_axis=0, tiled=True
    )
    sum_self, sum_neigh = whole.reshape(2, col_count, -1)
    grad_self = sum_self * grad_scale
    grad_neigh = sum_neigh * grad_scale
    target_block = jnp.where(usable, wanted, blocks)
    routing = (
        target_block[None] == jnp.arange(blocks, dtype=jnp.int32)[:, None, None]
    ).astype(jnp.bfloat16)
    owed = jnp.einsum("bps,psjc->bjc", routing, returned, preferred_element_type=jnp.float32)
    interior = (
        dense_grad
        + grad_padded[tile_size : tile_size + rows_dev]
        + owed.reshape(rows_dev, col_count)
    )
    interior = interior.at[:tile_size].add(from_above)
    grad_feats = interior.at[rows_dev - tile_size :].add(from_below)
    return (layer_out, grad_feats, grad_self, grad_neigh)


def solution(mesh):
    in_specs = (
        P("rows", "feat"),
        P("rows", None),
        P("rows", None),
        P("rows", None),
        P("rows", None),
        P(),
        P(),
        P("feat"),
        P("rows", "feat"),
    )
    out_specs = (P("rows", "feat"), P("rows", "feat"), P("feat", None), P("feat", None))
    return jax.shard_map(
        on_device, mesh=mesh, in_specs=in_specs, out_specs=out_specs, check_vma=False
    )
```
